32 devices in a mesh: groups: 2 (over x), seq: 8 (over z, y), tp: 2 (over core).
Axes of the slice: x: 2, y: 2, z: 4, core: 2. Of those that a mesh axis runs over, the one named last changes fastest.
Arguments:
- token_ids: int32 [2048], P(('groups', 'seq')), parts along dimension 0, may hold values from 0 to 511
- embed_table: bfloat16 [512, 4096], P(None, 'tp'), may hold values from -4 to 4
- hyena_qkv: bfloat16 [3, 2048, 4096], P(None, ('groups', 'seq'), 'tp'), parts along dimension 1, may hold values from -5 to 5
- conv_weights: float32 [3, 3, 4096], P(None, None, 'tp'), may hold values from -2.5 to 2.5
- decay_rates: float32 [8, 4096], P(None, 'tp'), may hold values from 0 to 1, as said below
- residues: float32 [8, 4096], P(None, 'tp'), may hold values from -2 to 2
- prior_state: float32 [16, 4096], P('groups', 'tp'), parts along dimension 0, may hold values from -4 to 4
Outputs:
- hyena_out: bfloat16 [2048, 4096], P(('groups', 'seq'), 'tp'), parts along dimension 0
- end_state: float32 [16, 4096], P('groups', ('tp', 'seq')), parts along dimension 0
The draws below stay inside these ranges and needn't reach their ends.
There are 2 independent parts, one for each index of `groups`. The reference program is written for one: setup_inputs(seed, part) draws one part's arguments, and reference() takes and returns one part's arrays. A program takes and returns all parts, laid end to end along the dimension named above; an argument that names none is the same for every part. Nothing has to cross between parts.
Inputs may be any that keep to these rules, and one draw needn't show every extreme that they name: `decay_rates`: decay rates of the modes, positive.
All inputs are finite; a program needn't handle non-finite values.
Results may differ from the reference program's by a relative error of at most 0.001.
Values may be sent and summed in bfloat16 or wider, within the bound.
No kernel may reach another device: no remote copies, remote signals or barrier semaphores. Data moves between devices by JAX's collectives and lax.ppermute only.
A program may use at most 128 MiB of HBM per device.

```python
import math
import jax
import jax.numpy as jnp
from jax import lax

D = 4096
VOCAB = 512
ORDER = 8
SHORT = 3
TOK_DEV = 128
TOKENS = 1024


def spread_rates(key, shape, low_end, high_end):
    return jnp.exp(jax.random.uniform(key, shape, jnp.float32, math.log(low_end), math.log(high_end)))


def draw_decay_rates(key, part):
    key_c, key_s, key_l, key_h, key_f = jax.random.split(jax.random.fold_in(key, 11), 5)
    shape = (ORDER, D)
    chooser = jax.random.uniform(key_c, shape, jnp.float32)
    first_cut = 0.3
    second_cut = 0.5
    third_cut = 0.75
    slow_rate = spread_rates(key_s, shape, 0.05 / TOKENS, 2.0 / TOKENS)
    lower_rate = spread_rates(key_l, shape, 0.3 / TOK_DEV, 0.95 / TOK_DEV)
    upper_rate = spread_rates(key_h, shape, 1.05 / TOK_DEV, 1.6 / TOK_DEV)
    fast_rate = spread_rates(key_f, shape, 1.0 / 48.0, 1.0 / 24.0)
    middle_rate = jnp.where(chooser < second_cut, lower_rate, jnp.where(chooser < third_cut, upper_rate, fast_rate))
    return jnp.where(chooser < first_cut, slow_rate, middle_rate).astype(jnp.float32)


def set_ends(drawn, key, low, top_value):
    longest = drawn.shape.index(max(drawn.shape))
    spots = []
    for shift in (0, 1):
        where = [jax.random.randint(jax.random.fold_in(key, axis), (), 0, length) for axis, length in enumerate(drawn.shape)]
        where[longest] = (where[longest] + shift) % drawn.shape[longest]
        spots.append(tuple(where))
    return drawn.at[spots[0]].set(low).at[spots[1]].set(top_value)


def levels(key, shape, shards, least, high):
    loudness, own = 1.0, jax.random.fold_in(key, 6)
    for position, shards_of in shards:
        draws = jnp.exp(jax.random.uniform(jax.random.fold_in(own, position), (shards_of,), jnp.float32, least / len(shards), high / len(shards)))
        loudness = loudness * jnp.repeat(draws, shape[position] // shards_of).reshape([-1 if axis == position else 1 for axis in range(len(shape))])
    return loudness


def scatter_about(rng, extent, width, bound, cuts=(), dtype=jnp.bfloat16):
    level = levels(rng, extent, cuts, -0.22, 0.18) if cuts else 1.0
    drawn = jax.random.normal(rng, extent, jnp.float32) * width * level
    return jnp.minimum(jnp.maximum(drawn, -bound), bound).astype(dtype)


def setup_inputs(seed: int = 0, part: int = 0) -> dict:
    streams_of = jax.random.split(jax.random.key(seed), 8)
    part_splits = jax.random.split(jax.random.fold_in(streams_of[7], part), 8)
    token_ids = set_ends(jax.random.randint(part_splits[0], (TOKENS,), 0, VOCAB), jax.random.fold_in(part_splits[0], 1), 0, VOCAB - 1).astype(jnp.int32)
    embed_table = scatter_about(streams_of[1], (VOCAB, D), 1.0, 4.0, ((1, 2),))
    hyena_qkv = scatter_about(part_splits[2], (3, TOKENS, D), 1.0, 5.0, ((1, 8), (2, 2)))
    conv_weights = scatter_about(streams_of[3], (3, SHORT, D), 0.6, 2.5, ((2, 2),), jnp.float32)
    decay_rates = draw_decay_rates(jax.random.fold_in(streams_of[7], 71), part)
    residues = scatter_about(streams_of[5], (ORDER, D), ORDER ** -0.5, 2.0, ((1, 2),), jnp.float32)
    prior_state = scatter_about(part_splits[6], (ORDER, D), 1.0, 4.0, ((1, 2),), jnp.float32)
    return dict(token_ids=token_ids, embed_table=embed_table, hyena_qkv=hyena_qkv, conv_weights=conv_weights, decay_rates=decay_rates, residues=residues, prior_state=prior_state)


def short_conv(signal, tap_weights):
    tok_count = signal.shape[0]
    widened = signal.astype(jnp.float32)
    total = jnp.zeros(widened.shape, jnp.float32)
    for tap_index in range(tap_weights.shape[0]):
        shifted = jnp.pad(widened, ((tap_index, 0), (0, 0)))[:tok_count]
        total = total + tap_weights[tap_index][None, :] * shifted
    return total

def reference(token_ids, embed_table, hyena_qkv, conv_weights, decay_rates, residues, prior_state):
    q_feat = short_conv(hyena_qkv[0], conv_weights[0])
    k_feat = short_conv(hyena_qkv[1], conv_weights[1])
    v_feat = short_conv(hyena_qkv[2], conv_weights[2])
    product_in = k_feat * v_feat
    pole = jnp.exp(-decay_rates)
    gain = jnp.sqrt(-jnp.expm1(-2.0 * decay_rates))

    def advance(state, row):
        state = pole * state + gain * row[None, :]
        return (state, lax.optimization_barrier(jnp.sum(residues * state, axis=0)))
    end_state, filtered = lax.scan(advance, prior_state, product_in)
    embedded = embed_table[token_ids].astype(jnp.float32)
    hyena_out = (embedded + q_feat * filtered).astype(jnp.bfloat16)
    return (hyena_out, end_state)
```

```python
import jax
import jax.numpy as jnp
from jax import lax
from jax.experimental import pallas as pl
from jax.experimental.pallas import tpu as pltpu
from jax.sharding import PartitionSpec as P

LANES = 256


def shifted(array, axis, by):
    size = lax.axis_size(axis)
    pairs = [(i, i + by) for i in range(size) if 0 <= i + by < size]
    return lax.ppermute(array, axis, pairs)


def front_kernel(qkv_ref, tails_ref, w_ref, pole_ref, gain_ref, qc_ref, pin_ref, end_ref):
    tok, channels = qc_ref.shape
    modes = pole_ref.shape[0]
    for c0 in range(0, channels, LANES):
        cs = pl.ds(c0, LANES)
        row = lax.broadcasted_iota(jnp.int32, (tok, LANES), 0)
        feats = []
        for member in range(3):
            x = qkv_ref[member, :, cs].astype(jnp.float32)
            tl = tails_ref[member, :, cs].astype(jnp.float32)
            x1 = pltpu.roll(x, 1, 0)
            x1 = jnp.where(row == 0, tl[1:2, :], x1)
            x2 = pltpu.roll(x, 2, 0)
            x2 = jnp.where(row == 0, tl[0:1, :], jnp.where(row == 1, tl[1:2, :], x2))
            w = w_ref[member, :, cs]
            feats.append(w[0:1, :] * x + w[1:2, :] * x1 + w[2:3, :] * x2)
        qc_ref[:, cs] = feats[0]
        pin_ref[:, cs] = feats[1] * feats[2]

    for c0 in range(0, channels, LANES):
        cs = pl.ds(c0, LANES)
        pole = pole_ref[:, cs]

        def step(blk, acc):
            base = pl.multiple_of(blk * 8, 8)
            rows = pin_ref[pl.ds(base, 8), cs]
            for i in range(8):
                acc = pole * acc + jnp.broadcast_to(rows[i : i + 1, :], (modes, LANES))
            return acc

        acc = lax.fori_loop(0, tok // 8, step, jnp.zeros((modes, LANES), jnp.float32))
        end_ref[:, cs] = gain_ref[:, cs] * acc


def back_kernel(pin_ref, qc_ref, emb_ref, inc_ref, pole_ref, gain_ref, res_ref, out_ref, f_scr):
    tok, channels = pin_ref.shape
    modes = pole_ref.shape[0]
    for c0 in range(0, channels, LANES):
        cs = pl.ds(c0, LANES)
        pole = pole_ref[:, cs]
        gain = gain_ref[:, cs]
        res = res_ref[:, cs]

        def step(blk, state):
            base = pl.multiple_of(blk * 16, 16)
            rows = pin_ref[pl.ds(base, 16), cs]
            for i in range(16):
                state = pole * state + gain * jnp.broadcast_to(rows[i : i + 1, :], (modes, LANES))
                f_scr[i : i + 1, :] = jnp.sum(res * state, axis=0, keepdims=True)
            total = emb_ref[pl.ds(base, 16), cs].astype(jnp.float32) + qc_ref[pl.ds(base, 16), cs] * f_scr[...]
            out_ref[pl.ds(base, 16), cs] = total.astype(out_ref.dtype)
            return state

        lax.fori_loop(0, tok // 16, step, inc_ref[:, cs])


def vmem_specs(count):
    return [pl.BlockSpec(memory_space=pltpu.VMEM)] * count


def front(qkv, tails, conv_weights, pole, gain):
    tok, channels = qkv.shape[1], qkv.shape[2]
    modes = pole.shape[0]
    return pl.pallas_call(
        front_kernel,
        out_shape=(
            jax.ShapeDtypeStruct((tok, channels), jnp.float32),
            jax.ShapeDtypeStruct((tok, channels), jnp.float32),
            jax.ShapeDtypeStruct((modes, channels), jnp.float32),
        ),
        in_specs=vmem_specs(5),
        out_specs=tuple(vmem_specs(3)),
        cost_estimate=pl.CostEstimate(
            flops=30 * tok * channels + 2 * tok * modes * channels,
            bytes_accessed=3 * tok * channels * 2 + 2 * tok * channels * 4,
            transcendentals=0,
        ),
    )(qkv, tails, conv_weights, pole, gain)


def back(pin, qc, embedded, incoming, pole, gain, residues):
    tok, channels = pin.shape
    modes = pole.shape[0]
    return pl.pallas_call(
        back_kernel,
        out_shape=jax.ShapeDtypeStruct((tok, channels), jnp.bfloat16),
        in_specs=vmem_specs(7),
        out_specs=pl.BlockSpec(memory_space=pltpu.VMEM),
        scratch_shapes=[pltpu.VMEM((16, LANES), jnp.float32)],
        cost_estimate=pl.CostEstimate(
            flops=6 * tok * modes * channels,
            bytes_accessed=tok * channels * (4 + 4 + 2 + 2),
            transcendentals=0,
        ),
    )(pin, qc, embedded, incoming, pole, gain, residues)


def butterfly(local_end, decay_rates, tok_local, axis):
    count = lax.axis_size(axis)
    me = lax.axis_index(axis)
    total = local_end
    prefix = jnp.zeros_like(local_end)
    span = 1
    while span < count:
        pairs = [(i, i ^ span) for i in range(count)]
        other = lax.ppermute(total, axis, pairs)
        upper = (me & span) != 0
        offset = (me % span).astype(jnp.float32) * tok_local
        near = jnp.exp(-decay_rates * offset)
        far = jnp.exp(-decay_rates * float(span * tok_local))
        prefix = jnp.where(upper, prefix + near * other, prefix)
        total = jnp.where(upper, total + far * other, other + far * total)
        span *= 2
    return prefix, total


def body(token_ids, embed_table, hyena_qkv, conv_weights, decay_rates, residues, prior_state):
    tok_local = hyena_qkv.shape[1]
    tap_count = conv_weights.shape[1]
    seq_count = lax.axis_size("seq")
    seq_index = lax.axis_index("seq")
    tails_local = hyena_qkv[:, tok_local - (tap_count - 1) :, :]
    tails_prev = shifted(tails_local, "seq", 1)
    pole = jnp.exp(-decay_rates)
    gain = jnp.sqrt(-jnp.expm1(-2.0 * decay_rates))
    qc, pin, local_end = front(hyena_qkv, tails_prev, conv_weights, pole, gain)
    prefix, total = butterfly(local_end, decay_rates, tok_local, "seq")
    incoming = prefix + jnp.exp(-decay_rates * (seq_index.astype(jnp.float32) * tok_local)) * prior_state
    vocab_ids = jnp.arange(embed_table.shape[0], dtype=jnp.int32)
    one_hot = (token_ids[:, None] == vocab_ids[None, :]).astype(jnp.bfloat16)
    embedded = jnp.dot(one_hot, embed_table, preferred_element_type=jnp.float32).astype(jnp.bfloat16)
    hyena_out = back(pin, qc, embedded, incoming, pole, gain, residues)
    end_full = total + jnp.exp(-decay_rates * float(seq_count * tok_local)) * prior_state
    share_cols = end_full.shape[1] // seq_count
    end_state = lax.dynamic_slice_in_dim(end_full, seq_index * share_cols, share_cols, 1)
    return (hyena_out, end_state)


def solution(mesh):
    return jax.shard_map(
        body,
        mesh=mesh,
        in_specs=(
            P(("groups", "seq")),
            P(None, "tp"),
            P(None, ("groups", "seq"), "tp"),
            P(None, None, "tp"),
            P(None, "tp"),
            P(None, "tp"),
            P("groups", "tp"),
        ),
        out_specs=(P(("groups", "seq"), "tp"), P("groups", ("tp", "seq"))),
        check_vma=False,
    )
```

```python
import jax
import jax.numpy as jnp
from jax import lax
from jax.experimental import pallas as pl
from jax.experimental.pallas import tpu as pltpu
from jax.sharding import PartitionSpec as P

LANES = 256
WIDE = 1024


def shifted(array, axis, by):
    size = lax.axis_size(axis)
    pairs = [(i, i + by) for i in range(size) if 0 <= i + by < size]
    return lax.ppermute(array, axis, pairs)


def front_kernel(qkv_ref, tails_ref, w_ref, pole_ref, gain_ref, qc_ref, pin_ref, end_ref):
    tok, channels = qc_ref.shape
    modes = pole_ref.shape[0]
    for c0 in range(0, channels, LANES):
        cs = pl.ds(c0, LANES)
        row = lax.broadcasted_iota(jnp.int32, (tok, LANES), 0)
        feats = []
        for member in range(3):
            x = qkv_ref[member, :, cs].astype(jnp.float32)
            tl = tails_ref[member, :, cs].astype(jnp.float32)
            x1 = pltpu.roll(x, 1, 0)
            x1 = jnp.where(row == 0, tl[1:2, :], x1)
            x2 = pltpu.roll(x, 2, 0)
            x2 = jnp.where(row == 0, tl[0:1, :], jnp.where(row == 1, tl[1:2, :], x2))
            w = w_ref[member, :, cs]
            feats.append(w[0:1, :] * x + w[1:2, :] * x1 + w[2:3, :] * x2)
        qc_ref[:, cs] = feats[0]
        pin_ref[:, cs] = feats[1] * feats[2]

    for c0 in range(0, channels, WIDE):
        cs = pl.ds(c0, WIDE)
        pole = pole_ref[:, cs]

        def step(blk, acc):
            base = pl.multiple_of(blk * 8, 8)
            rows = pin_ref[pl.ds(base, 8), cs]
            for i in range(8):
                acc = pole * acc + jnp.broadcast_to(rows[i : i + 1, :], (modes, WIDE))
            return acc

        acc = lax.fori_loop(0, tok // 8, step, jnp.zeros((modes, WIDE), jnp.float32))
        end_ref[:, cs] = gain_ref[:, cs] * acc


def back_kernel(pin_ref, qc_ref, emb_ref, inc_ref, pole_ref, gain_ref, res_ref, out_ref, f_scr):
    tok, channels = pin_ref.shape
    modes = pole_ref.shape[0]
    for c0 in range(0, channels, WIDE):
        cs = pl.ds(c0, WIDE)
        pole = pole_ref[:, cs]
        gain = gain_ref[:, cs]
        res = res_ref[:, cs]

        def step(blk, state):
            base = pl.multiple_of(blk * 16, 16)
            rows = pin_ref[pl.ds(base, 16), cs]
            for i in range(16):
                state = pole * state + gain * jnp.broadcast_to(rows[i : i + 1, :], (modes, WIDE))
                f_scr[i : i + 1, :] = jnp.sum(res * state, axis=0, keepdims=True)
            total = emb_ref[pl.ds(base, 16), cs].astype(jnp.float32) + qc_ref[pl.ds(base, 16), cs] * f_scr[...]
            out_ref[pl.ds(base, 16), cs] = total.astype(out_ref.dtype)
            return state

        lax.fori_loop(0, tok // 16, step, inc_ref[:, cs])


def vmem_specs(count):
    return [pl.BlockSpec(memory_space=pltpu.VMEM)] * count


def front(qkv, tails, conv_weights, pole, gain):
    tok, channels = qkv.shape[1], qkv.shape[2]
    modes = pole.shape[0]
    return pl.pallas_call(
        front_kernel,
        out_shape=(
            jax.ShapeDtypeStruct((tok, channels), jnp.float32),
            jax.ShapeDtypeStruct((tok, channels), jnp.float32),
            jax.ShapeDtypeStruct((modes, channels), jnp.float32),
        ),
        in_specs=vmem_specs(5),
        out_specs=tuple(vmem_specs(3)),
        cost_estimate=pl.CostEstimate(
            flops=30 * tok * channels + 2 * tok * modes * channels,
            bytes_accessed=3 * tok * channels * 2 + 2 * tok * channels * 4,
            transcendentals=0,
        ),
    )(qkv, tails, conv_weights, pole, gain)


def back(pin, qc, embedded, incoming, pole, gain, residues):
    tok, channels = pin.shape
    modes = pole.shape[0]
    return pl.pallas_call(
        back_kernel,
        out_shape=jax.ShapeDtypeStruct((tok, channels), jnp.bfloat16),
        in_specs=vmem_specs(7),
        out_specs=pl.BlockSpec(memory_space=pltpu.VMEM),
        scratch_shapes=[pltpu.VMEM((16, WIDE), jnp.float32)],
        cost_estimate=pl.CostEstimate(
            flops=6 * tok * modes * channels,
            bytes_accessed=tok * channels * (4 + 4 + 2 + 2),
            transcendentals=0,
        ),
    )(pin, qc, embedded, incoming, pole, gain, residues)


def butterfly(local_end, decay_rates, tok_local, axis):
    count = lax.axis_size(axis)
    me = lax.axis_index(axis)
    total = local_end
    prefix = jnp.zeros_like(local_end)
    span = 1
    while span < count:
        pairs = [(i, i ^ span) for i in range(count)]
        other = lax.ppermute(total, axis, pairs)
        upper = (me & span) != 0
        offset = (me % span).astype(jnp.float32) * tok_local
        near = jnp.exp(-decay_rates * offset)
        far = jnp.exp(-decay_rates * float(span * tok_local))
        prefix = jnp.where(upper, prefix + near * other, prefix)
        total = jnp.where(upper, total + far * other, other + far * total)
        span *= 2
    return prefix, total


def body(token_ids, embed_table, hyena_qkv, conv_weights, decay_rates, residues, prior_state):
    tok_local = hyena_qkv.shape[1]
    tap_count = conv_weights.shape[1]
    seq_count = lax.axis_size("seq")
    seq_index = lax.axis_index("seq")
    tails_local = hyena_qkv[:, tok_local - (tap_count - 1) :, :]
    tails_prev = shifted(tails_local, "seq", 1)
    pole = jnp.exp(-decay_rates)
    gain = jnp.sqrt(-jnp.expm1(-2.0 * decay_rates))
    qc, pin, local_end = front(hyena_qkv, tails_prev, conv_weights, pole, gain)
    prefix, total = butterfly(local_end, decay_rates, tok_local, "seq")
    incoming = prefix + jnp.exp(-decay_rates * (seq_index.astype(jnp.float32) * tok_local)) * prior_state
    vocab_ids = jnp.arange(embed_table.shape[0], dtype=jnp.int32)
    one_hot = (token_ids[:, None] == vocab_ids[None, :]).astype(jnp.bfloat16)
    embedded = jnp.dot(one_hot, embed_table, preferred_element_type=jnp.float32).astype(jnp.bfloat16)
    hyena_out = back(pin, qc, embedded, incoming, pole, gain, residues)
    end_full = total + jnp.exp(-decay_rates * float(seq_count * tok_local)) * prior_state
    share_cols = end_full.shape[1] // seq_count
    end_state = lax.dynamic_slice_in_dim(end_full, seq_index * share_cols, share_cols, 1)
    return (hyena_out, end_state)


def solution(mesh):
    return jax.shard_map(
        body,
        mesh=mesh,
        in_specs=(
            P(("groups", "seq")),
            P(None, "tp"),
            P(None, ("groups", "seq"), "tp"),
            P(None, None, "tp"),
            P(None, "tp"),
            P(None, "tp"),
            P("groups", "tp"),
        ),
        out_specs=(P(("groups", "seq"), "tp"), P("groups", ("tp", "seq"))),
        check_vma=False,
    )
```

```python
import jax
import jax.numpy as jnp
from jax import lax
from jax.experimental import pallas as pl
from jax.experimental.pallas import tpu as pltpu
from jax.sharding import PartitionSpec as P

LANES = 256
WIDE = 1024


def shifted(array, axis, by):
    size = lax.axis_size(axis)
    pairs = [(i, i + by) for i in range(size) if 0 <= i + by < size]
    return lax.ppermute(array, axis, pairs)


def front_kernel(qkv_ref, tails_ref, w_ref, pole_ref, gain_ref, qc_ref, pin_ref, end_ref):
    tok, channels = qc_ref.shape
    modes = pole_ref.shape[0]
    for c0 in range(0, channels, LANES):
        cs = pl.ds(c0, LANES)
        row = lax.broadcasted_iota(jnp.int32, (tok, LANES), 0)
        feats = []
        for member in range(3):
            x = qkv_ref[member, :, cs].astype(jnp.float32)
            tl = tails_ref[member, :, cs].astype(jnp.float32)
            x1 = pltpu.roll(x, 1, 0)
            x1 = jnp.where(row == 0, tl[1:2, :], x1)
            x2 = pltpu.roll(x, 2, 0)
            x2 = jnp.where(row == 0, tl[0:1, :], jnp.where(row == 1, tl[1:2, :], x2))
            w = w_ref[member, :, cs]
            feats.append(w[0:1, :] * x + w[1:2, :] * x1 + w[2:3, :] * x2)
        qc_ref[:, cs] = feats[0]
        pin_ref[:, cs] = feats[1] * feats[2]

    for c0 in range(0, channels, WIDE):
        cs = pl.ds(c0, WIDE)
        pole = pole_ref[:, cs]

        def step(blk, acc):
            base = pl.multiple_of(blk * 8, 8)
            rows = pin_ref[pl.ds(base, 8), cs]
            for i in range(8):
                acc = pole * acc + jnp.broadcast_to(rows[i : i + 1, :], (modes, WIDE))
            return acc

        acc = lax.fori_loop(0, tok // 8, step, jnp.zeros((modes, WIDE), jnp.float32))
        end_ref[:, cs] = gain_ref[:, cs] * acc


def rows_summed(parts, sub):
    half = [
        jnp.where(sub < 4, parts[j] + pltpu.roll(parts[j], 4, 0), parts[j + 4] + pltpu.roll(parts[j + 4], 4, 0))
        for j in range(4)
    ]
    quarter = [
        jnp.where(sub % 4 < 2, half[j] + pltpu.roll(half[j], 6, 0), half[j + 2] + pltpu.roll(half[j + 2], 2, 0))
        for j in range(2)
    ]
    return jnp.where(
        sub % 2 == 0,
        quarter[0] + pltpu.roll(quarter[0], 7, 0),
        quarter[1] + pltpu.roll(quarter[1], 1, 0),
    )


def back_kernel(pin_ref, qc_ref, emb_ref, inc_ref, pole_ref, gain_ref, res_ref, out_ref):
    tok, channels = pin_ref.shape
    modes = pole_ref.shape[0]
    sub = lax.broadcasted_iota(jnp.int32, (modes, WIDE), 0)
    for c0 in range(0, channels, WIDE):
        cs = pl.ds(c0, WIDE)
        pole = pole_ref[:, cs]
        gain = gain_ref[:, cs]
        res = res_ref[:, cs]

        def step(blk, state):
            base = pl.multiple_of(blk * 16, 16)
            rows = pin_ref[pl.ds(base, 16), cs]
            sums = []
            for half in range(2):
                parts = []
                for i in range(8):
                    r = half * 8 + i
                    state = pole * state + gain * jnp.broadcast_to(rows[r : r + 1, :], (modes, WIDE))
                    parts.append(res * state)
                sums.append(rows_summed(parts, sub))
            filtered = jnp.concatenate(sums, axis=0)
            total = emb_ref[pl.ds(base, 16), cs].astype(jnp.float32) + qc_ref[pl.ds(base, 16), cs] * filtered
            out_ref[pl.ds(base, 16), cs] = total.astype(out_ref.dtype)
            return state

        lax.fori_loop(0, tok // 16, step, inc_ref[:, cs])


def vmem_specs(count):
    return [pl.BlockSpec(memory_space=pltpu.VMEM)] * count


def front(qkv, tails, conv_weights, pole, gain):
    tok, channels = qkv.shape[1], qkv.shape[2]
    modes = pole.shape[0]
    return pl.pallas_call(
        front_kernel,
        out_shape=(
            jax.ShapeDtypeStruct((tok, channels), jnp.float32),
            jax.ShapeDtypeStruct((tok, channels), jnp.float32),
            jax.ShapeDtypeStruct((modes, channels), jnp.float32),
        ),
        in_specs=vmem_specs(5),
        out_specs=tuple(vmem_specs(3)),
        cost_estimate=pl.CostEstimate(
            flops=30 * tok * channels + 2 * tok * modes * channels,
            bytes_accessed=3 * tok * channels * 2 + 2 * tok * channels * 4,
            transcendentals=0,
        ),
    )(qkv, tails, conv_weights, pole, gain)


def back(pin, qc, embedded, incoming, pole, gain, residues):
    tok, channels = pin.shape
    modes = pole.shape[0]
    return pl.pallas_call(
        back_kernel,
        out_shape=jax.ShapeDtypeStruct((tok, channels), jnp.bfloat16),
        in_specs=vmem_specs(7),
        out_specs=pl.BlockSpec(memory_space=pltpu.VMEM),
        cost_estimate=pl.CostEstimate(
            flops=6 * tok * modes * channels,
            bytes_accessed=tok * channels * (4 + 4 + 2 + 2),
            transcendentals=0,
        ),
    )(pin, qc, embedded, incoming, pole, gain, residues)


def butterfly(local_end, decay_rates, tok_local, axis):
    count = lax.axis_size(axis)
    me = lax.axis_index(axis)
    total = local_end
    prefix = jnp.zeros_like(local_end)
    span = 1
    while span < count:
        pairs = [(i, i ^ span) for i in range(count)]
        other = lax.ppermute(total, axis, pairs)
        upper = (me & span) != 0
        offset = (me % span).astype(jnp.float32) * tok_local
        near = jnp.exp(-decay_rates * offset)
        far = jnp.exp(-decay_rates * float(span * tok_local))
        prefix = jnp.where(upper, prefix + near * other, prefix)
        total = jnp.where(upper, total + far * other, other + far * total)
        span *= 2
    return prefix, total


def body(token_ids, embed_table, hyena_qkv, conv_weights, decay_rates, residues, prior_state):
    tok_local = hyena_qkv.shape[1]
    tap_count = conv_weights.shape[1]
    seq_count = lax.axis_size("seq")
    seq_index = lax.axis_index("seq")
    tails_local = hyena_qkv[:, tok_local - (tap_count - 1) :, :]
    tails_prev = shifted(tails_local, "seq", 1)
    pole = jnp.exp(-decay_rates)
    gain = jnp.sqrt(-jnp.expm1(-2.0 * decay_rates))
    qc, pin, local_end = front(hyena_qkv, tails_prev, conv_weights, pole, gain)
    prefix, total = butterfly(local_end, decay_rates, tok_local, "seq")
    incoming = prefix + jnp.exp(-decay_rates * (seq_index.astype(jnp.float32) * tok_local)) * prior_state
    vocab_ids = jnp.arange(embed_table.shape[0], dtype=jnp.int32)
    one_hot = (token_ids[:, None] == vocab_ids[None, :]).astype(jnp.bfloat16)
    embedded = jnp.dot(one_hot, embed_table, preferred_element_type=jnp.float32).astype(jnp.bfloat16)
    hyena_out = back(pin, qc, embedded, incoming, pole, gain, residues)
    end_full = total + jnp.exp(-decay_rates * float(seq_count * tok_local)) * prior_state
    share_cols = end_full.shape[1] // seq_count
    end_state = lax.dynamic_slice_in_dim(end_full, seq_index * share_cols, share_cols, 1)
    return (hyena_out, end_state)


def solution(mesh):
    return jax.shard_map(
        body,
        mesh=mesh,
        in_specs=(
            P(("groups", "seq")),
            P(None, "tp"),
            P(None, ("groups", "seq"), "tp"),
            P(None, None, "tp"),
            P(None, "tp"),
            P(None, "tp"),
            P("groups", "tp"),
        ),
        out_specs=(P(("groups", "seq"), "tp"), P("groups", ("tp", "seq"))),
        check_vma=False,
    )
```

```python
import functools

import jax
import jax.numpy as jnp
from jax import lax
from jax.experimental import pallas as pl
from jax.experimental.pallas import tpu as pltpu
from jax.sharding import PartitionSpec as P

LANES = 256
WIDE = 1024
NARROW = 256


def shifted(array, axis, by):
    size = lax.axis_size(axis)
    pairs = [(i, i + by) for i in range(size) if 0 <= i + by < size]
    return lax.ppermute(array, axis, pairs)


def front_kernel(qkv_ref, tails_ref, w_ref, pole_ref, gain_ref, qc_ref, pin_ref, end_ref):
    tok, channels = qc_ref.shape
    modes = pole_ref.shape[0]
    for c0 in range(0, channels, LANES):
        cs = pl.ds(c0, LANES)
        row = lax.broadcasted_iota(jnp.int32, (tok, LANES), 0)
        feats = []
        for member in range(3):
            x = qkv_ref[member, :, cs].astype(jnp.float32)
            tl = tails_ref[member, :, cs].astype(jnp.float32)
            x1 = pltpu.roll(x, 1, 0)
            x1 = jnp.where(row == 0, tl[1:2, :], x1)
            x2 = pltpu.roll(x, 2, 0)
            x2 = jnp.where(row == 0, tl[0:1, :], jnp.where(row == 1, tl[1:2, :], x2))
            w = w_ref[member, :, cs]
            feats.append(w[0:1, :] * x + w[1:2, :] * x1 + w[2:3, :] * x2)
        qc_ref[:, cs] = feats[0]
        pin_ref[:, cs] = feats[1] * feats[2]

    for c0 in range(0, channels, WIDE):
        cs = pl.ds(c0, WIDE)
        pole = pole_ref[:, cs]

        def step(blk, acc):
            base = pl.multiple_of(blk * 8, 8)
            rows = pin_ref[pl.ds(base, 8), cs]
            for i in range(8):
                acc = pole * acc + jnp.broadcast_to(rows[i : i + 1, :], (modes, WIDE))
            return acc

        acc = lax.fori_loop(0, tok // 8, step, jnp.zeros((modes, WIDE), jnp.float32))
        end_ref[:, cs] = gain_ref[:, cs] * acc


def rows_summed(parts, sub):
    half = [
        jnp.where(sub < 4, parts[j] + pltpu.roll(parts[j], 4, 0), parts[j + 4] + pltpu.roll(parts[j + 4], 4, 0))
        for j in range(4)
    ]
    quarter = [
        jnp.where(sub % 4 < 2, half[j] + pltpu.roll(half[j], 6, 0), half[j + 2] + pltpu.roll(half[j + 2], 2, 0))
        for j in range(2)
    ]
    return jnp.where(
        sub % 2 == 0,
        quarter[0] + pltpu.roll(quarter[0], 7, 0),
        quarter[1] + pltpu.roll(quarter[1], 1, 0),
    )


def local_kernel(pin_ref, pole_ref, gain_ref, res_ref, out_ref, *, first):
    tok, channels = out_ref.shape
    modes = pole_ref.shape[0]
    sub = lax.broadcasted_iota(jnp.int32, (modes, WIDE), 0)
    for c0 in range(0, channels, WIDE):
        cs = pl.ds(first + c0, WIDE)
        ocs = pl.ds(c0, WIDE)
        pole = pole_ref[:, cs]
        gain = gain_ref[:, cs]
        res = res_ref[:, cs]

        def step(blk, state):
            base = pl.multiple_of(blk * 8, 8)
            rows = pin_ref[pl.ds(base, 8), cs]
            parts = []
            for i in range(8):
                state = pole * state + gain * jnp.broadcast_to(rows[i : i + 1, :], (modes, WIDE))
                parts.append(res * state)
            out_ref[pl.ds(base, 8), ocs] = rows_summed(parts, sub)
            return state

        lax.fori_loop(0, tok // 8, step, jnp.zeros((modes, WIDE), jnp.float32))


def finish_kernel(floc_a_ref, floc_b_ref, qc_ref, emb_ref, inc_ref, decay_ref, res_ref, out_ref):
    tok, channels = qc_ref.shape
    split = floc_a_ref.shape[1]
    modes = decay_ref.shape[0]
    later = (lax.broadcasted_iota(jnp.int32, (8, NARROW), 0) + 1).astype(jnp.float32)
    for c0 in range(0, channels, NARROW):
        cs = pl.ds(c0, NARROW)
        decay = decay_ref[:, cs]
        weight = res_ref[:, cs] * inc_ref[:, cs]
        terms = []
        steps = []
        for m in range(modes):
            rate = jnp.broadcast_to(decay[m : m + 1, :], (8, NARROW))
            terms.append(jnp.broadcast_to(weight[m : m + 1, :], (8, NARROW)) * jnp.exp(-rate * later))
            steps.append(jnp.exp(-rate * 8.0))

        def step(blk, terms):
            base = pl.multiple_of(blk * 16, 16)
            pieces = []
            for half in range(2):
                corr = terms[0]
                for m in range(1, modes):
                    corr = corr + terms[m]
                pieces.append(corr)
                terms = tuple(terms[m] * steps[m] for m in range(modes))
            corr = jnp.concatenate(pieces, axis=0)
            if c0 < split:
                local_part = floc_a_ref[pl.ds(base, 16), pl.ds(c0, NARROW)]
            else:
                local_part = floc_b_ref[pl.ds(base, 16), pl.ds(c0 - split, NARROW)]
            filtered = local_part + corr
            total = emb_ref[pl.ds(base, 16), cs].astype(jnp.float32) + qc_ref[pl.ds(base, 16), cs] * filtered
            out_ref[pl.ds(base, 16), cs] = total.astype(out_ref.dtype)
            return terms

        lax.fori_loop(0, tok // 16, step, tuple(terms))


def vmem_specs(count):
    return [pl.BlockSpec(memory_space=pltpu.VMEM)] * count


def front(qkv, tails, conv_weights, pole, gain):
    tok, channels = qkv.shape[1], qkv.shape[2]
    modes = pole.shape[0]
    return pl.pallas_call(
        front_kernel,
        out_shape=(
            jax.ShapeDtypeStruct((tok, channels), jnp.float32),
            jax.ShapeDtypeStruct((tok, channels), jnp.float32),
            jax.ShapeDtypeStruct((modes, channels), jnp.float32),
        ),
        in_specs=vmem_specs(5),
        out_specs=tuple(vmem_specs(3)),
        cost_estimate=pl.CostEstimate(
            flops=30 * tok * channels + 2 * tok * modes * channels,
            bytes_accessed=3 * tok * channels * 2 + 2 * tok * channels * 4,
            transcendentals=0,
        ),
    )(qkv, tails, conv_weights, pole, gain)


def local(pin, pole, gain, residues, first, channels):
    tok = pin.shape[0]
    modes = pole.shape[0]
    return pl.pallas_call(
        functools.partial(local_kernel, first=first),
        out_shape=jax.ShapeDtypeStruct((tok, channels), jnp.float32),
        in_specs=vmem_specs(4),
        out_specs=pl.BlockSpec(memory_space=pltpu.VMEM),
        cost_estimate=pl.CostEstimate(
            flops=10 * tok * modes * channels,
            bytes_accessed=tok * channels * 8,
            transcendentals=0,
        ),
    )(pin, pole, gain, residues)


def finish(floc_a, floc_b, qc, embedded, incoming, decay_rates, residues):
    tok, channels = qc.shape
    modes = decay_rates.shape[0]
    return pl.pallas_call(
        finish_kernel,
        out_shape=jax.ShapeDtypeStruct((tok, channels), jnp.bfloat16),
        in_specs=vmem_specs(7),
        out_specs=pl.BlockSpec(memory_space=pltpu.VMEM),
        cost_estimate=pl.CostEstimate(
            flops=2 * tok * modes * channels,
            bytes_accessed=tok * channels * (4 + 4 + 2 + 2),
            transcendentals=16 * modes * channels,
        ),
    )(floc_a, floc_b, qc, embedded, incoming, decay_rates, residues)


def butterfly(local_end, decay_rates, tok_local, axis, fillers):
    count = lax.axis_size(axis)
    me = lax.axis_index(axis)
    total = local_end
    prefix = jnp.zeros_like(local_end)
    done = []
    span = 1
    while span < count:
        pairs = [(i, i ^ span) for i in range(count)]
        other = lax.ppermute(total, axis, pairs)
        upper = (me & span) != 0
        offset = (me % span).astype(jnp.float32) * tok_local
        near = jnp.exp(-decay_rates * offset)
        far = jnp.exp(-decay_rates * float(span * tok_local))
        prefix = jnp.where(upper, prefix + near * other, prefix)
        total = jnp.where(upper, total + far * other, other + far * total)
        if fillers:
            prefix, total, made = lax.optimization_barrier((prefix, total, fillers.pop(0)()))
            done.append(made)
        span *= 2
    done.extend(filler() for filler in fillers)
    return prefix, total, done


def body(token_ids, embed_table, hyena_qkv, conv_weights, decay_rates, residues, prior_state):
    tok_local = hyena_qkv.shape[1]
    tap_count = conv_weights.shape[1]
    seq_count = lax.axis_size("seq")
    seq_index = lax.axis_index("seq")
    tails_local = hyena_qkv[:, tok_local - (tap_count - 1) :, :]
    tails_prev = shifted(tails_local, "seq", 1)
    pole = jnp.exp(-decay_rates)
    gain = jnp.sqrt(-jnp.expm1(-2.0 * decay_rates))
    qc, pin, local_end = front(hyena_qkv, tails_prev, conv_weights, pole, gain)
    channels = pin.shape[1]
    split = channels // 2
    fillers = [
        lambda: local(pin, pole, gain, residues, 0, split),
        lambda: local(pin, pole, gain, residues, split, channels - split),
    ]
    prefix, total, (floc_a, floc_b) = butterfly(local_end, decay_rates, tok_local, "seq", fillers)
    incoming = prefix + jnp.exp(-decay_rates * (seq_index.astype(jnp.float32) * tok_local)) * prior_state
    vocab_ids = jnp.arange(embed_table.shape[0], dtype=jnp.int32)
    one_hot = (token_ids[:, None] == vocab_ids[None, :]).astype(jnp.bfloat16)
    embedded = jnp.dot(one_hot, embed_table, preferred_element_type=jnp.float32).astype(jnp.bfloat16)
    hyena_out = finish(floc_a, floc_b, qc, embedded, incoming, decay_rates, residues)
    end_full = total + jnp.exp(-decay_rates * float(seq_count * tok_local)) * prior_state
    share_cols = end_full.shape[1] // seq_count
    end_state = lax.dynamic_slice_in_dim(end_full, seq_index * share_cols, share_cols, 1)
    return (hyena_out, end_state)


def solution(mesh):
    return jax.shard_map(
        body,
        mesh=mesh,
        in_specs=(
            P(("groups", "seq")),
            P(None, "tp"),
            P(None, ("groups", "seq"), "tp"),
            P(None, None, "tp"),
            P(None, "tp"),
            P(None, "tp"),
            P("groups", "tp"),
        ),
        out_specs=(P(("groups", "seq"), "tp"), P("groups", ("tp", "seq"))),
        check_vma=False,
    )
```

```python
import functools

import jax
import jax.numpy as jnp
from jax import lax
from jax.experimental import pallas as pl
from jax.experimental.pallas import tpu as pltpu
from jax.sharding import PartitionSpec as P

LANES = 256
WIDE = 1024
NARROW = 256


def shifted(array, axis, by):
    size = lax.axis_size(axis)
    pairs = [(i, i + by) for i in range(size) if 0 <= i + by < size]
    return lax.ppermute(array, axis, pairs)


def front_kernel(qkv_ref, w_ref, decay_ref, qc_ref, pin_ref, horner_ref, head_ref, tails_ref):
    tok, channels = qc_ref.shape
    modes = decay_ref.shape[0]
    history = tails_ref.shape[1]
    for member in range(3):
        tails_ref[member] = qkv_ref[member, tok - history :, :]
    for c0 in range(0, channels, LANES):
        cs = pl.ds(c0, LANES)
        row = lax.broadcasted_iota(jnp.int32, (tok, LANES), 0)
        feats = []
        for member in range(3):
            x = qkv_ref[member, :, cs].astype(jnp.float32)
            x1 = jnp.where(row < 1, 0.0, pltpu.roll(x, 1, 0))
            x2 = jnp.where(row < 2, 0.0, pltpu.roll(x, 2, 0))
            w = w_ref[member, :, cs]
            feat = w[0:1, :] * x + w[1:2, :] * x1 + w[2:3, :] * x2
            feats.append(feat)
            head_ref[member, :, cs] = feat[0:8, :]
        qc_ref[:, cs] = feats[0]
        pin_ref[:, cs] = feats[1] * feats[2]

    for c0 in range(0, channels, WIDE):
        cs = pl.ds(c0, WIDE)
        pole = jnp.exp(-decay_ref[:, cs])

        def step(blk, acc):
            base = pl.multiple_of(blk * 8, 8)
            rows = pin_ref[pl.ds(base, 8), cs]
            for i in range(8):
                acc = pole * acc + jnp.broadcast_to(rows[i : i + 1, :], (modes, WIDE))
            return acc

        horner_ref[:, cs] = lax.fori_loop(0, tok // 8, step, jnp.zeros((modes, WIDE), jnp.float32))


def rows_summed(parts, sub):
    half = [
        jnp.where(sub < 4, parts[j] + pltpu.roll(parts[j], 4, 0), parts[j + 4] + pltpu.roll(parts[j + 4], 4, 0))
        for j in range(4)
    ]
    quarter = [
        jnp.where(sub % 4 < 2, half[j] + pltpu.roll(half[j], 6, 0), half[j + 2] + pltpu.roll(half[j + 2], 2, 0))
        for j in range(2)
    ]
    return jnp.where(
        sub % 2 == 0,
        quarter[0] + pltpu.roll(quarter[0], 7, 0),
        quarter[1] + pltpu.roll(quarter[1], 1, 0),
    )


def local_kernel(pin_ref, pole_ref, gain_ref, res_ref, out_ref, *, first):
    tok, width = out_ref.shape
    modes = pole_ref.shape[0]
    sub = lax.broadcasted_iota(jnp.int32, (modes, width), 0)
    cs = pl.ds(first, width)
    pole = pole_ref[:, cs]
    gain = gain_ref[:, cs]
    res = res_ref[:, cs]

    def step(blk, state):
        base = pl.multiple_of(blk * 8, 8)
        rows = pin_ref[pl.ds(base, 8), cs]
        parts = []
        for i in range(8):
            state = pole * state + gain * jnp.broadcast_to(rows[i : i + 1, :], (modes, width))
            parts.append(res * state)
        out_ref[pl.ds(base, 8), :] = rows_summed(parts, sub)
        return state

    lax.fori_loop(0, tok // 8, step, jnp.zeros((modes, width), jnp.float32))


def tree_sum(values):
    while len(values) > 1:
        values = [values[i] + values[i + 1] for i in range(0, len(values) - 1, 2)] + (
            [values[-1]] if len(values) % 2 else []
        )
    return values[0]


def finish_kernel(*refs, bounds):
    count = len(bounds)
    local_refs = refs[:count]
    (qc_ref, emb_ref, prefix_ref, before_ref, a_ref, b_ref, c_ref, step_ref, jump_ref, fix_ref, unfix_ref, out_ref) = refs[
        count:
    ]
    tok, channels = qc_ref.shape
    modes = prefix_ref.shape[0]
    for c0 in range(0, channels, NARROW):
        cs = pl.ds(c0, NARROW)
        piece = max(i for i in range(count) if bounds[i] <= c0)
        local_ref = local_refs[piece]
        lcs = pl.ds(c0 - bounds[piece], NARROW)
        incoming = prefix_ref[:, cs] + before_ref[:, cs]
        jump = jump_ref[:, cs]
        first_jump = jnp.broadcast_to(jump[0:1, :], (8, NARROW))
        second_jump = jnp.broadcast_to(jump[1:2, :], (8, NARROW))
        steps = step_ref[:, cs]
        terms = []
        rates = []
        for m in range(modes):
            terms.append(
                a_ref[m, :, cs] * jnp.broadcast_to(incoming[m : m + 1, :], (8, NARROW))
                + b_ref[m, :, cs] * first_jump
                + c_ref[m, :, cs] * second_jump
            )
            rates.append(jnp.broadcast_to(steps[m : m + 1, :], (8, NARROW)))
        fix = fix_ref[:, cs]
        unfix = unfix_ref[:, cs]

        def step(blk, terms):
            base = pl.multiple_of(blk * 16, 16)
            pieces = []
            for half in range(2):
                pieces.append(tree_sum(list(terms)))
                terms = tuple(terms[m] * rates[m] for m in range(modes))
            corr = jnp.concatenate(pieces, axis=0)
            gate = (blk == 0).astype(jnp.float32)
            filtered = local_ref[pl.ds(base, 16), lcs] + corr + gate * unfix
            qc = qc_ref[pl.ds(base, 16), cs] + gate * fix
            total = emb_ref[pl.ds(base, 16), cs].astype(jnp.float32) + qc * filtered
            out_ref[pl.ds(base, 16), cs] = total.astype(out_ref.dtype)
            return terms

        lax.fori_loop(0, tok // 16, step, tuple(terms))


def vmem_specs(count):
    return [pl.BlockSpec(memory_space=pltpu.VMEM)] * count


def front(qkv, conv_weights, decay_rates, history):
    tok, channels = qkv.shape[1], qkv.shape[2]
    modes = decay_rates.shape[0]
    return pl.pallas_call(
        front_kernel,
        out_shape=(
            jax.ShapeDtypeStruct((tok, channels), jnp.float32),
            jax.ShapeDtypeStruct((tok, channels), jnp.float32),
            jax.ShapeDtypeStruct((modes, channels), jnp.float32),
            jax.ShapeDtypeStruct((3, 8, channels), jnp.float32),
            jax.ShapeDtypeStruct((3, history, channels), qkv.dtype),
        ),
        in_specs=vmem_specs(3),
        out_specs=tuple(vmem_specs(5)),
        cost_estimate=pl.CostEstimate(
            flops=30 * tok * channels + 2 * tok * modes * channels,
            bytes_accessed=3 * tok * channels * 2 + 2 * tok * channels * 4,
            transcendentals=modes * channels,
        ),
    )(qkv, conv_weights, decay_rates)


def local(pin, pole, gain, residues, first, width):
    tok = pin.shape[0]
    modes = pole.shape[0]
    return pl.pallas_call(
        functools.partial(local_kernel, first=first),
        out_shape=jax.ShapeDtypeStruct((tok, width), jnp.float32),
        in_specs=vmem_specs(4),
        out_specs=pl.BlockSpec(memory_space=pltpu.VMEM),
        cost_estimate=pl.CostEstimate(
            flops=10 * tok * modes * width,
            bytes_accessed=tok * width * 8,
            transcendentals=0,
        ),
    )(pin, pole, gain, residues)


def finish(locals_, bounds, qc, embedded, prefix, before, tables, steps, jumps, fix, unfix):
    tok, channels = qc.shape
    modes = prefix.shape[0]
    return pl.pallas_call(
        functools.partial(finish_kernel, bounds=tuple(bounds)),
        out_shape=jax.ShapeDtypeStruct((tok, channels), jnp.bfloat16),
        in_specs=vmem_specs(len(locals_) + 11),
        out_specs=pl.BlockSpec(memory_space=pltpu.VMEM),
        cost_estimate=pl.CostEstimate(
            flops=2 * tok * modes * channels,
            bytes_accessed=tok * channels * (4 + 4 + 2 + 2),
            transcendentals=0,
        ),
    )(*locals_, qc, embedded, prefix, before, *tables, steps, jumps, fix, unfix)


def butterfly(local_end, decay_rates, tok_local, axis, fillers):
    count = lax.axis_size(axis)
    me = lax.axis_index(axis)
    total = local_end
    prefix = jnp.zeros_like(local_end)
    done = []
    span = 1
    while span < count:
        pairs = [(i, i ^ span) for i in range(count)]
        other = lax.ppermute(total, axis, pairs)
        upper = (me & span) != 0
        offset = (me % span).astype(jnp.float32) * tok_local
        near = jnp.exp(-decay_rates * offset)
        far = jnp.exp(-decay_rates * float(span * tok_local))
        prefix = jnp.where(upper, prefix + near * other, prefix)
        total = jnp.where(upper, total + far * other, other + far * total)
        if fillers:
            prefix, total, made = lax.optimization_barrier((prefix, total, fillers.pop(0)()))
            done.append(made)
        span *= 2
    done.extend(filler() for filler in fillers)
    return prefix, total, done


def split_channels(channels, parts):
    tiles = channels // NARROW
    sizes = [tiles // parts] * parts
    sizes[0] += tiles - sum(sizes)
    bounds = [0]
    for size in sizes[:-1]:
        bounds.append(bounds[-1] + size * NARROW)
    return bounds, [size * NARROW for size in sizes]


def body(token_ids, embed_table, hyena_qkv, conv_weights, decay_rates, residues, prior_state):
    tok_local = hyena_qkv.shape[1]
    channels = hyena_qkv.shape[2]
    tap_count = conv_weights.shape[1]
    history = tap_count - 1
    seq_count = lax.axis_size("seq")
    seq_index = lax.axis_index("seq")

    qc, pin, horner, head, tails_local = front(hyena_qkv, conv_weights, decay_rates, history)
    pole = jnp.exp(-decay_rates)
    gain = jnp.sqrt(-jnp.expm1(-2.0 * decay_rates))
    bounds, widths = split_channels(channels, 3)
    fillers = [functools.partial(local, pin, pole, gain, residues, b, w) for b, w in zip(bounds, widths)]

    tails_prev = shifted(tails_local, "seq", 1)
    tails_prev, first_local = lax.optimization_barrier((tails_prev, fillers.pop(0)()))

    tails_f = tails_prev.astype(jnp.float32)
    extra = []
    for t in range(history):
        term = jnp.zeros((3, channels), jnp.float32)
        for tap in range(t + 1, tap_count):
            term = term + conv_weights[:, tap, :] * tails_f[:, history + t - tap, :]
        extra.append(term)
    extra = jnp.stack(extra, axis=1)
    true_head = head[:, :history, :] + extra
    jumps = true_head[1] * true_head[2] - head[1, :history, :] * head[2, :history, :]
    powers_end = [jnp.exp(-decay_rates * float(tok_local - 1 - t)) for t in range(history)]
    local_end = gain * (horner + sum(powers_end[t] * jumps[t][None, :] for t in range(history)))

    prefix, total, later_locals = butterfly(local_end, decay_rates, tok_local, "seq", fillers)
    locals_ = [first_local] + later_locals

    before = jnp.exp(-decay_rates * (seq_index.astype(jnp.float32) * tok_local)) * prior_state
    lag = jnp.arange(8, dtype=jnp.float32)[None, :, None]
    rate = decay_rates[:, None, :]
    weighted = (residues * gain)[:, None, :]
    table_a = residues[:, None, :] * jnp.exp(-rate * (lag + 1.0))
    table_b = weighted * jnp.exp(-rate * lag)
    table_c = weighted * jnp.exp(-rate * (lag - 1.0))
    ahead = jnp.sum((residues * gain) * jnp.exp(decay_rates), axis=0) * jumps[1]
    steps = jnp.exp(-decay_rates * 8.0)
    fix = jnp.zeros((16, channels), jnp.float32).at[:history].set(extra[0])
    unfix = jnp.zeros((16, channels), jnp.float32).at[0].set(-ahead)

    vocab_ids = jnp.arange(embed_table.shape[0], dtype=jnp.int32)
    one_hot = (token_ids[:, None] == vocab_ids[None, :]).astype(jnp.bfloat16)
    embedded = jnp.dot(one_hot, embed_table, preferred_element_type=jnp.float32).astype(jnp.bfloat16)
    hyena_out = finish(
        locals_, bounds, qc, embedded, prefix, before, (table_a, table_b, table_c), steps, jumps, fix, unfix
    )
    end_full = total + jnp.exp(-decay_rates * float(seq_count * tok_local)) * prior_state
    share_cols = end_full.shape[1] // seq_count
    end_state = lax.dynamic_slice_in_dim(end_full, seq_index * share_cols, share_cols, 1)
    return (hyena_out, end_state)


def solution(mesh):
    return jax.shard_map(
        body,
        mesh=mesh,
        in_specs=(
            P(("groups", "seq")),
            P(None, "tp"),
            P(None, ("groups", "seq"), "tp"),
            P(None, None, "tp"),
            P(None, "tp"),
            P(None, "tp"),
            P("groups", "tp"),
        ),
        out_specs=(P(("groups", "seq"), "tp"), P("groups", ("tp", "seq"))),
        check_vma=False,
    )
```

```python
import functools

import jax
import jax.numpy as jnp
from jax import lax
from jax.experimental import pallas as pl
from jax.experimental.pallas import tpu as pltpu
from jax.sharding import PartitionSpec as P

LANES = 256
WIDE = 1024
NARROW = 256
HORNER = 512


def shifted(array, axis, by):
    size = lax.axis_size(axis)
    pairs = [(i, i + by) for i in range(size) if 0 <= i + by < size]
    return lax.ppermute(array, axis, pairs)


def front_kernel(qkv_ref, w_ref, decay_ref, qc_ref, pin_ref, horner_ref, head_ref, tails_ref):
    tok, channels = qc_ref.shape
    modes = decay_ref.shape[0]
    history = tails_ref.shape[1]
    for member in range(3):
        tails_ref[member] = qkv_ref[member, tok - history :, :]
    for c0 in range(0, channels, LANES):
        cs = pl.ds(c0, LANES)
        row = lax.broadcasted_iota(jnp.int32, (tok, LANES), 0)
        feats = []
        for member in range(3):
            x = qkv_ref[member, :, cs].astype(jnp.float32)
            x1 = jnp.where(row < 1, 0.0, pltpu.roll(x, 1, 0))
            x2 = jnp.where(row < 2, 0.0, pltpu.roll(x, 2, 0))
            w = w_ref[member, :, cs]
            feat = w[0:1, :] * x + w[1:2, :] * x1 + w[2:3, :] * x2
            feats.append(feat)
            head_ref[member, :, cs] = feat[0:8, :]
        qc_ref[:, cs] = feats[0]
        pin_ref[:, cs] = feats[1] * feats[2]

    chains = 4
    span = tok // chains
    for c0 in range(0, channels, HORNER):
        cs = pl.ds(c0, HORNER)
        decay = decay_ref[:, cs]
        pole = jnp.exp(-decay)

        def step(blk, accs):
            accs = list(accs)
            for q in range(chains):
                base = pl.multiple_of(q * span + blk * 8, 8)
                rows = pin_ref[pl.ds(base, 8), cs]
                for i in range(8):
                    accs[q] = pole * accs[q] + jnp.broadcast_to(rows[i : i + 1, :], (modes, HORNER))
            return tuple(accs)

        zero = jnp.zeros((modes, HORNER), jnp.float32)
        accs = lax.fori_loop(0, span // 8, step, (zero,) * chains)
        total = accs[0]
        jump = jnp.exp(-decay * float(span))
        for q in range(1, chains):
            total = jump * total + accs[q]
        horner_ref[:, cs] = total


def rows_summed(parts, sub):
    half = [
        jnp.where(sub < 4, parts[j] + pltpu.roll(parts[j], 4, 0), parts[j + 4] + pltpu.roll(parts[j + 4], 4, 0))
        for j in range(4)
    ]
    quarter = [
        jnp.where(sub % 4 < 2, half[j] + pltpu.roll(half[j], 6, 0), half[j + 2] + pltpu.roll(half[j + 2], 2, 0))
        for j in range(2)
    ]
    return jnp.where(
        sub % 2 == 0,
        quarter[0] + pltpu.roll(quarter[0], 7, 0),
        quarter[1] + pltpu.roll(quarter[1], 1, 0),
    )


def local_kernel(pin_ref, pole_ref, gain_ref, res_ref, out_ref, *, first):
    tok, width = out_ref.shape
    modes = pole_ref.shape[0]
    sub = lax.broadcasted_iota(jnp.int32, (modes, width), 0)
    cs = pl.ds(first, width)
    pole = pole_ref[:, cs]
    gain = gain_ref[:, cs]
    res = res_ref[:, cs]

    def step(blk, state):
        base = pl.multiple_of(blk * 8, 8)
        rows = pin_ref[pl.ds(base, 8), cs]
        parts = []
        for i in range(8):
            state = pole * state + gain * jnp.broadcast_to(rows[i : i + 1, :], (modes, width))
            parts.append(res * state)
        out_ref[pl.ds(base, 8), :] = rows_summed(parts, sub)
        return state

    lax.fori_loop(0, tok // 8, step, jnp.zeros((modes, width), jnp.float32))


def tree_sum(values):
    while len(values) > 1:
        values = [values[i] + values[i + 1] for i in range(0, len(values) - 1, 2)] + (
            [values[-1]] if len(values) % 2 else []
        )
    return values[0]


def finish_kernel(*refs):
    (local_ref, qc_ref, emb_ref, prefix_ref, before_ref, a_ref, b_ref, c_ref, step_ref, jump_ref, fix_ref, unfix_ref,
     out_ref, terms_ref, rates_ref) = refs
    tok, channels = qc_ref.shape
    modes = prefix_ref.shape[0]
    for c0 in range(0, channels, NARROW):
        cs = pl.ds(c0, NARROW)
        incoming = prefix_ref[:, cs] + before_ref[:, cs]
        jump = jump_ref[:, cs]
        first_jump = jnp.broadcast_to(jump[0:1, :], (8, NARROW))
        second_jump = jnp.broadcast_to(jump[1:2, :], (8, NARROW))
        steps = step_ref[:, cs]
        for m in range(modes):
            terms_ref[m, :, cs] = (
                a_ref[m, :, cs] * jnp.broadcast_to(incoming[m : m + 1, :], (8, NARROW))
                + b_ref[m, :, cs] * first_jump
                + c_ref[m, :, cs] * second_jump
            )
            rates_ref[m, :, cs] = jnp.broadcast_to(steps[m : m + 1, :], (8, NARROW))

    def step(blk, carry):
        base = pl.multiple_of(blk * 16, 16)
        gate = (blk == 0).astype(jnp.float32)
        for c0 in range(0, channels, NARROW):
            cs = pl.ds(c0, NARROW)
            terms = [terms_ref[m, :, cs] for m in range(modes)]
            rates = [rates_ref[m, :, cs] for m in range(modes)]
            pieces = []
            for half in range(2):
                pieces.append(tree_sum(list(terms)))
                terms = [terms[m] * rates[m] for m in range(modes)]
            for m in range(modes):
                terms_ref[m, :, cs] = terms[m]
            corr = jnp.concatenate(pieces, axis=0)
            filtered = local_ref[pl.ds(base, 16), cs] + corr + gate * unfix_ref[:, cs]
            qc = qc_ref[pl.ds(base, 16), cs] + gate * fix_ref[:, cs]
            total = emb_ref[pl.ds(base, 16), cs].astype(jnp.float32) + qc * filtered
            out_ref[pl.ds(base, 16), cs] = total.astype(out_ref.dtype)
        return carry

    lax.fori_loop(0, tok // 16, step, 0)


def vmem_specs(count):
    return [pl.BlockSpec(memory_space=pltpu.VMEM)] * count


def front(qkv, conv_weights, decay_rates, history):
    tok, channels = qkv.shape[1], qkv.shape[2]
    modes = decay_rates.shape[0]
    return pl.pallas_call(
        front_kernel,
        out_shape=(
            jax.ShapeDtypeStruct((tok, channels), jnp.float32),
            jax.ShapeDtypeStruct((tok, channels), jnp.float32),
            jax.ShapeDtypeStruct((modes, channels), jnp.float32),
            jax.ShapeDtypeStruct((3, 8, channels), jnp.float32),
            jax.ShapeDtypeStruct((3, history, channels), qkv.dtype),
        ),
        in_specs=vmem_specs(3),
        out_specs=tuple(vmem_specs(5)),
        cost_estimate=pl.CostEstimate(
            flops=30 * tok * channels + 2 * tok * modes * channels,
            bytes_accessed=3 * tok * channels * 2 + 2 * tok * channels * 4,
            transcendentals=modes * channels,
        ),
    )(qkv, conv_weights, decay_rates)


def local(pin, pole, gain, residues, first, width):
    tok = pin.shape[0]
    modes = pole.shape[0]
    return pl.pallas_call(
        functools.partial(local_kernel, first=first),
        out_shape=jax.ShapeDtypeStruct((tok, width), jnp.float32),
        in_specs=vmem_specs(4),
        out_specs=pl.BlockSpec(memory_space=pltpu.VMEM),
        cost_estimate=pl.CostEstimate(
            flops=10 * tok * modes * width,
            bytes_accessed=tok * width * 8,
            transcendentals=0,
        ),
    )(pin, pole, gain, residues)


def finish(floc, qc, embedded, prefix, before, tables, steps, jumps, fix, unfix):
    tok, channels = qc.shape
    modes = prefix.shape[0]
    return pl.pallas_call(
        finish_kernel,
        out_shape=jax.ShapeDtypeStruct((tok, channels), jnp.bfloat16),
        in_specs=vmem_specs(12),
        out_specs=pl.BlockSpec(memory_space=pltpu.VMEM),
        scratch_shapes=[pltpu.VMEM((modes, 8, channels), jnp.float32)] * 2,
        cost_estimate=pl.CostEstimate(
            flops=2 * tok * modes * channels,
            bytes_accessed=tok * channels * (4 + 4 + 2 + 2),
            transcendentals=0,
        ),
    )(floc, qc, embedded, prefix, before, *tables, steps, jumps, fix, unfix)


def butterfly(local_end, decay_rates, tok_local, axis, fillers):
    count = lax.axis_size(axis)
    me = lax.axis_index(axis)
    total = local_end
    prefix = jnp.zeros_like(local_end)
    done = []
    span = 1
    while span < count:
        pairs = [(i, i ^ span) for i in range(count)]
        other = lax.ppermute(total, axis, pairs)
        upper = (me & span) != 0
        offset = (me % span).astype(jnp.float32) * tok_local
        near = jnp.exp(-decay_rates * offset)
        far = jnp.exp(-decay_rates * float(span * tok_local))
        prefix = jnp.where(upper, prefix + near * other, prefix)
        total = jnp.where(upper, total + far * other, other + far * total)
        if fillers:
            prefix, total, made = lax.optimization_barrier((prefix, total, fillers.pop(0)()))
            done.append(made)
        span *= 2
    done.extend(filler() for filler in fillers)
    return prefix, total, done


def body(token_ids, embed_table, hyena_qkv, conv_weights, decay_rates, residues, prior_state):
    tok_local = hyena_qkv.shape[1]
    channels = hyena_qkv.shape[2]
    tap_count = conv_weights.shape[1]
    history = tap_count - 1
    seq_count = lax.axis_size("seq")
    seq_index = lax.axis_index("seq")

    qc, pin, horner, head, tails_local = front(hyena_qkv, conv_weights, decay_rates, history)
    pole = jnp.exp(-decay_rates)
    gain = jnp.sqrt(-jnp.expm1(-2.0 * decay_rates))
    fillers = []

    tails_prev = shifted(tails_local, "seq", 1)
    tails_prev, floc = lax.optimization_barrier((tails_prev, local(pin, pole, gain, residues, 0, channels)))

    tails_f = tails_prev.astype(jnp.float32)
    extra = []
    for t in range(history):
        term = jnp.zeros((3, channels), jnp.float32)
        for tap in range(t + 1, tap_count):
            term = term + conv_weights[:, tap, :] * tails_f[:, history + t - tap, :]
        extra.append(term)
    extra = jnp.stack(extra, axis=1)
    true_head = head[:, :history, :] + extra
    jumps = true_head[1] * true_head[2] - head[1, :history, :] * head[2, :history, :]
    powers_end = [jnp.exp(-decay_rates * float(tok_local - 1 - t)) for t in range(history)]
    local_end = gain * (horner + sum(powers_end[t] * jumps[t][None, :] for t in range(history)))

    prefix, total, _ = butterfly(local_end, decay_rates, tok_local, "seq", fillers)

    before = jnp.exp(-decay_rates * (seq_index.astype(jnp.float32) * tok_local)) * prior_state
    lag = jnp.arange(8, dtype=jnp.float32)[None, :, None]
    rate = decay_rates[:, None, :]
    weighted = (residues * gain)[:, None, :]
    table_a = residues[:, None, :] * jnp.exp(-rate * (lag + 1.0))
    table_b = weighted * jnp.exp(-rate * lag)
    table_c = weighted * jnp.exp(-rate * (lag - 1.0))
    ahead = jnp.sum((residues * gain) * jnp.exp(decay_rates), axis=0) * jumps[1]
    steps = jnp.exp(-decay_rates * 8.0)
    fix = jnp.concatenate([extra[0], jnp.zeros((16 - history, channels), jnp.float32)], axis=0)
    unfix = jnp.concatenate([-ahead[None, :], jnp.zeros((15, channels), jnp.float32)], axis=0)

    vocab_ids = jnp.arange(embed_table.shape[0], dtype=jnp.int32)
    one_hot = (token_ids[:, None] == vocab_ids[None, :]).astype(jnp.bfloat16)
    embedded = jnp.dot(one_hot, embed_table, preferred_element_type=jnp.float32).astype(jnp.bfloat16)
    hyena_out = finish(
        floc, qc, embedded, prefix, before, (table_a, table_b, table_c), steps, jumps, fix, unfix
    )
    end_full = total + jnp.exp(-decay_rates * float(seq_count * tok_local)) * prior_state
    share_cols = end_full.shape[1] // seq_count
    end_state = lax.dynamic_slice_in_dim(end_full, seq_index * share_cols, share_cols, 1)
    return (hyena_out, end_state)


def solution(mesh):
    return jax.shard_map(
        body,
        mesh=mesh,
        in_specs=(
            P(("groups", "seq")),
            P(None, "tp"),
            P(None, ("groups", "seq"), "tp"),
            P(None, None, "tp"),
            P(None, "tp"),
            P(None, "tp"),
            P("groups", "tp"),
        ),
        out_specs=(P(("groups", "seq"), "tp"), P("groups", ("tp", "seq"))),
        check_vma=False,
    )
```

```python
import functools

import jax
import jax.numpy as jnp
from jax import lax
from jax.experimental import pallas as pl
from jax.experimental.pallas import tpu as pltpu
from jax.sharding import PartitionSpec as P

LANES = 256
WIDE = 1024
BLOCK = 1024


def shifted(array, axis, by):
    size = lax.axis_size(axis)
    pairs = [(i, i + by) for i in range(size) if 0 <= i + by < size]
    return lax.ppermute(array, axis, pairs)


def front_kernel(qkv_ref, tails_ref, w_ref, pole_ref, gain_ref, qc_ref, pin_ref, end_ref):
    tok, channels = qc_ref.shape
    modes = pole_ref.shape[0]
    for c0 in range(0, channels, LANES):
        cs = pl.ds(c0, LANES)
        row = lax.broadcasted_iota(jnp.int32, (tok, LANES), 0)
        feats = []
        for member in range(3):
            x = qkv_ref[member, :, cs].astype(jnp.float32)
            tl = tails_ref[member, :, cs].astype(jnp.float32)
            x1 = pltpu.roll(x, 1, 0)
            x1 = jnp.where(row == 0, tl[1:2, :], x1)
            x2 = pltpu.roll(x, 2, 0)
            x2 = jnp.where(row == 0, tl[0:1, :], jnp.where(row == 1, tl[1:2, :], x2))
            w = w_ref[member, :, cs]
            feats.append(w[0:1, :] * x + w[1:2, :] * x1 + w[2:3, :] * x2)
        qc_ref[:, cs] = feats[0]
        pin_ref[:, cs] = feats[1] * feats[2]

    for c0 in range(0, channels, WIDE):
        cs = pl.ds(c0, WIDE)
        pole = pole_ref[:, cs]

        def step(blk, acc):
            base = pl.multiple_of(blk * 8, 8)
            rows = pin_ref[pl.ds(base, 8), cs]
            for i in range(8):
                acc = pole * acc + jnp.broadcast_to(rows[i : i + 1, :], (modes, WIDE))
            return acc

        acc = lax.fori_loop(0, tok // 8, step, jnp.zeros((modes, WIDE), jnp.float32))
        end_ref[:, cs] = gain_ref[:, cs] * acc


def rows_summed(parts, sub):
    half = [
        jnp.where(sub < 4, parts[j] + pltpu.roll(parts[j], 4, 0), parts[j + 4] + pltpu.roll(parts[j + 4], 4, 0))
        for j in range(4)
    ]
    quarter = [
        jnp.where(sub % 4 < 2, half[j] + pltpu.roll(half[j], 6, 0), half[j + 2] + pltpu.roll(half[j + 2], 2, 0))
        for j in range(2)
    ]
    return jnp.where(
        sub % 2 == 0,
        quarter[0] + pltpu.roll(quarter[0], 7, 0),
        quarter[1] + pltpu.roll(quarter[1], 1, 0),
    )


def back_kernel(pin_ref, qc_ref, emb_ref, prefix_ref, before_ref, pole_ref, drive_ref, res_ref, out_ref):
    tok, channels = pin_ref.shape
    modes = pole_ref.shape[0]
    sub = lax.broadcasted_iota(jnp.int32, (modes, WIDE), 0)
    for c0 in range(0, channels, WIDE):
        cs = pl.ds(c0, WIDE)
        pole = pole_ref[:, cs]
        drive = drive_ref[:, cs]
        start = res_ref[:, cs] * (prefix_ref[:, cs] + before_ref[:, cs])

        def step(blk, state):
            base = pl.multiple_of(blk * 16, 16)
            rows = pin_ref[pl.ds(base, 16), cs]
            sums = []
            for half in range(2):
                parts = []
                for i in range(8):
                    r = half * 8 + i
                    state = pole * state + drive * jnp.broadcast_to(rows[r : r + 1, :], (modes, WIDE))
                    parts.append(state)
                sums.append(rows_summed(parts, sub))
            filtered = jnp.concatenate(sums, axis=0)
            total = emb_ref[pl.ds(base, 16), cs].astype(jnp.float32) + qc_ref[pl.ds(base, 16), cs] * filtered
            out_ref[pl.ds(base, 16), cs] = total.astype(out_ref.dtype)
            return state

        lax.fori_loop(0, tok // 16, step, start)


def vmem_specs(count):
    return [pl.BlockSpec(memory_space=pltpu.VMEM)] * count


def channel_spec(*lead):
    rank = len(lead) + 1
    return pl.BlockSpec(lead + (BLOCK,), lambda j: (0,) * (rank - 1) + (j,))


def front(qkv, tails, conv_weights, pole, gain):
    tok, channels = qkv.shape[1], qkv.shape[2]
    modes = pole.shape[0]
    taps = conv_weights.shape[1]
    return pl.pallas_call(
        front_kernel,
        out_shape=(
            jax.ShapeDtypeStruct((tok, channels), jnp.float32),
            jax.ShapeDtypeStruct((tok, channels), jnp.float32),
            jax.ShapeDtypeStruct((modes, channels), jnp.float32),
        ),
        grid=(channels // BLOCK,),
        in_specs=[
            channel_spec(3, tok),
            channel_spec(3, tails.shape[1]),
            channel_spec(3, taps),
            channel_spec(modes),
            channel_spec(modes),
        ],
        out_specs=(channel_spec(tok), channel_spec(tok), channel_spec(modes)),
        cost_estimate=pl.CostEstimate(
            flops=30 * tok * channels + 2 * tok * modes * channels,
            bytes_accessed=3 * tok * channels * 2 + 2 * tok * channels * 4,
            transcendentals=0,
        ),
    )(qkv, tails, conv_weights, pole, gain)


def back(pin, qc, embedded, prefix, before, pole, drive, residues):
    tok, channels = pin.shape
    modes = pole.shape[0]
    return pl.pallas_call(
        back_kernel,
        out_shape=jax.ShapeDtypeStruct((tok, channels), jnp.bfloat16),
        grid=(channels // BLOCK,),
        in_specs=[channel_spec(tok)] * 3 + [channel_spec(modes)] * 5,
        out_specs=channel_spec(tok),
        cost_estimate=pl.CostEstimate(
            flops=6 * tok * modes * channels,
            bytes_accessed=tok * channels * (4 + 4 + 2 + 2),
            transcendentals=0,
        ),
    )(pin, qc, embedded, prefix, before, pole, drive, residues)


def butterfly(local_end, decay_rates, tok_local, axis):
    count = lax.axis_size(axis)
    me = lax.axis_index(axis)
    total = local_end
    prefix = jnp.zeros_like(local_end)
    span = 1
    while span < count:
        pairs = [(i, i ^ span) for i in range(count)]
        other = lax.ppermute(total, axis, pairs)
        upper = (me & span) != 0
        offset = (me % span).astype(jnp.float32) * tok_local
        near = jnp.exp(-decay_rates * offset)
        far = jnp.exp(-decay_rates * float(span * tok_local))
        prefix = jnp.where(upper, prefix + near * other, prefix)
        total = jnp.where(upper, total + far * other, other + far * total)
        span *= 2
    return prefix, total


def body(token_ids, embed_table, hyena_qkv, conv_weights, decay_rates, residues, prior_state):
    tok_local = hyena_qkv.shape[1]
    tap_count = conv_weights.shape[1]
    seq_count = lax.axis_size("seq")
    seq_index = lax.axis_index("seq")
    tails_local = hyena_qkv[:, tok_local - (tap_count - 1) :, :]
    tails_prev = shifted(tails_local, "seq", 1)
    pole = jnp.exp(-decay_rates)
    gain = jnp.sqrt(-jnp.expm1(-2.0 * decay_rates))
    qc, pin, local_end = front(hyena_qkv, tails_prev, conv_weights, pole, gain)
    prefix, total = butterfly(local_end, decay_rates, tok_local, "seq")
    before = jnp.exp(-decay_rates * (seq_index.astype(jnp.float32) * tok_local)) * prior_state
    vocab_ids = jnp.arange(embed_table.shape[0], dtype=jnp.int32)
    one_hot = (token_ids[:, None] == vocab_ids[None, :]).astype(jnp.bfloat16)
    embedded = jnp.dot(one_hot, embed_table, preferred_element_type=jnp.float32).astype(jnp.bfloat16)
    hyena_out = back(pin, qc, embedded, prefix, before, pole, residues * gain, residues)
    end_full = total + jnp.exp(-decay_rates * float(seq_count * tok_local)) * prior_state
    share_cols = end_full.shape[1] // seq_count
    end_state = lax.dynamic_slice_in_dim(end_full, seq_index * share_cols, share_cols, 1)
    return (hyena_out, end_state)


def solution(mesh):
    return jax.shard_map(
        body,
        mesh=mesh,
        in_specs=(
            P(("groups", "seq")),
            P(None, "tp"),
            P(None, ("groups", "seq"), "tp"),
            P(None, None, "tp"),
            P(None, "tp"),
            P(None, "tp"),
            P("groups", "tp"),
        ),
        out_specs=(P(("groups", "seq"), "tp"), P("groups", ("tp", "seq"))),
        check_vma=False,
    )
```

```python
import functools

import jax
import jax.numpy as jnp
from jax import lax
from jax.experimental import pallas as pl
from jax.experimental.pallas import tpu as pltpu
from jax.sharding import PartitionSpec as P

LANES = 256
WIDE = 1024
BLOCK = 1024


def shifted(array, axis, by):
    size = lax.axis_size(axis)
    pairs = [(i, i + by) for i in range(size) if 0 <= i + by < size]
    return lax.ppermute(array, axis, pairs)


def front_kernel(qkv_ref, tails_ref, w_ref, pole_ref, gain_ref, qc_ref, pin_ref, end_ref):
    tok, channels = qc_ref.shape
    modes = pole_ref.shape[0]
    for c0 in range(0, channels, LANES):
        cs = pl.ds(c0, LANES)
        row = lax.broadcasted_iota(jnp.int32, (tok, LANES), 0)
        feats = []
        for member in range(3):
            x = qkv_ref[member, :, cs].astype(jnp.float32)
            tl = tails_ref[member, :, cs].astype(jnp.float32)
            x1 = pltpu.roll(x, 1, 0)
            x1 = jnp.where(row == 0, tl[1:2, :], x1)
            x2 = pltpu.roll(x, 2, 0)
            x2 = jnp.where(row == 0, tl[0:1, :], jnp.where(row == 1, tl[1:2, :], x2))
            w = w_ref[member, :, cs]
            feats.append(w[0:1, :] * x + w[1:2, :] * x1 + w[2:3, :] * x2)
        qc_ref[:, cs] = feats[0]
        pin_ref[:, cs] = feats[1] * feats[2]

    for c0 in range(0, channels, WIDE):
        cs = pl.ds(c0, WIDE)
        pole = pole_ref[:, cs]

        def step(blk, acc):
            base = pl.multiple_of(blk * 8, 8)
            rows = pin_ref[pl.ds(base, 8), cs]
            for i in range(8):
                acc = pole * acc + jnp.broadcast_to(rows[i : i + 1, :], (modes, WIDE))
            return acc

        acc = lax.fori_loop(0, tok // 8, step, jnp.zeros((modes, WIDE), jnp.float32))
        end_ref[:, cs] = gain_ref[:, cs] * acc


def rows_summed(parts, sub):
    half = [
        jnp.where(sub < 4, parts[j] + pltpu.roll(parts[j], 4, 0), parts[j + 4] + pltpu.roll(parts[j + 4], 4, 0))
        for j in range(4)
    ]
    quarter = [
        jnp.where(sub % 4 < 2, half[j] + pltpu.roll(half[j], 6, 0), half[j + 2] + pltpu.roll(half[j + 2], 2, 0))
        for j in range(2)
    ]
    return jnp.where(
        sub % 2 == 0,
        quarter[0] + pltpu.roll(quarter[0], 7, 0),
        quarter[1] + pltpu.roll(quarter[1], 1, 0),
    )


def back_kernel(pin_ref, qc_ref, emb_ref, prefix_ref, near_ref, other_ref, before_ref, pole_ref, drive_ref, res_ref, out_ref):
    tok, channels = pin_ref.shape
    modes = pole_ref.shape[0]
    sub = lax.broadcasted_iota(jnp.int32, (modes, WIDE), 0)
    for c0 in range(0, channels, WIDE):
        cs = pl.ds(c0, WIDE)
        pole = pole_ref[:, cs]
        drive = drive_ref[:, cs]
        incoming = prefix_ref[:, cs] + near_ref[:, cs] * other_ref[:, cs] + before_ref[:, cs]
        start = res_ref[:, cs] * incoming

        def step(blk, state):
            base = pl.multiple_of(blk * 16, 16)
            rows = pin_ref[pl.ds(base, 16), cs]
            sums = []
            for half in range(2):
                parts = []
                for i in range(8):
                    r = half * 8 + i
                    state = pole * state + drive * jnp.broadcast_to(rows[r : r + 1, :], (modes, WIDE))
                    parts.append(state)
                sums.append(rows_summed(parts, sub))
            filtered = jnp.concatenate(sums, axis=0)
            total = emb_ref[pl.ds(base, 16), cs].astype(jnp.float32) + qc_ref[pl.ds(base, 16), cs] * filtered
            out_ref[pl.ds(base, 16), cs] = total.astype(out_ref.dtype)
            return state

        lax.fori_loop(0, tok // 16, step, start)


def vmem_specs(count):
    return [pl.BlockSpec(memory_space=pltpu.VMEM)] * count


def channel_spec(*lead):
    rank = len(lead) + 1
    return pl.BlockSpec(lead + (BLOCK,), lambda j: (0,) * (rank - 1) + (j,))


def front(qkv, tails, conv_weights, pole, gain):
    tok, channels = qkv.shape[1], qkv.shape[2]
    modes = pole.shape[0]
    taps = conv_weights.shape[1]
    return pl.pallas_call(
        front_kernel,
        out_shape=(
            jax.ShapeDtypeStruct((tok, channels), jnp.float32),
            jax.ShapeDtypeStruct((tok, channels), jnp.float32),
            jax.ShapeDtypeStruct((modes, channels), jnp.float32),
        ),
        grid=(channels // BLOCK,),
        in_specs=[
            channel_spec(3, tok),
            channel_spec(3, tails.shape[1]),
            channel_spec(3, taps),
            channel_spec(modes),
            channel_spec(modes),
        ],
        out_specs=(channel_spec(tok), channel_spec(tok), channel_spec(modes)),
        cost_estimate=pl.CostEstimate(
            flops=30 * tok * channels + 2 * tok * modes * channels,
            bytes_accessed=3 * tok * channels * 2 + 2 * tok * channels * 4,
            transcendentals=0,
        ),
    )(qkv, tails, conv_weights, pole, gain)


def back(pin, qc, embedded, prefix, near, other, before, pole, drive, residues):
    tok, channels = pin.shape
    modes = pole.shape[0]
    return pl.pallas_call(
        back_kernel,
        out_shape=jax.ShapeDtypeStruct((tok, channels), jnp.bfloat16),
        grid=(channels // BLOCK,),
        in_specs=[channel_spec(tok)] * 3 + [channel_spec(modes)] * 7,
        out_specs=channel_spec(tok),
        cost_estimate=pl.CostEstimate(
            flops=6 * tok * modes * channels,
            bytes_accessed=tok * channels * (4 + 4 + 2 + 2),
            transcendentals=0,
        ),
    )(pin, qc, embedded, prefix, near, other, before, pole, drive, residues)


def butterfly(local_end, decay_rates, tok_local, axis):
    count = lax.axis_size(axis)
    me = lax.axis_index(axis)
    total = local_end
    prefix = jnp.zeros_like(local_end)
    span = 1
    while True:
        pairs = [(i, i ^ span) for i in range(count)]
        other = lax.ppermute(total, axis, pairs)
        upper = (me & span) != 0
        offset = (me % span).astype(jnp.float32) * tok_local
        near = jnp.where(upper, jnp.exp(-decay_rates * offset), 0.0)
        far = jnp.exp(-decay_rates * float(span * tok_local))
        keep = jnp.where(upper, 1.0, far)
        take = jnp.where(upper, far, 1.0)
        if span * 2 >= count:
            return prefix, near, other, total, keep, take
        prefix = prefix + near * other
        total = keep * total + take * other
        span *= 2


def body(token_ids, embed_table, hyena_qkv, conv_weights, decay_rates, residues, prior_state):
    tok_local = hyena_qkv.shape[1]
    channels = hyena_qkv.shape[2]
    tap_count = conv_weights.shape[1]
    seq_count = lax.axis_size("seq")
    seq_index = lax.axis_index("seq")
    tails_local = hyena_qkv[:, tok_local - (tap_count - 1) :, :]
    tails_prev = shifted(tails_local, "seq", 1)
    pole = jnp.exp(-decay_rates)
    gain = jnp.sqrt(-jnp.expm1(-2.0 * decay_rates))
    qc, pin, local_end = front(hyena_qkv, tails_prev, conv_weights, pole, gain)
    prefix, near, other, total, keep, take = butterfly(local_end, decay_rates, tok_local, "seq")
    before = jnp.exp(-decay_rates * (seq_index.astype(jnp.float32) * tok_local)) * prior_state
    vocab_ids = jnp.arange(embed_table.shape[0], dtype=jnp.int32)
    one_hot = (token_ids[:, None] == vocab_ids[None, :]).astype(jnp.bfloat16)
    embedded = jnp.dot(one_hot, embed_table, preferred_element_type=jnp.float32).astype(jnp.bfloat16)
    hyena_out = back(pin, qc, embedded, prefix, near, other, before, pole, residues * gain, residues)
    share_cols = channels // seq_count
    mine = lambda a: lax.dynamic_slice_in_dim(a, seq_index * share_cols, share_cols, 1)
    after = jnp.exp(-mine(decay_rates) * float(seq_count * tok_local)) * mine(prior_state)
    end_state = mine(keep) * mine(total) + mine(take) * mine(other) + after
    return (hyena_out, end_state)


def solution(mesh):
    return jax.shard_map(
        body,
        mesh=mesh,
        in_specs=(
            P(("groups", "seq")),
            P(None, "tp"),
            P(None, ("groups", "seq"), "tp"),
            P(None, None, "tp"),
            P(None, "tp"),
            P(None, "tp"),
            P("groups", "tp"),
        ),
        out_specs=(P(("groups", "seq"), "tp"), P("groups", ("tp", "seq"))),
        check_vma=False,
    )
```

```python
import functools

import jax
import jax.numpy as jnp
from jax import lax
from jax.experimental import pallas as pl
from jax.experimental.pallas import tpu as pltpu
from jax.sharding import PartitionSpec as P

LANES = 256
WIDE = 1024
BLOCK = 1024


def shifted(array, axis, by):
    size = lax.axis_size(axis)
    pairs = [(i, i + by) for i in range(size) if 0 <= i + by < size]
    return lax.ppermute(array, axis, pairs)


def front_kernel(qkv_ref, tails_ref, w_ref, pole_ref, gain_ref, qc_ref, pin_ref, end_ref):
    tok, channels = qc_ref.shape
    modes = pole_ref.shape[0]
    for c0 in range(0, channels, LANES):
        cs = pl.ds(c0, LANES)
        row = lax.broadcasted_iota(jnp.int32, (tok, LANES), 0)
        feats = []
        for member in range(3):
            x = qkv_ref[member, :, cs].astype(jnp.float32)
            tl = tails_ref[member, :, cs].astype(jnp.float32)
            x1 = pltpu.roll(x, 1, 0)
            x1 = jnp.where(row == 0, tl[1:2, :], x1)
            x2 = pltpu.roll(x, 2, 0)
            x2 = jnp.where(row == 0, tl[0:1, :], jnp.where(row == 1, tl[1:2, :], x2))
            w = w_ref[member, :, cs]
            feats.append(w[0:1, :] * x + w[1:2, :] * x1 + w[2:3, :] * x2)
        qc_ref[:, cs] = feats[0]
        pin_ref[:, cs] = feats[1] * feats[2]

    for c0 in range(0, channels, WIDE):
        cs = pl.ds(c0, WIDE)
        pole = pole_ref[:, cs]

        def step(blk, acc):
            base = pl.multiple_of(blk * 8, 8)
            rows = pin_ref[pl.ds(base, 8), cs]
            for i in range(8):
                acc = pole * acc + jnp.broadcast_to(rows[i : i + 1, :], (modes, WIDE))
            return acc

        acc = lax.fori_loop(0, tok // 8, step, jnp.zeros((modes, WIDE), jnp.float32))
        end_ref[:, cs] = gain_ref[:, cs] * acc


def rows_summed(parts, sub):
    half = [
        jnp.where(sub < 4, parts[j] + pltpu.roll(parts[j], 4, 0), parts[j + 4] + pltpu.roll(parts[j + 4], 4, 0))
        for j in range(4)
    ]
    quarter = [
        jnp.where(sub % 4 < 2, half[j] + pltpu.roll(half[j], 6, 0), half[j + 2] + pltpu.roll(half[j + 2], 2, 0))
        for j in range(2)
    ]
    return jnp.where(
        sub % 2 == 0,
        quarter[0] + pltpu.roll(quarter[0], 7, 0),
        quarter[1] + pltpu.roll(quarter[1], 1, 0),
    )


def back_kernel(pin_ref, qc_ref, emb_ref, prefix_ref, near_ref, other_ref, before_ref, pole_ref, drive_ref, res_ref, out_ref):
    tok, channels = pin_ref.shape
    modes = pole_ref.shape[0]
    sub = lax.broadcasted_iota(jnp.int32, (modes, WIDE), 0)
    for c0 in range(0, channels, WIDE):
        cs = pl.ds(c0, WIDE)
        pole = pole_ref[:, cs]
        drive = drive_ref[:, cs]
        incoming = prefix_ref[:, cs] + near_ref[:, cs] * other_ref[:, cs] + before_ref[:, cs]
        start = res_ref[:, cs] * incoming

        def step(blk, state):
            base = pl.multiple_of(blk * 16, 16)
            rows = pin_ref[pl.ds(base, 16), cs]
            sums = []
            for half in range(2):
                parts = []
                for i in range(8):
                    r = half * 8 + i
                    state = pole * state + drive * jnp.broadcast_to(rows[r : r + 1, :], (modes, WIDE))
                    parts.append(state)
                sums.append(rows_summed(parts, sub))
            filtered = jnp.concatenate(sums, axis=0)
            total = emb_ref[pl.ds(base, 16), cs].astype(jnp.float32) + qc_ref[pl.ds(base, 16), cs] * filtered
            out_ref[pl.ds(base, 16), cs] = total.astype(out_ref.dtype)
            return state

        lax.fori_loop(0, tok // 16, step, start)


def vmem_specs(count):
    return [pl.BlockSpec(memory_space=pltpu.VMEM)] * count


def channel_spec(*lead):
    rank = len(lead) + 1
    return pl.BlockSpec(lead + (BLOCK,), lambda j: (0,) * (rank - 1) + (j,))


def front(qkv, tails, conv_weights, pole, gain):
    tok, channels = qkv.shape[1], qkv.shape[2]
    modes = pole.shape[0]
    taps = conv_weights.shape[1]
    return pl.pallas_call(
        front_kernel,
        out_shape=(
            jax.ShapeDtypeStruct((tok, channels), jnp.float32),
            jax.ShapeDtypeStruct((tok, channels), jnp.float32),
            jax.ShapeDtypeStruct((modes, channels), jnp.float32),
        ),
        grid=(channels // BLOCK,),
        in_specs=[
            channel_spec(3, tok),
            channel_spec(3, tails.shape[1]),
            channel_spec(3, taps),
            channel_spec(modes),
            channel_spec(modes),
        ],
        out_specs=(channel_spec(tok), channel_spec(tok), channel_spec(modes)),
        cost_estimate=pl.CostEstimate(
            flops=30 * tok * channels + 2 * tok * modes * channels,
            bytes_accessed=3 * tok * channels * 2 + 2 * tok * channels * 4,
            transcendentals=0,
        ),
    )(qkv, tails, conv_weights, pole, gain)


def back(pin, qc, embedded, prefix, near, other, before, pole, drive, residues):
    tok, channels = pin.shape
    modes = pole.shape[0]
    return pl.pallas_call(
        back_kernel,
        out_shape=jax.ShapeDtypeStruct((tok, channels), jnp.bfloat16),
        grid=(channels // BLOCK,),
        in_specs=[channel_spec(tok)] * 3 + [channel_spec(modes)] * 7,
        out_specs=channel_spec(tok),
        cost_estimate=pl.CostEstimate(
            flops=6 * tok * modes * channels,
            bytes_accessed=tok * channels * (4 + 4 + 2 + 2),
            transcendentals=0,
        ),
    )(pin, qc, embedded, prefix, near, other, before, pole, drive, residues)


def round_factors(decay_rates, me, span, tok_local):
    upper = (me & span) != 0
    offset = (me % span).astype(jnp.float32) * tok_local
    near = jnp.where(upper, jnp.exp(-decay_rates * offset), 0.0)
    far = jnp.exp(-decay_rates * float(span * tok_local))
    return near, jnp.where(upper, 1.0, far), jnp.where(upper, far, 1.0)


def butterfly(local_end, factors, decay_rates, tok_local, axis, extra):
    count = lax.axis_size(axis)
    me = lax.axis_index(axis)
    total = local_end
    prefix = jnp.zeros_like(local_end)
    span = 1
    while True:
        pairs = [(i, i ^ span) for i in range(count)]
        other = lax.ppermute(total, axis, pairs)
        near, keep, take = factors
        if span * 2 >= count:
            other, extra = lax.optimization_barrier((other, extra))
            return prefix, near, other, total, keep, take, extra
        other, factors = lax.optimization_barrier((other, round_factors(decay_rates, me, span * 2, tok_local)))
        prefix = prefix + near * other
        total = keep * total + take * other
        span *= 2


def body(token_ids, embed_table, hyena_qkv, conv_weights, decay_rates, residues, prior_state):
    tok_local = hyena_qkv.shape[1]
    channels = hyena_qkv.shape[2]
    tap_count = conv_weights.shape[1]
    seq_count = lax.axis_size("seq")
    seq_index = lax.axis_index("seq")
    tails_local = hyena_qkv[:, tok_local - (tap_count - 1) :, :]
    tails_prev = shifted(tails_local, "seq", 1)
    tails_prev, factors = lax.optimization_barrier((tails_prev, round_factors(decay_rates, seq_index, 1, tok_local)))
    pole = jnp.exp(-decay_rates)
    gain = jnp.sqrt(-jnp.expm1(-2.0 * decay_rates))
    qc, pin, local_end = front(hyena_qkv, tails_prev, conv_weights, pole, gain)
    share_cols = channels // seq_count
    mine = lambda a: lax.dynamic_slice_in_dim(a, seq_index * share_cols, share_cols, 1)
    after = jnp.exp(-mine(decay_rates) * float(seq_count * tok_local)) * mine(prior_state)
    before = jnp.exp(-decay_rates * (seq_index.astype(jnp.float32) * tok_local)) * prior_state
    prefix, near, other, total, keep, take, (after, before) = butterfly(
        local_end, factors, decay_rates, tok_local, "seq", (after, before)
    )
    vocab_ids = jnp.arange(embed_table.shape[0], dtype=jnp.int32)
    one_hot = (token_ids[:, None] == vocab_ids[None, :]).astype(jnp.bfloat16)
    embedded = jnp.dot(one_hot, embed_table, preferred_element_type=jnp.float32).astype(jnp.bfloat16)
    hyena_out = back(pin, qc, embedded, prefix, near, other, before, pole, residues * gain, residues)
    end_state = mine(keep) * mine(total) + mine(take) * mine(other) + after
    return (hyena_out, end_state)


def solution(mesh):
    return jax.shard_map(
        body,
        mesh=mesh,
        in_specs=(
            P(("groups", "seq")),
            P(None, "tp"),
            P(None, ("groups", "seq"), "tp"),
            P(None, None, "tp"),
            P(None, "tp"),
            P(None, "tp"),
            P("groups", "tp"),
        ),
        out_specs=(P(("groups", "seq"), "tp"), P("groups", ("tp", "seq"))),
        check_vma=False,
    )
```

```python
import functools

import jax
import jax.numpy as jnp
from jax import lax
from jax.experimental import pallas as pl
from jax.experimental.pallas import tpu as pltpu
from jax.sharding import PartitionSpec as P

LANES = 256
WIDE = 1024
BLOCK = 1024


def shifted(array, axis, by):
    size = lax.axis_size(axis)
    pairs = [(i, i + by) for i in range(size) if 0 <= i + by < size]
    return lax.ppermute(array, axis, pairs)


def front_kernel(qkv_ref, tails_ref, w_ref, pole_ref, gain_ref, qc_ref, pin_ref, end_ref):
    tok, channels = qc_ref.shape
    modes = pole_ref.shape[0]
    for c0 in range(0, channels, LANES):
        cs = pl.ds(c0, LANES)
        row = lax.broadcasted_iota(jnp.int32, (tok, LANES), 0)
        feats = []
        for member in range(3):
            x = qkv_ref[member, :, cs].astype(jnp.float32)
            tl = tails_ref[member, :, cs].astype(jnp.float32)
            x1 = pltpu.roll(x, 1, 0)
            x1 = jnp.where(row == 0, tl[1:2, :], x1)
            x2 = pltpu.roll(x, 2, 0)
            x2 = jnp.where(row == 0, tl[0:1, :], jnp.where(row == 1, tl[1:2, :], x2))
            w = w_ref[member, :, cs]
            feats.append(w[0:1, :] * x + w[1:2, :] * x1 + w[2:3, :] * x2)
        qc_ref[:, cs] = feats[0]
        pin_ref[:, cs] = feats[1] * feats[2]

    for c0 in range(0, channels, WIDE):
        cs = pl.ds(c0, WIDE)
        pole = pole_ref[:, cs]

        def step(blk, acc):
            base = pl.multiple_of(blk * 8, 8)
            rows = pin_ref[pl.ds(base, 8), cs]
            for i in range(8):
                acc = pole * acc + jnp.broadcast_to(rows[i : i + 1, :], (modes, WIDE))
            return acc

        acc = lax.fori_loop(0, tok // 8, step, jnp.zeros((modes, WIDE), jnp.float32))
        end_ref[:, cs] = gain_ref[:, cs] * acc


def rows_summed(parts, sub):
    half = [
        jnp.where(sub < 4, parts[j] + pltpu.roll(parts[j], 4, 0), parts[j + 4] + pltpu.roll(parts[j + 4], 4, 0))
        for j in range(4)
    ]
    quarter = [
        jnp.where(sub % 4 < 2, half[j] + pltpu.roll(half[j], 6, 0), half[j + 2] + pltpu.roll(half[j + 2], 2, 0))
        for j in range(2)
    ]
    return jnp.where(
        sub % 2 == 0,
        quarter[0] + pltpu.roll(quarter[0], 7, 0),
        quarter[1] + pltpu.roll(quarter[1], 1, 0),
    )


def back_kernel(pin_ref, qc_ref, emb_ref, prefix_ref, near_ref, other_ref, before_ref, pole_ref, drive_ref, res_ref, out_ref):
    tok, channels = pin_ref.shape
    modes = pole_ref.shape[0]
    sub = lax.broadcasted_iota(jnp.int32, (modes, WIDE), 0)
    for c0 in range(0, channels, WIDE):
        cs = pl.ds(c0, WIDE)
        pole = pole_ref[:, cs]
        drive = drive_ref[:, cs]
        incoming = prefix_ref[:, cs] + near_ref[:, cs] * other_ref[:, cs] + before_ref[:, cs]
        start = res_ref[:, cs] * incoming

        def step(blk, state):
            base = pl.multiple_of(blk * 16, 16)
            rows = pin_ref[pl.ds(base, 16), cs]
            sums = []
            for half in range(2):
                parts = []
                for i in range(8):
                    r = half * 8 + i
                    state = pole * state + drive * jnp.broadcast_to(rows[r : r + 1, :], (modes, WIDE))
                    parts.append(state)
                sums.append(rows_summed(parts, sub))
            filtered = jnp.concatenate(sums, axis=0)
            total = emb_ref[pl.ds(base, 16), cs].astype(jnp.float32) + qc_ref[pl.ds(base, 16), cs] * filtered
            out_ref[pl.ds(base, 16), cs] = total.astype(out_ref.dtype)
            return state

        lax.fori_loop(0, tok // 16, step, start)


def vmem_specs(count):
    return [pl.BlockSpec(memory_space=pltpu.VMEM)] * count


def channel_spec(*lead):
    rank = len(lead) + 1
    return pl.BlockSpec(lead + (BLOCK,), lambda j: (0,) * (rank - 1) + (j,))


def front(qkv, tails, conv_weights, pole, gain):
    tok, channels = qkv.shape[1], qkv.shape[2]
    modes = pole.shape[0]
    taps = conv_weights.shape[1]
    return pl.pallas_call(
        front_kernel,
        out_shape=(
            jax.ShapeDtypeStruct((tok, channels), jnp.float32),
            jax.ShapeDtypeStruct((tok, channels), jnp.float32),
            jax.ShapeDtypeStruct((modes, channels), jnp.float32),
        ),
        grid=(channels // BLOCK,),
        in_specs=[
            channel_spec(3, tok),
            channel_spec(3, tails.shape[1]),
            channel_spec(3, taps),
            channel_spec(modes),
            channel_spec(modes),
        ],
        out_specs=(channel_spec(tok), channel_spec(tok), channel_spec(modes)),
        cost_estimate=pl.CostEstimate(
            flops=30 * tok * channels + 2 * tok * modes * channels,
            bytes_accessed=3 * tok * channels * 2 + 2 * tok * channels * 4,
            transcendentals=0,
        ),
    )(qkv, tails, conv_weights, pole, gain)


def back(pin, qc, embedded, prefix, near, other, before, pole, drive, residues):
    tok, channels = pin.shape
    modes = pole.shape[0]
    return pl.pallas_call(
        back_kernel,
        out_shape=jax.ShapeDtypeStruct((tok, channels), jnp.bfloat16),
        grid=(channels // BLOCK,),
        in_specs=[channel_spec(tok)] * 3 + [channel_spec(modes)] * 7,
        out_specs=channel_spec(tok),
        cost_estimate=pl.CostEstimate(
            flops=6 * tok * modes * channels,
            bytes_accessed=tok * channels * (4 + 4 + 2 + 2),
            transcendentals=0,
        ),
    )(pin, qc, embedded, prefix, near, other, before, pole, drive, residues)


def level_factors(decay_rates, me, block, radix, tok_local):
    digit = (me // block) % radix
    within = me % (block * radix)
    nears, takes = [], []
    for j in range(1, radix):
        theirs = digit ^ j
        lower = theirs < digit
        gap = jnp.where(lower, within - (theirs + 1) * block, 0).astype(jnp.float32) * tok_local
        nears.append(jnp.where(lower, jnp.exp(-decay_rates * gap), 0.0))
        takes.append(jnp.exp(-decay_rates * ((radix - 1 - theirs) * block * tok_local).astype(jnp.float32)))
    keep = jnp.exp(-decay_rates * ((radix - 1 - digit) * block * tok_local).astype(jnp.float32))
    return nears, keep, takes


def exchange_levels(count):
    levels = []
    while count > 4:
        levels.append(4)
        count //= 4
    return levels + [2] * (count.bit_length() - 1)


def butterfly(local_end, factors, decay_rates, tok_local, axis, levels, extra):
    count = lax.axis_size(axis)
    me = lax.axis_index(axis)
    total = local_end
    prefix = jnp.zeros_like(local_end)
    block = 1
    for level, radix in enumerate(levels):
        others = [
            lax.ppermute(total, axis, [(i, i ^ (j * block)) for i in range(count)]) for j in range(1, radix)
        ]
        nears, keep, takes = factors
        if level == len(levels) - 1:
            others, extra = lax.optimization_barrier((others, extra))
            return prefix, nears[0], others[0], total, keep, takes[0], extra
        nxt = level_factors(decay_rates, me, block * radix, levels[level + 1], tok_local)
        others, factors = lax.optimization_barrier((others, nxt))
        for near, other in zip(nears, others):
            prefix = prefix + near * other
        fresh = keep * total
        for take, other in zip(takes, others):
            fresh = fresh + take * other
        total = fresh
        block *= radix


def body(token_ids, embed_table, hyena_qkv, conv_weights, decay_rates, residues, prior_state):
    tok_local = hyena_qkv.shape[1]
    channels = hyena_qkv.shape[2]
    tap_count = conv_weights.shape[1]
    seq_count = lax.axis_size("seq")
    seq_index = lax.axis_index("seq")
    tails_local = hyena_qkv[:, tok_local - (tap_count - 1) :, :]
    tails_prev = shifted(tails_local, "seq", 1)
    levels = exchange_levels(seq_count)
    tails_prev, factors = lax.optimization_barrier(
        (tails_prev, level_factors(decay_rates, seq_index, 1, levels[0], tok_local))
    )
    pole = jnp.exp(-decay_rates)
    gain = jnp.sqrt(-jnp.expm1(-2.0 * decay_rates))
    qc, pin, local_end = front(hyena_qkv, tails_prev, conv_weights, pole, gain)
    share_cols = channels // seq_count
    mine = lambda a: lax.dynamic_slice_in_dim(a, seq_index * share_cols, share_cols, 1)
    after = jnp.exp(-mine(decay_rates) * float(seq_count * tok_local)) * mine(prior_state)
    before = jnp.exp(-decay_rates * (seq_index.astype(jnp.float32) * tok_local)) * prior_state
    prefix, near, other, total, keep, take, (after, before) = butterfly(
        local_end, factors, decay_rates, tok_local, "seq", levels, (after, before)
    )
    vocab_ids = jnp.arange(embed_table.shape[0], dtype=jnp.int32)
    one_hot = (token_ids[:, None] == vocab_ids[None, :]).astype(jnp.bfloat16)
    embedded = jnp.dot(one_hot, embed_table, preferred_element_type=jnp.float32).astype(jnp.bfloat16)
    hyena_out = back(pin, qc, embedded, prefix, near, other, before, pole, residues * gain, residues)
    end_state = mine(keep) * mine(total) + mine(take) * mine(other) + after
    return (hyena_out, end_state)


def solution(mesh):
    return jax.shard_map(
        body,
        mesh=mesh,
        in_specs=(
            P(("groups", "seq")),
            P(None, "tp"),
            P(None, ("groups", "seq"), "tp"),
            P(None, None, "tp"),
            P(None, "tp"),
            P(None, "tp"),
            P("groups", "tp"),
        ),
        out_specs=(P(("groups", "seq"), "tp"), P("groups", ("tp", "seq"))),
        check_vma=False,
    )
```

```python
import functools

import jax
import jax.numpy as jnp
from jax import lax
from jax.experimental import pallas as pl
from jax.experimental.pallas import tpu as pltpu
from jax.sharding import PartitionSpec as P

LANES = 256
WIDE = 1024
BLOCK = 1024


def shifted(array, axis, by):
    size = lax.axis_size(axis)
    pairs = [(i, i + by) for i in range(size) if 0 <= i + by < size]
    return lax.ppermute(array, axis, pairs)


def front_kernel(qkv_ref, tails_ref, w_ref, decay_ref, gain_ref, qc_ref, pin_ref, end_ref):
    tok, channels = qc_ref.shape
    modes = decay_ref.shape[0]
    for c0 in range(0, channels, LANES):
        cs = pl.ds(c0, LANES)
        row = lax.broadcasted_iota(jnp.int32, (tok, LANES), 0)
        feats = []
        for member in range(3):
            x = qkv_ref[member, :, cs].astype(jnp.float32)
            tl = tails_ref[member, :, cs].astype(jnp.float32)
            x1 = pltpu.roll(x, 1, 0)
            x1 = jnp.where(row == 0, tl[1:2, :], x1)
            x2 = pltpu.roll(x, 2, 0)
            x2 = jnp.where(row == 0, tl[0:1, :], jnp.where(row == 1, tl[1:2, :], x2))
            w = w_ref[member, :, cs]
            feats.append(w[0:1, :] * x + w[1:2, :] * x1 + w[2:3, :] * x2)
        qc_ref[:, cs] = feats[0]
        pin_ref[:, cs] = feats[1] * feats[2]

    sub = lax.broadcasted_iota(jnp.int32, (8, LANES), 0)
    to_end = (7 - sub).astype(jnp.float32)
    for c0 in range(0, channels, LANES):
        cs = pl.ds(c0, LANES)
        decay = decay_ref[:, cs]
        rates = [jnp.broadcast_to(decay[m : m + 1, :], (8, LANES)) for m in range(modes)]
        jumps = [jnp.exp(-rate * 8.0) for rate in rates]

        def step(blk, accs):
            base = pl.multiple_of(blk * 8, 8)
            rows = pin_ref[pl.ds(base, 8), cs]
            return tuple(jumps[m] * accs[m] + rows for m in range(modes))

        zero = jnp.zeros((8, LANES), jnp.float32)
        accs = lax.fori_loop(0, tok // 8, step, (zero,) * modes)
        parts = [jnp.exp(-rates[m] * to_end) * accs[m] for m in range(modes)]
        end_ref[:, cs] = gain_ref[:, cs] * rows_summed(parts, sub)


def rows_summed(parts, sub):
    half = [
        jnp.where(sub < 4, parts[j] + pltpu.roll(parts[j], 4, 0), parts[j + 4] + pltpu.roll(parts[j + 4], 4, 0))
        for j in range(4)
    ]
    quarter = [
        jnp.where(sub % 4 < 2, half[j] + pltpu.roll(half[j], 6, 0), half[j + 2] + pltpu.roll(half[j + 2], 2, 0))
        for j in range(2)
    ]
    return jnp.where(
        sub % 2 == 0,
        quarter[0] + pltpu.roll(quarter[0], 7, 0),
        quarter[1] + pltpu.roll(quarter[1], 1, 0),
    )


def back_kernel(pin_ref, qc_ref, emb_ref, prefix_ref, near_ref, other_ref, before_ref, pole_ref, drive_ref, res_ref, out_ref):
    tok, channels = pin_ref.shape
    modes = pole_ref.shape[0]
    sub = lax.broadcasted_iota(jnp.int32, (modes, WIDE), 0)
    for c0 in range(0, channels, WIDE):
        cs = pl.ds(c0, WIDE)
        pole = pole_ref[:, cs]
        drive = drive_ref[:, cs]
        incoming = prefix_ref[:, cs] + near_ref[:, cs] * other_ref[:, cs] + before_ref[:, cs]
        start = res_ref[:, cs] * incoming

        def step(blk, state):
            base = pl.multiple_of(blk * 16, 16)
            rows = pin_ref[pl.ds(base, 16), cs]
            sums = []
            for half in range(2):
                parts = []
                for i in range(8):
                    r = half * 8 + i
                    state = pole * state + drive * jnp.broadcast_to(rows[r : r + 1, :], (modes, WIDE))
                    parts.append(state)
                sums.append(rows_summed(parts, sub))
            filtered = jnp.concatenate(sums, axis=0)
            total = emb_ref[pl.ds(base, 16), cs].astype(jnp.float32) + qc_ref[pl.ds(base, 16), cs] * filtered
            out_ref[pl.ds(base, 16), cs] = total.astype(out_ref.dtype)
            return state

        lax.fori_loop(0, tok // 16, step, start)


def vmem_specs(count):
    return [pl.BlockSpec(memory_space=pltpu.VMEM)] * count


def channel_spec(*lead):
    rank = len(lead) + 1
    return pl.BlockSpec(lead + (BLOCK,), lambda j: (0,) * (rank - 1) + (j,))


def front(qkv, tails, conv_weights, decay_rates, gain):
    tok, channels = qkv.shape[1], qkv.shape[2]
    modes = decay_rates.shape[0]
    taps = conv_weights.shape[1]
    return pl.pallas_call(
        front_kernel,
        out_shape=(
            jax.ShapeDtypeStruct((tok, channels), jnp.float32),
            jax.ShapeDtypeStruct((tok, channels), jnp.float32),
            jax.ShapeDtypeStruct((modes, channels), jnp.float32),
        ),
        grid=(channels // BLOCK,),
        in_specs=[
            channel_spec(3, tok),
            channel_spec(3, tails.shape[1]),
            channel_spec(3, taps),
            channel_spec(modes),
            channel_spec(modes),
        ],
        out_specs=(channel_spec(tok), channel_spec(tok), channel_spec(modes)),
        cost_estimate=pl.CostEstimate(
            flops=30 * tok * channels + 2 * tok * modes * channels,
            bytes_accessed=3 * tok * channels * 2 + 2 * tok * channels * 4,
            transcendentals=0,
        ),
    )(qkv, tails, conv_weights, decay_rates, gain)


def back(pin, qc, embedded, prefix, near, other, before, pole, drive, residues):
    tok, channels = pin.shape
    modes = pole.shape[0]
    return pl.pallas_call(
        back_kernel,
        out_shape=jax.ShapeDtypeStruct((tok, channels), jnp.bfloat16),
        grid=(channels // BLOCK,),
        in_specs=[channel_spec(tok)] * 3 + [channel_spec(modes)] * 7,
        out_specs=channel_spec(tok),
        cost_estimate=pl.CostEstimate(
            flops=6 * tok * modes * channels,
            bytes_accessed=tok * channels * (4 + 4 + 2 + 2),
            transcendentals=0,
        ),
    )(pin, qc, embedded, prefix, near, other, before, pole, drive, residues)


def level_factors(decay_rates, me, block, radix, tok_local):
    digit = (me // block) % radix
    within = me % (block * radix)
    nears, takes = [], []
    for j in range(1, radix):
        theirs = digit ^ j
        lower = theirs < digit
        gap = jnp.where(lower, within - (theirs + 1) * block, 0).astype(jnp.float32) * tok_local
        nears.append(jnp.where(lower, jnp.exp(-decay_rates * gap), 0.0))
        takes.append(jnp.exp(-decay_rates * ((radix - 1 - theirs) * block * tok_local).astype(jnp.float32)))
    keep = jnp.exp(-decay_rates * ((radix - 1 - digit) * block * tok_local).astype(jnp.float32))
    return nears, keep, takes


def exchange_levels(count):
    levels = []
    while count > 4:
        levels.append(4)
        count //= 4
    return levels + [2] * (count.bit_length() - 1)


def butterfly(local_end, factors, decay_rates, tok_local, axis, levels, extra):
    count = lax.axis_size(axis)
    me = lax.axis_index(axis)
    total = local_end
    prefix = jnp.zeros_like(local_end)
    block = 1
    for level, radix in enumerate(levels):
        others = [
            lax.ppermute(total, axis, [(i, i ^ (j * block)) for i in range(count)]) for j in range(1, radix)
        ]
        nears, keep, takes = factors
        if level == len(levels) - 1:
            others, extra = lax.optimization_barrier((others, extra))
            return prefix, nears[0], others[0], total, keep, takes[0], extra
        nxt = level_factors(decay_rates, me, block * radix, levels[level + 1], tok_local)
        others, factors = lax.optimization_barrier((others, nxt))
        for near, other in zip(nears, others):
            prefix = prefix + near * other
        fresh = keep * total
        for take, other in zip(takes, others):
            fresh = fresh + take * other
        total = fresh
        block *= radix


def body(token_ids, embed_table, hyena_qkv, conv_weights, decay_rates, residues, prior_state):
    tok_local = hyena_qkv.shape[1]
    channels = hyena_qkv.shape[2]
    tap_count = conv_weights.shape[1]
    seq_count = lax.axis_size("seq")
    seq_index = lax.axis_index("seq")
    tails_local = hyena_qkv[:, tok_local - (tap_count - 1) :, :]
    tails_prev = shifted(tails_local, "seq", 1)
    levels = exchange_levels(seq_count)
    tails_prev, factors = lax.optimization_barrier(
        (tails_prev, level_factors(decay_rates, seq_index, 1, levels[0], tok_local))
    )
    pole = jnp.exp(-decay_rates)
    gain = jnp.sqrt(-jnp.expm1(-2.0 * decay_rates))
    qc, pin, local_end = front(hyena_qkv, tails_prev, conv_weights, decay_rates, gain)
    share_cols = channels // seq_count
    mine = lambda a: lax.dynamic_slice_in_dim(a, seq_index * share_cols, share_cols, 1)
    after = jnp.exp(-mine(decay_rates) * float(seq_count * tok_local)) * mine(prior_state)
    before = jnp.exp(-decay_rates * (seq_index.astype(jnp.float32) * tok_local)) * prior_state
    prefix, near, other, total, keep, take, (after, before) = butterfly(
        local_end, factors, decay_rates, tok_local, "seq", levels, (after, before)
    )
    vocab_ids = jnp.arange(embed_table.shape[0], dtype=jnp.int32)
    one_hot = (token_ids[:, None] == vocab_ids[None, :]).astype(jnp.bfloat16)
    embedded = jnp.dot(one_hot, embed_table, preferred_element_type=jnp.float32).astype(jnp.bfloat16)
    hyena_out = back(pin, qc, embedded, prefix, near, other, before, pole, residues * gain, residues)
    end_state = mine(keep) * mine(total) + mine(take) * mine(other) + after
    return (hyena_out, end_state)


def solution(mesh):
    return jax.shard_map(
        body,
        mesh=mesh,
        in_specs=(
            P(("groups", "seq")),
            P(None, "tp"),
            P(None, ("groups", "seq"), "tp"),
            P(None, None, "tp"),
            P(None, "tp"),
            P(None, "tp"),
            P("groups", "tp"),
        ),
        out_specs=(P(("groups", "seq"), "tp"), P("groups", ("tp", "seq"))),
        check_vma=False,
    )
```

```python
import functools

import jax
import jax.numpy as jnp
from jax import lax
from jax.experimental import pallas as pl
from jax.experimental.pallas import tpu as pltpu
from jax.sharding import PartitionSpec as P

LANES = 256
WIDE = 1024
BLOCK = 1024


def shifted(array, axis, by):
    size = lax.axis_size(axis)
    pairs = [(i, i + by) for i in range(size) if 0 <= i + by < size]
    return lax.ppermute(array, axis, pairs)


def front_kernel(qkv_ref, tails_ref, w_ref, pole_ref, gain_ref, qc_ref, pin_ref, end_ref):
    tok, channels = qc_ref.shape
    modes = pole_ref.shape[0]
    for c0 in range(0, channels, LANES):
        cs = pl.ds(c0, LANES)
        row = lax.broadcasted_iota(jnp.int32, (tok, LANES), 0)
        feats = []
        for member in range(3):
            x = qkv_ref[member, :, cs].astype(jnp.float32)
            tl = tails_ref[member, :, cs].astype(jnp.float32)
            x1 = pltpu.roll(x, 1, 0)
            x1 = jnp.where(row == 0, tl[1:2, :], x1)
            x2 = pltpu.roll(x, 2, 0)
            x2 = jnp.where(row == 0, tl[0:1, :], jnp.where(row == 1, tl[1:2, :], x2))
            w = w_ref[member, :, cs]
            feats.append(w[0:1, :] * x + w[1:2, :] * x1 + w[2:3, :] * x2)
        qc_ref[:, cs] = feats[0]
        pin_ref[:, cs] = feats[1] * feats[2]

    for c0 in range(0, channels, WIDE):
        cs = pl.ds(c0, WIDE)
        pole = pole_ref[:, cs]

        def step(blk, acc):
            base = pl.multiple_of(blk * 8, 8)
            rows = pin_ref[pl.ds(base, 8), cs]
            for i in range(8):
                acc = pole * acc + jnp.broadcast_to(rows[i : i + 1, :], (modes, WIDE))
            return acc

        acc = lax.fori_loop(0, tok // 8, step, jnp.zeros((modes, WIDE), jnp.float32))
        end_ref[:, cs] = gain_ref[:, cs] * acc


def rows_summed(parts, sub):
    half = [
        jnp.where(sub < 4, parts[j] + pltpu.roll(parts[j], 4, 0), parts[j + 4] + pltpu.roll(parts[j + 4], 4, 0))
        for j in range(4)
    ]
    quarter = [
        jnp.where(sub % 4 < 2, half[j] + pltpu.roll(half[j], 6, 0), half[j + 2] + pltpu.roll(half[j + 2], 2, 0))
        for j in range(2)
    ]
    return jnp.where(
        sub % 2 == 0,
        quarter[0] + pltpu.roll(quarter[0], 7, 0),
        quarter[1] + pltpu.roll(quarter[1], 1, 0),
    )


def back_kernel(pin_ref, qc_ref, emb_ref, prefix_ref, near_ref, other_ref, before_ref, pole_ref, drive_ref, res_ref, out_ref):
    tok, channels = pin_ref.shape
    modes = pole_ref.shape[0]
    sub = lax.broadcasted_iota(jnp.int32, (modes, WIDE), 0)
    for c0 in range(0, channels, WIDE):
        cs = pl.ds(c0, WIDE)
        pole = pole_ref[:, cs]
        drive = drive_ref[:, cs]
        incoming = prefix_ref[:, cs] + near_ref[:, cs] * other_ref[:, cs] + before_ref[:, cs]
        start = res_ref[:, cs] * incoming

        def step(blk, state):
            base = pl.multiple_of(blk * 16, 16)
            rows = pin_ref[pl.ds(base, 16), cs]
            sums = []
            for half in range(2):
                parts = []
                for i in range(8):
                    r = half * 8 + i
                    state = pole * state + drive * jnp.broadcast_to(rows[r : r + 1, :], (modes, WIDE))
                    parts.append(state)
                sums.append(rows_summed(parts, sub))
            filtered = jnp.concatenate(sums, axis=0)
            total = emb_ref[pl.ds(base, 16), cs].astype(jnp.float32) + qc_ref[pl.ds(base, 16), cs] * filtered
            out_ref[pl.ds(base, 16), cs] = total.astype(out_ref.dtype)
            return state

        lax.fori_loop(0, tok // 16, step, start)


def vmem_specs(count):
    return [pl.BlockSpec(memory_space=pltpu.VMEM)] * count


def channel_spec(*lead):
    rank = len(lead) + 1
    return pl.BlockSpec(lead + (BLOCK,), lambda j: (0,) * (rank - 1) + (j,))


def front(qkv, tails, conv_weights, pole, gain):
    tok, channels = qkv.shape[1], qkv.shape[2]
    modes = pole.shape[0]
    taps = conv_weights.shape[1]
    return pl.pallas_call(
        front_kernel,
        out_shape=(
            jax.ShapeDtypeStruct((tok, channels), jnp.float32),
            jax.ShapeDtypeStruct((tok, channels), jnp.float32),
            jax.ShapeDtypeStruct((modes, channels), jnp.float32),
        ),
        grid=(channels // BLOCK,),
        in_specs=[
            channel_spec(3, tok),
            channel_spec(3, tails.shape[1]),
            channel_spec(3, taps),
            channel_spec(modes),
            channel_spec(modes),
        ],
        out_specs=(channel_spec(tok), channel_spec(tok), channel_spec(modes)),
        cost_estimate=pl.CostEstimate(
            flops=30 * tok * channels + 2 * tok * modes * channels,
            bytes_accessed=3 * tok * channels * 2 + 2 * tok * channels * 4,
            transcendentals=0,
        ),
    )(qkv, tails, conv_weights, pole, gain)


def back(pin, qc, embedded, prefix, near, other, before, pole, drive, residues):
    tok, channels = pin.shape
    modes = pole.shape[0]
    return pl.pallas_call(
        back_kernel,
        out_shape=jax.ShapeDtypeStruct((tok, channels), jnp.bfloat16),
        grid=(channels // BLOCK,),
        in_specs=[channel_spec(tok)] * 3 + [channel_spec(modes)] * 7,
        out_specs=channel_spec(tok),
        cost_estimate=pl.CostEstimate(
            flops=6 * tok * modes * channels,
            bytes_accessed=tok * channels * (4 + 4 + 2 + 2),
            transcendentals=0,
        ),
    )(pin, qc, embedded, prefix, near, other, before, pole, drive, residues)


def level_factors(decay_rates, me, block, radix, tok_local):
    digit = (me // block) % radix
    within = me % (block * radix)
    nears, takes = [], []
    for j in range(1, radix):
        theirs = digit ^ j
        lower = theirs < digit
        gap = jnp.where(lower, within - (theirs + 1) * block, 0).astype(jnp.float32) * tok_local
        nears.append(jnp.where(lower, jnp.exp(-decay_rates * gap), 0.0))
        takes.append(jnp.exp(-decay_rates * ((radix - 1 - theirs) * block * tok_local).astype(jnp.float32)))
    keep = jnp.exp(-decay_rates * ((radix - 1 - digit) * block * tok_local).astype(jnp.float32))
    return nears, keep, takes


def exchange_levels(count):
    levels = []
    while count > 4:
        levels.append(4)
        count //= 4
    return levels + [2] * (count.bit_length() - 1)


def butterfly(local_end, factors, decay_rates, tok_local, axis, levels, extra):
    count = lax.axis_size(axis)
    me = lax.axis_index(axis)
    total = local_end
    prefix = jnp.zeros_like(local_end)
    block = 1
    for level, radix in enumerate(levels):
        others = [
            lax.ppermute(total, axis, [(i, i ^ (j * block)) for i in range(count)]) for j in range(1, radix)
        ]
        nears, keep, takes = factors
        if level == len(levels) - 1:
            others, extra = lax.optimization_barrier((others, extra))
            return prefix, nears[0], others[0], total, keep, takes[0], extra
        nxt = level_factors(decay_rates, me, block * radix, levels[level + 1], tok_local)
        others, factors = lax.optimization_barrier((others, nxt))
        for near, other in zip(nears, others):
            prefix = prefix + near * other
        fresh = keep * total
        for take, other in zip(takes, others):
            fresh = fresh + take * other
        total = fresh
        block *= radix


def body(token_ids, embed_table, hyena_qkv, conv_weights, decay_rates, residues, prior_state):
    tok_local = hyena_qkv.shape[1]
    channels = hyena_qkv.shape[2]
    tap_count = conv_weights.shape[1]
    seq_count = lax.axis_size("seq")
    seq_index = lax.axis_index("seq")
    tails_local = hyena_qkv[:, tok_local - (tap_count - 1) :, :]
    ring = [(i, (i + 1) % seq_count) for i in range(seq_count)]
    tails_prev = lax.ppermute(tails_local, "seq", ring)
    tails_prev = jnp.where(seq_index == 0, jnp.zeros_like(tails_prev), tails_prev)
    levels = exchange_levels(seq_count)
    tails_prev, factors = lax.optimization_barrier(
        (tails_prev, level_factors(decay_rates, seq_index, 1, levels[0], tok_local))
    )
    pole = jnp.exp(-decay_rates)
    gain = jnp.sqrt(-jnp.expm1(-2.0 * decay_rates))
    qc, pin, local_end = front(hyena_qkv, tails_prev, conv_weights, pole, gain)
    share_cols = channels // seq_count
    mine = lambda a: lax.dynamic_slice_in_dim(a, seq_index * share_cols, share_cols, 1)
    after = jnp.exp(-mine(decay_rates) * float(seq_count * tok_local)) * mine(prior_state)
    before = jnp.exp(-decay_rates * (seq_index.astype(jnp.float32) * tok_local)) * prior_state
    prefix, near, other, total, keep, take, (after, before) = butterfly(
        local_end, factors, decay_rates, tok_local, "seq", levels, (after, before)
    )
    vocab_ids = jnp.arange(embed_table.shape[0], dtype=jnp.int32)
    one_hot = (token_ids[:, None] == vocab_ids[None, :]).astype(jnp.bfloat16)
    embedded = jnp.dot(one_hot, embed_table, preferred_element_type=jnp.float32).astype(jnp.bfloat16)
    hyena_out = back(pin, qc, embedded, prefix, near, other, before, pole, residues * gain, residues)
    end_state = mine(keep) * mine(total) + mine(take) * mine(other) + after
    return (hyena_out, end_state)


def solution(mesh):
    return jax.shard_map(
        body,
        mesh=mesh,
        in_specs=(
            P(("groups", "seq")),
            P(None, "tp"),
            P(None, ("groups", "seq"), "tp"),
            P(None, None, "tp"),
            P(None, "tp"),
            P(None, "tp"),
            P("groups", "tp"),
        ),
        out_specs=(P(("groups", "seq"), "tp"), P("groups", ("tp", "seq"))),
        check_vma=False,
    )
```

```python
import functools

import jax
import jax.numpy as jnp
from jax import lax
from jax.experimental import pallas as pl
from jax.experimental.pallas import tpu as pltpu
from jax.sharding import PartitionSpec as P

LANES = 256
WIDE = 1024
BLOCK = 1024


def shifted(array, axis, by):
    size = lax.axis_size(axis)
    pairs = [(i, i + by) for i in range(size) if 0 <= i + by < size]
    return lax.ppermute(array, axis, pairs)


def front_kernel(qkv_ref, tails_ref, w_ref, pole_ref, gain_ref, qc_ref, pin_ref, end_ref):
    tok, channels = qc_ref.shape
    modes = pole_ref.shape[0]
    for c0 in range(0, channels, LANES):
        cs = pl.ds(c0, LANES)
        row = lax.broadcasted_iota(jnp.int32, (tok, LANES), 0)
        feats = []
        for member in range(3):
            x = qkv_ref[member, :, cs].astype(jnp.float32)
            tl = tails_ref[member, :, cs].astype(jnp.float32)
            last = tl.shape[0]
            x1 = pltpu.roll(x, 1, 0)
            x1 = jnp.where(row == 0, tl[last - 1 : last, :], x1)
            x2 = pltpu.roll(x, 2, 0)
            x2 = jnp.where(row == 0, tl[last - 2 : last - 1, :], jnp.where(row == 1, tl[last - 1 : last, :], x2))
            w = w_ref[member, :, cs]
            feats.append(w[0:1, :] * x + w[1:2, :] * x1 + w[2:3, :] * x2)
        qc_ref[:, cs] = feats[0]
        pin_ref[:, cs] = feats[1] * feats[2]

    for c0 in range(0, channels, WIDE):
        cs = pl.ds(c0, WIDE)
        pole = pole_ref[:, cs]

        def step(blk, acc):
            base = pl.multiple_of(blk * 8, 8)
            rows = pin_ref[pl.ds(base, 8), cs]
            for i in range(8):
                acc = pole * acc + jnp.broadcast_to(rows[i : i + 1, :], (modes, WIDE))
            return acc

        acc = lax.fori_loop(0, tok // 8, step, jnp.zeros((modes, WIDE), jnp.float32))
        end_ref[:, cs] = gain_ref[:, cs] * acc


def rows_summed(parts, sub):
    half = [
        jnp.where(sub < 4, parts[j] + pltpu.roll(parts[j], 4, 0), parts[j + 4] + pltpu.roll(parts[j + 4], 4, 0))
        for j in range(4)
    ]
    quarter = [
        jnp.where(sub % 4 < 2, half[j] + pltpu.roll(half[j], 6, 0), half[j + 2] + pltpu.roll(half[j + 2], 2, 0))
        for j in range(2)
    ]
    return jnp.where(
        sub % 2 == 0,
        quarter[0] + pltpu.roll(quarter[0], 7, 0),
        quarter[1] + pltpu.roll(quarter[1], 1, 0),
    )


def back_kernel(pin_ref, qc_ref, emb_ref, prefix_ref, near_ref, other_ref, before_ref, pole_ref, drive_ref, res_ref, out_ref):
    tok, channels = pin_ref.shape
    modes = pole_ref.shape[0]
    sub = lax.broadcasted_iota(jnp.int32, (modes, WIDE), 0)
    for c0 in range(0, channels, WIDE):
        cs = pl.ds(c0, WIDE)
        pole = pole_ref[:, cs]
        drive = drive_ref[:, cs]
        incoming = prefix_ref[:, cs] + near_ref[:, cs] * other_ref[:, cs] + before_ref[:, cs]
        start = res_ref[:, cs] * incoming

        def step(blk, state):
            base = pl.multiple_of(blk * 16, 16)
            rows = pin_ref[pl.ds(base, 16), cs]
            sums = []
            for half in range(2):
                parts = []
                for i in range(8):
                    r = half * 8 + i
                    state = pole * state + drive * jnp.broadcast_to(rows[r : r + 1, :], (modes, WIDE))
                    parts.append(state)
                sums.append(rows_summed(parts, sub))
            filtered = jnp.concatenate(sums, axis=0)
            total = emb_ref[pl.ds(base, 16), cs].astype(jnp.float32) + qc_ref[pl.ds(base, 16), cs] * filtered
            out_ref[pl.ds(base, 16), cs] = total.astype(out_ref.dtype)
            return state

        lax.fori_loop(0, tok // 16, step, start)


def vmem_specs(count):
    return [pl.BlockSpec(memory_space=pltpu.VMEM)] * count


def channel_spec(*lead):
    rank = len(lead) + 1
    return pl.BlockSpec(lead + (BLOCK,), lambda j: (0,) * (rank - 1) + (j,))


def front(qkv, tails, conv_weights, pole, gain):
    tok, channels = qkv.shape[1], qkv.shape[2]
    modes = pole.shape[0]
    taps = conv_weights.shape[1]
    return pl.pallas_call(
        front_kernel,
        out_shape=(
            jax.ShapeDtypeStruct((tok, channels), jnp.float32),
            jax.ShapeDtypeStruct((tok, channels), jnp.float32),
            jax.ShapeDtypeStruct((modes, channels), jnp.float32),
        ),
        grid=(channels // BLOCK,),
        in_specs=[
            channel_spec(3, tok),
            channel_spec(3, tails.shape[1]),
            channel_spec(3, taps),
            channel_spec(modes),
            channel_spec(modes),
        ],
        out_specs=(channel_spec(tok), channel_spec(tok), channel_spec(modes)),
        cost_estimate=pl.CostEstimate(
            flops=30 * tok * channels + 2 * tok * modes * channels,
            bytes_accessed=3 * tok * channels * 2 + 2 * tok * channels * 4,
            transcendentals=0,
        ),
    )(qkv, tails, conv_weights, pole, gain)


def back(pin, qc, embedded, prefix, near, other, before, pole, drive, residues):
    tok, channels = pin.shape
    modes = pole.shape[0]
    return pl.pallas_call(
        back_kernel,
        out_shape=jax.ShapeDtypeStruct((tok, channels), jnp.bfloat16),
        grid=(channels // BLOCK,),
        in_specs=[channel_spec(tok)] * 3 + [channel_spec(modes)] * 7,
        out_specs=channel_spec(tok),
        cost_estimate=pl.CostEstimate(
            flops=6 * tok * modes * channels,
            bytes_accessed=tok * channels * (4 + 4 + 2 + 2),
            transcendentals=0,
        ),
    )(pin, qc, embedded, prefix, near, other, before, pole, drive, residues)


def level_factors(decay_rates, me, block, radix, tok_local):
    digit = (me // block) % radix
    within = me % (block * radix)
    nears, takes = [], []
    for j in range(1, radix):
        theirs = digit ^ j
        lower = theirs < digit
        gap = jnp.where(lower, within - (theirs + 1) * block, 0).astype(jnp.float32) * tok_local
        nears.append(jnp.where(lower, jnp.exp(-decay_rates * gap), 0.0))
        takes.append(jnp.exp(-decay_rates * ((radix - 1 - theirs) * block * tok_local).astype(jnp.float32)))
    keep = jnp.exp(-decay_rates * ((radix - 1 - digit) * block * tok_local).astype(jnp.float32))
    return nears, keep, takes


def exchange_levels(count):
    levels = []
    while count > 4:
        levels.append(4)
        count //= 4
    return levels + [2] * (count.bit_length() - 1)


def butterfly(local_end, factors, decay_rates, tok_local, axis, levels, extra):
    count = lax.axis_size(axis)
    me = lax.axis_index(axis)
    total = local_end
    prefix = jnp.zeros_like(local_end)
    block = 1
    for level, radix in enumerate(levels):
        others = [
            lax.ppermute(total, axis, [(i, i ^ (j * block)) for i in range(count)]) for j in range(1, radix)
        ]
        nears, keep, takes = factors
        if level == len(levels) - 1:
            others, extra = lax.optimization_barrier((others, extra))
            return prefix, nears[0], others[0], total, keep, takes[0], extra
        nxt = level_factors(decay_rates, me, block * radix, levels[level + 1], tok_local)
        others, factors = lax.optimization_barrier((others, nxt))
        for near, other in zip(nears, others):
            prefix = prefix + near * other
        fresh = keep * total
        for take, other in zip(takes, others):
            fresh = fresh + take * other
        total = fresh
        block *= radix


def body(token_ids, embed_table, hyena_qkv, conv_weights, decay_rates, residues, prior_state):
    tok_local = hyena_qkv.shape[1]
    channels = hyena_qkv.shape[2]
    tap_count = conv_weights.shape[1]
    seq_count = lax.axis_size("seq")
    seq_index = lax.axis_index("seq")
    tails_local = hyena_qkv[:, tok_local - 16 :, :]
    ring = [(i, (i + 1) % seq_count) for i in range(seq_count)]
    tails_prev = lax.ppermute(tails_local, "seq", ring)
    tails_prev = jnp.where(seq_index == 0, jnp.zeros_like(tails_prev), tails_prev)
    levels = exchange_levels(seq_count)
    tails_prev, factors = lax.optimization_barrier(
        (tails_prev, level_factors(decay_rates, seq_index, 1, levels[0], tok_local))
    )
    pole = jnp.exp(-decay_rates)
    gain = jnp.sqrt(-jnp.expm1(-2.0 * decay_rates))
    qc, pin, local_end = front(hyena_qkv, tails_prev, conv_weights, pole, gain)
    share_cols = channels // seq_count
    mine = lambda a: lax.dynamic_slice_in_dim(a, seq_index * share_cols, share_cols, 1)
    after = jnp.exp(-mine(decay_rates) * float(seq_count * tok_local)) * mine(prior_state)
    before = jnp.exp(-decay_rates * (seq_index.astype(jnp.float32) * tok_local)) * prior_state
    prefix, near, other, total, keep, take, (after, before) = butterfly(
        local_end, factors, decay_rates, tok_local, "seq", levels, (after, before)
    )
    vocab_ids = jnp.arange(embed_table.shape[0], dtype=jnp.int32)
    one_hot = (token_ids[:, None] == vocab_ids[None, :]).astype(jnp.bfloat16)
    embedded = jnp.dot(one_hot, embed_table, preferred_element_type=jnp.float32).astype(jnp.bfloat16)
    hyena_out = back(pin, qc, embedded, prefix, near, other, before, pole, residues * gain, residues)
    end_state = mine(keep) * mine(total) + mine(take) * mine(other) + after
    return (hyena_out, end_state)


def solution(mesh):
    return jax.shard_map(
        body,
        mesh=mesh,
        in_specs=(
            P(("groups", "seq")),
            P(None, "tp"),
            P(None, ("groups", "seq"), "tp"),
            P(None, None, "tp"),
            P(None, "tp"),
            P(None, "tp"),
            P("groups", "tp"),
        ),
        out_specs=(P(("groups", "seq"), "tp"), P("groups", ("tp", "seq"))),
        check_vma=False,
    )
```

```python
import functools

import jax
import jax.numpy as jnp
from jax import lax
from jax.experimental import pallas as pl
from jax.experimental.pallas import tpu as pltpu
from jax.sharding import PartitionSpec as P

LANES = 256
WIDE = 1024
BLOCK = 1024


def shifted(array, axis, by):
    size = lax.axis_size(axis)
    pairs = [(i, i + by) for i in range(size) if 0 <= i + by < size]
    return lax.ppermute(array, axis, pairs)


def front_kernel(qkv_ref, w_ref, pole_ref, gain_ref, qc_ref, pin_ref, end_ref, head_ref):
    tok, channels = qc_ref.shape
    modes = pole_ref.shape[0]
    for c0 in range(0, channels, LANES):
        cs = pl.ds(c0, LANES)
        row = lax.broadcasted_iota(jnp.int32, (tok, LANES), 0)
        feats = []
        for member in range(3):
            x = qkv_ref[member, :, cs].astype(jnp.float32)
            x1 = jnp.where(row < 1, 0.0, pltpu.roll(x, 1, 0))
            x2 = jnp.where(row < 2, 0.0, pltpu.roll(x, 2, 0))
            w = w_ref[member, :, cs]
            feat = w[0:1, :] * x + w[1:2, :] * x1 + w[2:3, :] * x2
            feats.append(feat)
            head_ref[member, :, cs] = feat[0:8, :]
        qc_ref[:, cs] = feats[0]
        pin_ref[:, cs] = feats[1] * feats[2]

    for c0 in range(0, channels, WIDE):
        cs = pl.ds(c0, WIDE)
        pole = pole_ref[:, cs]

        def step(blk, acc):
            base = pl.multiple_of(blk * 8, 8)
            rows = pin_ref[pl.ds(base, 8), cs]
            for i in range(8):
                acc = pole * acc + jnp.broadcast_to(rows[i : i + 1, :], (modes, WIDE))
            return acc

        acc = lax.fori_loop(0, tok // 8, step, jnp.zeros((modes, WIDE), jnp.float32))
        end_ref[:, cs] = gain_ref[:, cs] * acc


def rows_summed(parts, sub):
    half = [
        jnp.where(sub < 4, parts[j] + pltpu.roll(parts[j], 4, 0), parts[j + 4] + pltpu.roll(parts[j + 4], 4, 0))
        for j in range(4)
    ]
    quarter = [
        jnp.where(sub % 4 < 2, half[j] + pltpu.roll(half[j], 6, 0), half[j + 2] + pltpu.roll(half[j + 2], 2, 0))
        for j in range(2)
    ]
    return jnp.where(
        sub % 2 == 0,
        quarter[0] + pltpu.roll(quarter[0], 7, 0),
        quarter[1] + pltpu.roll(quarter[1], 1, 0),
    )


def back_kernel(
    pin_ref, qc_ref, emb_ref, prefix_ref, near_ref, other_ref, before_ref, pole_ref, drive_ref, res_ref, pfix_ref, qfix_ref, out_ref
):
    tok, channels = pin_ref.shape
    modes = pole_ref.shape[0]
    sub = lax.broadcasted_iota(jnp.int32, (modes, WIDE), 0)
    row = lax.broadcasted_iota(jnp.int32, (16, WIDE), 0)
    history = pfix_ref.shape[0]
    for c0 in range(0, channels, WIDE):
        cs = pl.ds(c0, WIDE)
        pole = pole_ref[:, cs]
        drive = drive_ref[:, cs]
        pfix = pfix_ref[:, cs]
        qfix = qfix_ref[:, cs]
        qrows = jnp.zeros((16, WIDE), jnp.float32)
        for r in range(history):
            qrows = jnp.where(row == r, jnp.broadcast_to(qfix[r : r + 1, :], (16, WIDE)), qrows)
        incoming = prefix_ref[:, cs] + near_ref[:, cs] * other_ref[:, cs] + before_ref[:, cs]
        start = res_ref[:, cs] * incoming

        def step(blk, state):
            base = pl.multiple_of(blk * 16, 16)
            gate = (blk == 0).astype(jnp.float32)
            rows = pin_ref[pl.ds(base, 16), cs]
            sums = []
            for half in range(2):
                parts = []
                for i in range(8):
                    r = half * 8 + i
                    x = rows[r : r + 1, :]
                    if r < history:
                        x = x + gate * pfix[r : r + 1, :]
                    state = pole * state + drive * jnp.broadcast_to(x, (modes, WIDE))
                    parts.append(state)
                sums.append(rows_summed(parts, sub))
            filtered = jnp.concatenate(sums, axis=0)
            qc = qc_ref[pl.ds(base, 16), cs] + gate * qrows
            total = emb_ref[pl.ds(base, 16), cs].astype(jnp.float32) + qc * filtered
            out_ref[pl.ds(base, 16), cs] = total.astype(out_ref.dtype)
            return state

        lax.fori_loop(0, tok // 16, step, start)


def vmem_specs(count):
    return [pl.BlockSpec(memory_space=pltpu.VMEM)] * count


def channel_spec(*lead):
    rank = len(lead) + 1
    return pl.BlockSpec(lead + (BLOCK,), lambda j: (0,) * (rank - 1) + (j,))


def front(qkv, conv_weights, pole, gain):
    tok, channels = qkv.shape[1], qkv.shape[2]
    modes = pole.shape[0]
    taps = conv_weights.shape[1]
    return pl.pallas_call(
        front_kernel,
        out_shape=(
            jax.ShapeDtypeStruct((tok, channels), jnp.float32),
            jax.ShapeDtypeStruct((tok, channels), jnp.float32),
            jax.ShapeDtypeStruct((modes, channels), jnp.float32),
            jax.ShapeDtypeStruct((3, 8, channels), jnp.float32),
        ),
        grid=(channels // BLOCK,),
        in_specs=[
            channel_spec(3, tok),
            channel_spec(3, taps),
            channel_spec(modes),
            channel_spec(modes),
        ],
        out_specs=(channel_spec(tok), channel_spec(tok), channel_spec(modes), channel_spec(3, 8)),
        cost_estimate=pl.CostEstimate(
            flops=30 * tok * channels + 2 * tok * modes * channels,
            bytes_accessed=3 * tok * channels * 2 + 2 * tok * channels * 4,
            transcendentals=0,
        ),
    )(qkv, conv_weights, pole, gain)


def back(pin, qc, embedded, prefix, near, other, before, pole, drive, residues, pfix, qfix):
    tok, channels = pin.shape
    modes = pole.shape[0]
    return pl.pallas_call(
        back_kernel,
        out_shape=jax.ShapeDtypeStruct((tok, channels), jnp.bfloat16),
        grid=(channels // BLOCK,),
        in_specs=[channel_spec(tok)] * 3 + [channel_spec(modes)] * 7 + [channel_spec(pfix.shape[0])] * 2,
        out_specs=channel_spec(tok),
        cost_estimate=pl.CostEstimate(
            flops=6 * tok * modes * channels,
            bytes_accessed=tok * channels * (4 + 4 + 2 + 2),
            transcendentals=0,
        ),
    )(pin, qc, embedded, prefix, near, other, before, pole, drive, residues, pfix, qfix)


def level_factors(decay_rates, me, block, radix, tok_local):
    digit = (me // block) % radix
    within = me % (block * radix)
    nears, takes = [], []
    for j in range(1, radix):
        theirs = digit ^ j
        lower = theirs < digit
        gap = jnp.where(lower, within - (theirs + 1) * block, 0).astype(jnp.float32) * tok_local
        nears.append(jnp.where(lower, jnp.exp(-decay_rates * gap), 0.0))
        takes.append(jnp.exp(-decay_rates * ((radix - 1 - theirs) * block * tok_local).astype(jnp.float32)))
    keep = jnp.exp(-decay_rates * ((radix - 1 - digit) * block * tok_local).astype(jnp.float32))
    return nears, keep, takes


def exchange_levels(count):
    levels = []
    while count > 4:
        levels.append(4)
        count //= 4
    return levels + [2] * (count.bit_length() - 1)


def butterfly(local_end, factors, decay_rates, tok_local, axis, levels, extra):
    count = lax.axis_size(axis)
    me = lax.axis_index(axis)
    total = local_end
    prefix = jnp.zeros_like(local_end)
    block = 1
    for level, radix in enumerate(levels):
        others = [
            lax.ppermute(total, axis, [(i, i ^ (j * block)) for i in range(count)]) for j in range(1, radix)
        ]
        nears, keep, takes = factors
        if level == len(levels) - 1:
            others, extra = lax.optimization_barrier((others, extra))
            return prefix, nears[0], others[0], total, keep, takes[0], extra
        nxt = level_factors(decay_rates, me, block * radix, levels[level + 1], tok_local)
        others, factors = lax.optimization_barrier((others, nxt))
        for near, other in zip(nears, others):
            prefix = prefix + near * other
        fresh = keep * total
        for take, other in zip(takes, others):
            fresh = fresh + take * other
        total = fresh
        block *= radix


def body(token_ids, embed_table, hyena_qkv, conv_weights, decay_rates, residues, prior_state):
    tok_local = hyena_qkv.shape[1]
    channels = hyena_qkv.shape[2]
    tap_count = conv_weights.shape[1]
    seq_count = lax.axis_size("seq")
    seq_index = lax.axis_index("seq")
    history = tap_count - 1
    tails_local = hyena_qkv[:, tok_local - history :, :]
    ring = [(i, (i + 1) % seq_count) for i in range(seq_count)]
    tails_prev = lax.ppermute(tails_local, "seq", ring)
    levels = exchange_levels(seq_count)
    tails_prev, factors = lax.optimization_barrier(
        (tails_prev, level_factors(decay_rates, seq_index, 1, levels[0], tok_local))
    )
    pole = jnp.exp(-decay_rates)
    gain = jnp.sqrt(-jnp.expm1(-2.0 * decay_rates))
    qc, pin, local_zero, head = front(hyena_qkv, conv_weights, pole, gain)
    tails_f = jnp.where(seq_index == 0, 0.0, tails_prev.astype(jnp.float32))
    extra = []
    for t in range(history):
        term = jnp.zeros((3, channels), jnp.float32)
        for tap in range(t + 1, tap_count):
            term = term + conv_weights[:, tap, :] * tails_f[:, history + t - tap, :]
        extra.append(term)
    extra = jnp.stack(extra, axis=1)
    true_head = head[:, :history, :] + extra
    pfix = true_head[1] * true_head[2] - head[1, :history, :] * head[2, :history, :]
    qfix = extra[0]
    shift = sum(jnp.exp(-decay_rates * float(tok_local - 1 - t)) * pfix[t][None, :] for t in range(history))
    local_end = local_zero + gain * shift
    share_cols = channels // seq_count
    mine = lambda a: lax.dynamic_slice_in_dim(a, seq_index * share_cols, share_cols, 1)
    after = jnp.exp(-mine(decay_rates) * float(seq_count * tok_local)) * mine(prior_state)
    before = jnp.exp(-decay_rates * (seq_index.astype(jnp.float32) * tok_local)) * prior_state
    prefix, near, other, total, keep, take, (after, before) = butterfly(
        local_end, factors, decay_rates, tok_local, "seq", levels, (after, before)
    )
    vocab_ids = jnp.arange(embed_table.shape[0], dtype=jnp.int32)
    one_hot = (token_ids[:, None] == vocab_ids[None, :]).astype(jnp.bfloat16)
    embedded = jnp.dot(one_hot, embed_table, preferred_element_type=jnp.float32).astype(jnp.bfloat16)
    hyena_out = back(pin, qc, embedded, prefix, near, other, before, pole, residues * gain, residues, pfix, qfix)
    end_state = mine(keep) * mine(total) + mine(take) * mine(other) + after
    return (hyena_out, end_state)


def solution(mesh):
    return jax.shard_map(
        body,
        mesh=mesh,
        in_specs=(
            P(("groups", "seq")),
            P(None, "tp"),
            P(None, ("groups", "seq"), "tp"),
            P(None, None, "tp"),
            P(None, "tp"),
            P(None, "tp"),
            P("groups", "tp"),
        ),
        out_specs=(P(("groups", "seq"), "tp"), P("groups", ("tp", "seq"))),
        check_vma=False,
    )
```

```python
import functools

import jax
import jax.numpy as jnp
from jax import lax
from jax.experimental import pallas as pl
from jax.experimental.pallas import tpu as pltpu
from jax.sharding import PartitionSpec as P

LANES = 256
WIDE = 1024
BLOCK = 1024


def shifted(array, axis, by):
    size = lax.axis_size(axis)
    pairs = [(i, i + by) for i in range(size) if 0 <= i + by < size]
    return lax.ppermute(array, axis, pairs)


def front_kernel(qkv_ref, tails_ref, w_ref, pole_ref, gain_ref, qc_ref, pin_ref, end_ref):
    tok, channels = qc_ref.shape
    modes = pole_ref.shape[0]
    for c0 in range(0, channels, LANES):
        cs = pl.ds(c0, LANES)
        row = lax.broadcasted_iota(jnp.int32, (tok, LANES), 0)
        feats = []
        for member in range(3):
            x = qkv_ref[member, :, cs].astype(jnp.float32)
            tl = tails_ref[pl.ds(member * 2, 2), cs].astype(jnp.float32)
            x1 = pltpu.roll(x, 1, 0)
            x1 = jnp.where(row == 0, tl[1:2, :], x1)
            x2 = pltpu.roll(x, 2, 0)
            x2 = jnp.where(row == 0, tl[0:1, :], jnp.where(row == 1, tl[1:2, :], x2))
            w = w_ref[member, :, cs]
            feats.append(w[0:1, :] * x + w[1:2, :] * x1 + w[2:3, :] * x2)
        qc_ref[:, cs] = feats[0]
        pin_ref[:, cs] = feats[1] * feats[2]

    for c0 in range(0, channels, WIDE):
        cs = pl.ds(c0, WIDE)
        pole = pole_ref[:, cs]

        def step(blk, acc):
            base = pl.multiple_of(blk * 8, 8)
            rows = pin_ref[pl.ds(base, 8), cs]
            for i in range(8):
                acc = pole * acc + jnp.broadcast_to(rows[i : i + 1, :], (modes, WIDE))
            return acc

        acc = lax.fori_loop(0, tok // 8, step, jnp.zeros((modes, WIDE), jnp.float32))
        end_ref[:, cs] = gain_ref[:, cs] * acc


def rows_summed(parts, sub):
    half = [
        jnp.where(sub < 4, parts[j] + pltpu.roll(parts[j], 4, 0), parts[j + 4] + pltpu.roll(parts[j + 4], 4, 0))
        for j in range(4)
    ]
    quarter = [
        jnp.where(sub % 4 < 2, half[j] + pltpu.roll(half[j], 6, 0), half[j + 2] + pltpu.roll(half[j + 2], 2, 0))
        for j in range(2)
    ]
    return jnp.where(
        sub % 2 == 0,
        quarter[0] + pltpu.roll(quarter[0], 7, 0),
        quarter[1] + pltpu.roll(quarter[1], 1, 0),
    )


def back_kernel(pin_ref, qc_ref, emb_ref, prefix_ref, near_ref, other_ref, before_ref, pole_ref, drive_ref, res_ref, out_ref):
    tok, channels = pin_ref.shape
    modes = pole_ref.shape[0]
    sub = lax.broadcasted_iota(jnp.int32, (modes, WIDE), 0)
    for c0 in range(0, channels, WIDE):
        cs = pl.ds(c0, WIDE)
        pole = pole_ref[:, cs]
        drive = drive_ref[:, cs]
        incoming = prefix_ref[:, cs] + near_ref[:, cs] * other_ref[:, cs] + before_ref[:, cs]
        start = res_ref[:, cs] * incoming

        def step(blk, state):
            base = pl.multiple_of(blk * 16, 16)
            rows = pin_ref[pl.ds(base, 16), cs]
            sums = []
            for half in range(2):
                parts = []
                for i in range(8):
                    r = half * 8 + i
                    state = pole * state + drive * jnp.broadcast_to(rows[r : r + 1, :], (modes, WIDE))
                    parts.append(state)
                sums.append(rows_summed(parts, sub))
            filtered = jnp.concatenate(sums, axis=0)
            total = emb_ref[pl.ds(base, 16), cs].astype(jnp.float32) + qc_ref[pl.ds(base, 16), cs] * filtered
            out_ref[pl.ds(base, 16), cs] = total.astype(out_ref.dtype)
            return state

        lax.fori_loop(0, tok // 16, step, start)


def vmem_specs(count):
    return [pl.BlockSpec(memory_space=pltpu.VMEM)] * count


def channel_spec(*lead):
    rank = len(lead) + 1
    return pl.BlockSpec(lead + (BLOCK,), lambda j: (0,) * (rank - 1) + (j,))


def front(qkv, tails, conv_weights, pole, gain):
    tok, channels = qkv.shape[1], qkv.shape[2]
    modes = pole.shape[0]
    taps = conv_weights.shape[1]
    return pl.pallas_call(
        front_kernel,
        out_shape=(
            jax.ShapeDtypeStruct((tok, channels), jnp.float32),
            jax.ShapeDtypeStruct((tok, channels), jnp.float32),
            jax.ShapeDtypeStruct((modes, channels), jnp.float32),
        ),
        grid=(channels // BLOCK,),
        in_specs=[
            channel_spec(3, tok),
            channel_spec(tails.shape[0]),
            channel_spec(3, taps),
            channel_spec(modes),
            channel_spec(modes),
        ],
        out_specs=(channel_spec(tok), channel_spec(tok), channel_spec(modes)),
        cost_estimate=pl.CostEstimate(
            flops=30 * tok * channels + 2 * tok * modes * channels,
            bytes_accessed=3 * tok * channels * 2 + 2 * tok * channels * 4,
            transcendentals=0,
        ),
    )(qkv, tails, conv_weights, pole, gain)


def back(pin, qc, embedded, prefix, near, other, before, pole, drive, residues):
    tok, channels = pin.shape
    modes = pole.shape[0]
    return pl.pallas_call(
        back_kernel,
        out_shape=jax.ShapeDtypeStruct((tok, channels), jnp.bfloat16),
        grid=(channels // BLOCK,),
        in_specs=[channel_spec(tok)] * 3 + [channel_spec(modes)] * 7,
        out_specs=channel_spec(tok),
        cost_estimate=pl.CostEstimate(
            flops=6 * tok * modes * channels,
            bytes_accessed=tok * channels * (4 + 4 + 2 + 2),
            transcendentals=0,
        ),
    )(pin, qc, embedded, prefix, near, other, before, pole, drive, residues)


def level_factors(decay_rates, me, block, radix, tok_local):
    digit = (me // block) % radix
    within = me % (block * radix)
    nears, takes = [], []
    for j in range(1, radix):
        theirs = digit ^ j
        lower = theirs < digit
        gap = jnp.where(lower, within - (theirs + 1) * block, 0).astype(jnp.float32) * tok_local
        nears.append(jnp.where(lower, jnp.exp(-decay_rates * gap), 0.0))
        takes.append(jnp.exp(-decay_rates * ((radix - 1 - theirs) * block * tok_local).astype(jnp.float32)))
    keep = jnp.exp(-decay_rates * ((radix - 1 - digit) * block * tok_local).astype(jnp.float32))
    return nears, keep, takes


def exchange_levels(count):
    levels = []
    while count > 4:
        levels.append(4)
        count //= 4
    return levels + [2] * (count.bit_length() - 1)


def butterfly(local_end, factors, decay_rates, tok_local, axis, levels, extra):
    count = lax.axis_size(axis)
    me = lax.axis_index(axis)
    total = local_end
    prefix = jnp.zeros_like(local_end)
    block = 1
    for level, radix in enumerate(levels):
        others = [
            lax.ppermute(total, axis, [(i, i ^ (j * block)) for i in range(count)]) for j in range(1, radix)
        ]
        nears, keep, takes = factors
        if level == len(levels) - 1:
            others, extra = lax.optimization_barrier((others, extra))
            return prefix, nears[0], others[0], total, keep, takes[0], extra
        nxt = level_factors(decay_rates, me, block * radix, levels[level + 1], tok_local)
        others, factors = lax.optimization_barrier((others, nxt))
        for near, other in zip(nears, others):
            prefix = prefix + near * other
        fresh = keep * total
        for take, other in zip(takes, others):
            fresh = fresh + take * other
        total = fresh
        block *= radix


def body(token_ids, embed_table, hyena_qkv, conv_weights, decay_rates, residues, prior_state):
    tok_local = hyena_qkv.shape[1]
    channels = hyena_qkv.shape[2]
    tap_count = conv_weights.shape[1]
    seq_count = lax.axis_size("seq")
    seq_index = lax.axis_index("seq")
    history = tap_count - 1
    tails_local = hyena_qkv[:, tok_local - history :, :].reshape(3 * history, channels)
    ring = [(i, (i + 1) % seq_count) for i in range(seq_count)]
    tails_prev = lax.ppermute(tails_local, "seq", ring)
    tails_prev = jnp.where(seq_index == 0, jnp.zeros_like(tails_prev), tails_prev)
    levels = exchange_levels(seq_count)
    tails_prev, factors = lax.optimization_barrier(
        (tails_prev, level_factors(decay_rates, seq_index, 1, levels[0], tok_local))
    )
    pole = jnp.exp(-decay_rates)
    gain = jnp.sqrt(-jnp.expm1(-2.0 * decay_rates))
    qc, pin, local_end = front(hyena_qkv, tails_prev, conv_weights, pole, gain)
    share_cols = channels // seq_count
    mine = lambda a: lax.dynamic_slice_in_dim(a, seq_index * share_cols, share_cols, 1)
    after = jnp.exp(-mine(decay_rates) * float(seq_count * tok_local)) * mine(prior_state)
    before = jnp.exp(-decay_rates * (seq_index.astype(jnp.float32) * tok_local)) * prior_state
    prefix, near, other, total, keep, take, (after, before) = butterfly(
        local_end, factors, decay_rates, tok_local, "seq", levels, (after, before)
    )
    vocab_ids = jnp.arange(embed_table.shape[0], dtype=jnp.int32)
    one_hot = (token_ids[:, None] == vocab_ids[None, :]).astype(jnp.bfloat16)
    embedded = jnp.dot(one_hot, embed_table, preferred_element_type=jnp.float32).astype(jnp.bfloat16)
    hyena_out = back(pin, qc, embedded, prefix, near, other, before, pole, residues * gain, residues)
    end_state = mine(keep) * mine(total) + mine(take) * mine(other) + after
    return (hyena_out, end_state)


def solution(mesh):
    return jax.shard_map(
        body,
        mesh=mesh,
        in_specs=(
            P(("groups", "seq")),
            P(None, "tp"),
            P(None, ("groups", "seq"), "tp"),
            P(None, None, "tp"),
            P(None, "tp"),
            P(None, "tp"),
            P("groups", "tp"),
        ),
        out_specs=(P(("groups", "seq"), "tp"), P("groups", ("tp", "seq"))),
        check_vma=False,
    )
```

```python
import functools

import jax
import jax.numpy as jnp
from jax import lax
from jax.experimental import pallas as pl
from jax.experimental.pallas import tpu as pltpu
from jax.sharding import PartitionSpec as P

LANES = 256
WIDE = 1024
BLOCK = 1024


def shifted(array, axis, by):
    size = lax.axis_size(axis)
    pairs = [(i, i + by) for i in range(size) if 0 <= i + by < size]
    return lax.ppermute(array, axis, pairs)


def front_kernel(qkv_ref, tails_ref, w_ref, pole_ref, gain_ref, qc_ref, pin_ref, end_ref):
    tok, channels = qc_ref.shape
    modes = pole_ref.shape[0]
    for c0 in range(0, channels, LANES):
        cs = pl.ds(c0, LANES)
        row = lax.broadcasted_iota(jnp.int32, (tok, LANES), 0)
        feats = []
        for member in range(3):
            x = qkv_ref[member, :, cs].astype(jnp.float32)
            tl = tails_ref[member, :, cs].astype(jnp.float32)
            x1 = pltpu.roll(x, 1, 0)
            x1 = jnp.where(row == 0, tl[1:2, :], x1)
            x2 = pltpu.roll(x, 2, 0)
            x2 = jnp.where(row == 0, tl[0:1, :], jnp.where(row == 1, tl[1:2, :], x2))
            w = w_ref[member, :, cs]
            feats.append(w[0:1, :] * x + w[1:2, :] * x1 + w[2:3, :] * x2)
        qc_ref[:, cs] = feats[0]
        pin_ref[:, cs] = feats[1] * feats[2]

    for c0 in range(0, channels, WIDE):
        cs = pl.ds(c0, WIDE)
        pole = pole_ref[:, cs]

        def step(blk, acc):
            base = pl.multiple_of(blk * 8, 8)
            rows = pin_ref[pl.ds(base, 8), cs]
            for i in range(8):
                acc = pole * acc + jnp.broadcast_to(rows[i : i + 1, :], (modes, WIDE))
            return acc

        acc = lax.fori_loop(0, tok // 8, step, jnp.zeros((modes, WIDE), jnp.float32))
        end_ref[:, cs] = gain_ref[:, cs] * acc


def rows_summed(parts, sub):
    half = [
        jnp.where(sub < 4, parts[j] + pltpu.roll(parts[j], 4, 0), parts[j + 4] + pltpu.roll(parts[j + 4], 4, 0))
        for j in range(4)
    ]
    quarter = [
        jnp.where(sub % 4 < 2, half[j] + pltpu.roll(half[j], 6, 0), half[j + 2] + pltpu.roll(half[j + 2], 2, 0))
        for j in range(2)
    ]
    return jnp.where(
        sub % 2 == 0,
        quarter[0] + pltpu.roll(quarter[0], 7, 0),
        quarter[1] + pltpu.roll(quarter[1], 1, 0),
    )


def back_kernel(
    seq_ref, pin_ref, qc_ref, emb_ref, prefix_ref, near_ref, other_ref, before_ref, pole_ref, drive_ref, res_ref,
    keep_ref, take_ref, total_ref, after_ref, out_ref, end_ref
):
    tok, channels = pin_ref.shape
    share = end_ref.shape[1]
    first_col = seq_ref[0] * share
    here = pl.program_id(0)

    @pl.when(first_col // channels == here)
    def _():
        cols = pl.ds(pl.multiple_of(first_col - here * channels, share), share)
        end_ref[...] = keep_ref[:, cols] * total_ref[:, cols] + take_ref[:, cols] * other_ref[:, cols] + after_ref[...]

    modes = pole_ref.shape[0]
    sub = lax.broadcasted_iota(jnp.int32, (modes, WIDE), 0)
    for c0 in range(0, channels, WIDE):
        cs = pl.ds(c0, WIDE)
        pole = pole_ref[:, cs]
        drive = drive_ref[:, cs]
        incoming = prefix_ref[:, cs] + near_ref[:, cs] * other_ref[:, cs] + before_ref[:, cs]
        start = res_ref[:, cs] * incoming

        def step(blk, state):
            base = pl.multiple_of(blk * 16, 16)
            rows = pin_ref[pl.ds(base, 16), cs]
            sums = []
            for half in range(2):
                parts = []
                for i in range(8):
                    r = half * 8 + i
                    state = pole * state + drive * jnp.broadcast_to(rows[r : r + 1, :], (modes, WIDE))
                    parts.append(state)
                sums.append(rows_summed(parts, sub))
            filtered = jnp.concatenate(sums, axis=0)
            total = emb_ref[pl.ds(base, 16), cs].astype(jnp.float32) + qc_ref[pl.ds(base, 16), cs] * filtered
            out_ref[pl.ds(base, 16), cs] = total.astype(out_ref.dtype)
            return state

        lax.fori_loop(0, tok // 16, step, start)


def vmem_specs(count):
    return [pl.BlockSpec(memory_space=pltpu.VMEM)] * count


def channel_spec(*lead):
    rank = len(lead) + 1
    return pl.BlockSpec(lead + (BLOCK,), lambda j, *_: (0,) * (rank - 1) + (j,))


def front(qkv, tails, conv_weights, pole, gain):
    tok, channels = qkv.shape[1], qkv.shape[2]
    modes = pole.shape[0]
    taps = conv_weights.shape[1]
    return pl.pallas_call(
        front_kernel,
        out_shape=(
            jax.ShapeDtypeStruct((tok, channels), jnp.float32),
            jax.ShapeDtypeStruct((tok, channels), jnp.float32),
            jax.ShapeDtypeStruct((modes, channels), jnp.float32),
        ),
        grid=(channels // BLOCK,),
        in_specs=[
            channel_spec(3, tok),
            channel_spec(3, tails.shape[1]),
            channel_spec(3, taps),
            channel_spec(modes),
            channel_spec(modes),
        ],
        out_specs=(channel_spec(tok), channel_spec(tok), channel_spec(modes)),
        cost_estimate=pl.CostEstimate(
            flops=30 * tok * channels + 2 * tok * modes * channels,
            bytes_accessed=3 * tok * channels * 2 + 2 * tok * channels * 4,
            transcendentals=0,
        ),
    )(qkv, tails, conv_weights, pole, gain)


def back(seq_index, pin, qc, embedded, prefix, near, other, before, pole, drive, residues, keep, take, total, after):
    tok, channels = pin.shape
    modes = pole.shape[0]
    share = after.shape[1]
    return pl.pallas_call(
        back_kernel,
        out_shape=(
            jax.ShapeDtypeStruct((tok, channels), jnp.bfloat16),
            jax.ShapeDtypeStruct((modes, share), jnp.float32),
        ),
        grid_spec=pltpu.PrefetchScalarGridSpec(
            num_scalar_prefetch=1,
            grid=(channels // BLOCK,),
            in_specs=[channel_spec(tok)] * 3
            + [channel_spec(modes)] * 10
            + [pl.BlockSpec((modes, share), lambda j, *_: (0, 0))],
            out_specs=(channel_spec(tok), pl.BlockSpec((modes, share), lambda j, *_: (0, 0))),
        ),
        cost_estimate=pl.CostEstimate(
            flops=6 * tok * modes * channels,
            bytes_accessed=tok * channels * (4 + 4 + 2 + 2),
            transcendentals=0,
        ),
    )(seq_index, pin, qc, embedded, prefix, near, other, before, pole, drive, residues, keep, take, total, after)


def level_factors(decay_rates, me, block, radix, tok_local):
    digit = (me // block) % radix
    within = me % (block * radix)
    nears, takes = [], []
    for j in range(1, radix):
        theirs = digit ^ j
        lower = theirs < digit
        gap = jnp.where(lower, within - (theirs + 1) * block, 0).astype(jnp.float32) * tok_local
        nears.append(jnp.where(lower, jnp.exp(-decay_rates * gap), 0.0))
        takes.append(jnp.exp(-decay_rates * ((radix - 1 - theirs) * block * tok_local).astype(jnp.float32)))
    keep = jnp.exp(-decay_rates * ((radix - 1 - digit) * block * tok_local).astype(jnp.float32))
    return nears, keep, takes


def exchange_levels(count):
    levels = []
    while count > 4:
        levels.append(4)
        count //= 4
    return levels + [2] * (count.bit_length() - 1)


def butterfly(local_end, factors, decay_rates, tok_local, axis, levels, extra):
    count = lax.axis_size(axis)
    me = lax.axis_index(axis)
    total = local_end
    prefix = jnp.zeros_like(local_end)
    block = 1
    for level, radix in enumerate(levels):
        others = [
            lax.ppermute(total, axis, [(i, i ^ (j * block)) for i in range(count)]) for j in range(1, radix)
        ]
        nears, keep, takes = factors
        if level == len(levels) - 1:
            others, extra = lax.optimization_barrier((others, extra))
            return prefix, nears[0], others[0], total, keep, takes[0], extra
        nxt = level_factors(decay_rates, me, block * radix, levels[level + 1], tok_local)
        others, factors = lax.optimization_barrier((others, nxt))
        for near, other in zip(nears, others):
            prefix = prefix + near * other
        fresh = keep * total
        for take, other in zip(takes, others):
            fresh = fresh + take * other
        total = fresh
        block *= radix


def body(token_ids, embed_table, hyena_qkv, conv_weights, decay_rates, residues, prior_state):
    tok_local = hyena_qkv.shape[1]
    channels = hyena_qkv.shape[2]
    tap_count = conv_weights.shape[1]
    seq_count = lax.axis_size("seq")
    seq_index = lax.axis_index("seq")
    tails_local = hyena_qkv[:, tok_local - (tap_count - 1) :, :]
    ring = [(i, (i + 1) % seq_count) for i in range(seq_count)]
    tails_prev = lax.ppermute(tails_local, "seq", ring)
    tails_prev = jnp.where(seq_index == 0, jnp.zeros_like(tails_prev), tails_prev)
    levels = exchange_levels(seq_count)
    tails_prev, factors = lax.optimization_barrier(
        (tails_prev, level_factors(decay_rates, seq_index, 1, levels[0], tok_local))
    )
    pole = jnp.exp(-decay_rates)
    gain = jnp.sqrt(-jnp.expm1(-2.0 * decay_rates))
    qc, pin, local_end = front(hyena_qkv, tails_prev, conv_weights, pole, gain)
    share_cols = channels // seq_count
    mine = lambda a: lax.dynamic_slice_in_dim(a, seq_index * share_cols, share_cols, 1)
    after = jnp.exp(-mine(decay_rates) * float(seq_count * tok_local)) * mine(prior_state)
    before = jnp.exp(-decay_rates * (seq_index.astype(jnp.float32) * tok_local)) * prior_state
    prefix, near, other, total, keep, take, (after, before) = butterfly(
        local_end, factors, decay_rates, tok_local, "seq", levels, (after, before)
    )
    vocab_ids = jnp.arange(embed_table.shape[0], dtype=jnp.int32)
    one_hot = (token_ids[:, None] == vocab_ids[None, :]).astype(jnp.bfloat16)
    embedded = jnp.dot(one_hot, embed_table, preferred_element_type=jnp.float32).astype(jnp.bfloat16)
    if share_cols % 128 == 0:
        seq_scalar = jnp.reshape(seq_index, (1,)).astype(jnp.int32)
        hyena_out, end_state = back(
            seq_scalar, pin, qc, embedded, prefix, near, other, before, pole, residues * gain, residues,
            keep, take, total, after,
        )
    else:
        hyena_out, _ = back(
            jnp.zeros((1,), jnp.int32), pin, qc, embedded, prefix, near, other, before, pole, residues * gain,
            residues, keep, take, total, jnp.zeros((keep.shape[0], 128), jnp.float32),
        )
        end_state = mine(keep) * mine(total) + mine(take) * mine(other) + after
    return (hyena_out, end_state)


def solution(mesh):
    return jax.shard_map(
        body,
        mesh=mesh,
        in_specs=(
            P(("groups", "seq")),
            P(None, "tp"),
            P(None, ("groups", "seq"), "tp"),
            P(None, None, "tp"),
            P(None, "tp"),
            P(None, "tp"),
            P("groups", "tp"),
        ),
        out_specs=(P(("groups", "seq"), "tp"), P("groups", ("tp", "seq"))),
        check_vma=False,
    )
```

```python
import functools

import jax
import jax.numpy as jnp
from jax import lax
from jax.experimental import pallas as pl
from jax.experimental.pallas import tpu as pltpu
from jax.sharding import PartitionSpec as P

LANES = 256
WIDE = 1024
BLOCK = 1024


def shifted(array, axis, by):
    size = lax.axis_size(axis)
    pairs = [(i, i + by) for i in range(size) if 0 <= i + by < size]
    return lax.ppermute(array, axis, pairs)


def front_kernel(qkv_ref, tails_ref, w_ref, pole_ref, gain_ref, qc_ref, pin_ref, end_ref):
    tok, channels = qc_ref.shape
    modes = pole_ref.shape[0]
    for c0 in range(0, channels, LANES):
        cs = pl.ds(c0, LANES)
        row = lax.broadcasted_iota(jnp.int32, (tok, LANES), 0)
        feats = []
        for member in range(3):
            x = qkv_ref[member, :, cs].astype(jnp.float32)
            tl = tails_ref[pl.ds(member * 2, 2), cs].astype(jnp.float32)
            x1 = pltpu.roll(x, 1, 0)
            x1 = jnp.where(row == 0, tl[1:2, :], x1)
            x2 = pltpu.roll(x, 2, 0)
            x2 = jnp.where(row == 0, tl[0:1, :], jnp.where(row == 1, tl[1:2, :], x2))
            w = w_ref[member, :, cs]
            feats.append(w[0:1, :] * x + w[1:2, :] * x1 + w[2:3, :] * x2)
        qc_ref[:, cs] = feats[0]
        pin_ref[:, cs] = feats[1] * feats[2]

    for c0 in range(0, channels, WIDE):
        cs = pl.ds(c0, WIDE)
        pole = pole_ref[:, cs]

        def step(blk, acc):
            base = pl.multiple_of(blk * 8, 8)
            rows = pin_ref[pl.ds(base, 8), cs]
            for i in range(8):
                acc = pole * acc + jnp.broadcast_to(rows[i : i + 1, :], (modes, WIDE))
            return acc

        acc = lax.fori_loop(0, tok // 8, step, jnp.zeros((modes, WIDE), jnp.float32))
        end_ref[:, cs] = gain_ref[:, cs] * acc


def rows_summed(parts, sub):
    half = [
        jnp.where(sub < 4, parts[j] + pltpu.roll(parts[j], 4, 0), parts[j + 4] + pltpu.roll(parts[j + 4], 4, 0))
        for j in range(4)
    ]
    quarter = [
        jnp.where(sub % 4 < 2, half[j] + pltpu.roll(half[j], 6, 0), half[j + 2] + pltpu.roll(half[j + 2], 2, 0))
        for j in range(2)
    ]
    return jnp.where(
        sub % 2 == 0,
        quarter[0] + pltpu.roll(quarter[0], 7, 0),
        quarter[1] + pltpu.roll(quarter[1], 1, 0),
    )


def back_kernel(pin_ref, qc_ref, emb_ref, prefix_ref, near_ref, other_ref, before_ref, pole_ref, drive_ref, res_ref, out_ref):
    tok, channels = pin_ref.shape
    modes = pole_ref.shape[0]
    sub = lax.broadcasted_iota(jnp.int32, (modes, WIDE), 0)
    for c0 in range(0, channels, WIDE):
        cs = pl.ds(c0, WIDE)
        pole = pole_ref[:, cs]
        drive = drive_ref[:, cs]
        incoming = prefix_ref[:, cs] + near_ref[:, cs] * other_ref[:, cs] + before_ref[:, cs]
        start = res_ref[:, cs] * incoming

        def step(blk, state):
            base = pl.multiple_of(blk * 16, 16)
            rows = pin_ref[pl.ds(base, 16), cs]
            sums = []
            for half in range(2):
                parts = []
                for i in range(8):
                    r = half * 8 + i
                    state = pole * state + drive * jnp.broadcast_to(rows[r : r + 1, :], (modes, WIDE))
                    parts.append(state)
                sums.append(rows_summed(parts, sub))
            filtered = jnp.concatenate(sums, axis=0)
            total = emb_ref[pl.ds(base, 16), cs].astype(jnp.float32) + qc_ref[pl.ds(base, 16), cs] * filtered
            out_ref[pl.ds(base, 16), cs] = total.astype(out_ref.dtype)
            return state

        lax.fori_loop(0, tok // 16, step, start)


def vmem_specs(count):
    return [pl.BlockSpec(memory_space=pltpu.VMEM)] * count


def channel_spec(*lead):
    rank = len(lead) + 1
    return pl.BlockSpec(lead + (BLOCK,), lambda j: (0,) * (rank - 1) + (j,))


def front(qkv, tails, conv_weights, pole, gain):
    tok, channels = qkv.shape[1], qkv.shape[2]
    modes = pole.shape[0]
    taps = conv_weights.shape[1]
    return pl.pallas_call(
        front_kernel,
        out_shape=(
            jax.ShapeDtypeStruct((tok, channels), jnp.float32),
            jax.ShapeDtypeStruct((tok, channels), jnp.float32),
            jax.ShapeDtypeStruct((modes, channels), jnp.float32),
        ),
        grid=(channels // BLOCK,),
        in_specs=[
            channel_spec(3, tok),
            channel_spec(tails.shape[0]),
            channel_spec(3, taps),
            channel_spec(modes),
            channel_spec(modes),
        ],
        out_specs=(channel_spec(tok), channel_spec(tok), channel_spec(modes)),
        cost_estimate=pl.CostEstimate(
            flops=30 * tok * channels + 2 * tok * modes * channels,
            bytes_accessed=3 * tok * channels * 2 + 2 * tok * channels * 4,
            transcendentals=0,
        ),
    )(qkv, tails, conv_weights, pole, gain)


def back(pin, qc, embedded, prefix, near, other, before, pole, drive, residues):
    tok, channels = pin.shape
    modes = pole.shape[0]
    return pl.pallas_call(
        back_kernel,
        out_shape=jax.ShapeDtypeStruct((tok, channels), jnp.bfloat16),
        grid=(channels // BLOCK,),
        in_specs=[channel_spec(tok)] * 3 + [channel_spec(modes)] * 7,
        out_specs=channel_spec(tok),
        cost_estimate=pl.CostEstimate(
            flops=6 * tok * modes * channels,
            bytes_accessed=tok * channels * (4 + 4 + 2 + 2),
            transcendentals=0,
        ),
    )(pin, qc, embedded, prefix, near, other, before, pole, drive, residues)


def level_factors(decay_rates, me, block, radix, tok_local):
    digit = (me // block) % radix
    within = me % (block * radix)
    nears, takes = [], []
    for j in range(1, radix):
        theirs = digit ^ j
        lower = theirs < digit
        gap = jnp.where(lower, within - (theirs + 1) * block, 0).astype(jnp.float32) * tok_local
        nears.append(jnp.where(lower, jnp.exp(-decay_rates * gap), 0.0))
        takes.append(jnp.exp(-decay_rates * ((radix - 1 - theirs) * block * tok_local).astype(jnp.float32)))
    keep = jnp.exp(-decay_rates * ((radix - 1 - digit) * block * tok_local).astype(jnp.float32))
    return nears, keep, takes


def exchange_levels(count):
    levels = []
    while count > 4:
        levels.append(4)
        count //= 4
    return levels + [2] * (count.bit_length() - 1)


def butterfly(local_end, factors, decay_rates, tok_local, axis, levels, extra):
    count = lax.axis_size(axis)
    me = lax.axis_index(axis)
    total = local_end
    prefix = jnp.zeros_like(local_end)
    block = 1
    for level, radix in enumerate(levels):
        others = [
            lax.ppermute(total, axis, [(i, i ^ (j * block)) for i in range(count)]) for j in range(1, radix)
        ]
        nears, keep, takes = factors
        if level == len(levels) - 1:
            others, extra = lax.optimization_barrier((others, extra))
            return prefix, nears[0], others[0], total, keep, takes[0], extra
        nxt = level_factors(decay_rates, me, block * radix, levels[level + 1], tok_local)
        others, factors = lax.optimization_barrier((others, nxt))
        for near, other in zip(nears, others):
            prefix = prefix + near * other
        fresh = keep * total
        for take, other in zip(takes, others):
            fresh = fresh + take * other
        total = fresh
        block *= radix


def body(token_ids, embed_table, hyena_qkv, conv_weights, decay_rates, residues, prior_state):
    tok_local = hyena_qkv.shape[1]
    channels = hyena_qkv.shape[2]
    tap_count = conv_weights.shape[1]
    seq_count = lax.axis_size("seq")
    seq_index = lax.axis_index("seq")
    history = tap_count - 1
    tails_local = hyena_qkv[:, tok_local - history :, :].reshape(3 * history, channels).astype(jnp.float32)
    ring = [(i, (i + 1) % seq_count) for i in range(seq_count)]
    tails_prev = lax.ppermute(tails_local, "seq", ring)
    tails_prev = jnp.where(seq_index == 0, jnp.zeros_like(tails_prev), tails_prev)
    levels = exchange_levels(seq_count)
    tails_prev, factors = lax.optimization_barrier(
        (tails_prev, level_factors(decay_rates, seq_index, 1, levels[0], tok_local))
    )
    pole = jnp.exp(-decay_rates)
    gain = jnp.sqrt(-jnp.expm1(-2.0 * decay_rates))
    qc, pin, local_end = front(hyena_qkv, tails_prev, conv_weights, pole, gain)
    share_cols = channels // seq_count
    mine = lambda a: lax.dynamic_slice_in_dim(a, seq_index * share_cols, share_cols, 1)
    after = jnp.exp(-mine(decay_rates) * float(seq_count * tok_local)) * mine(prior_state)
    before = jnp.exp(-decay_rates * (seq_index.astype(jnp.float32) * tok_local)) * prior_state
    prefix, near, other, total, keep, take, (after, before) = butterfly(
        local_end, factors, decay_rates, tok_local, "seq", levels, (after, before)
    )
    vocab_ids = jnp.arange(embed_table.shape[0], dtype=jnp.int32)
    one_hot = (token_ids[:, None] == vocab_ids[None, :]).astype(jnp.bfloat16)
    embedded = jnp.dot(one_hot, embed_table, preferred_element_type=jnp.float32).astype(jnp.bfloat16)
    hyena_out = back(pin, qc, embedded, prefix, near, other, before, pole, residues * gain, residues)
    end_state = mine(keep) * mine(total) + mine(take) * mine(other) + after
    return (hyena_out, end_state)


def solution(mesh):
    return jax.shard_map(
        body,
        mesh=mesh,
        in_specs=(
            P(("groups", "seq")),
            P(None, "tp"),
            P(None, ("groups", "seq"), "tp"),
            P(None, None, "tp"),
            P(None, "tp"),
            P(None, "tp"),
            P("groups", "tp"),
        ),
        out_specs=(P(("groups", "seq"), "tp"), P("groups", ("tp", "seq"))),
        check_vma=False,
    )
```

```python
import functools

import jax
import jax.numpy as jnp
from jax import lax
from jax.experimental import pallas as pl
from jax.experimental.pallas import tpu as pltpu
from jax.sharding import PartitionSpec as P

LANES = 512
WIDE = 1024
BLOCK = 1024


def shifted(array, axis, by):
    size = lax.axis_size(axis)
    pairs = [(i, i + by) for i in range(size) if 0 <= i + by < size]
    return lax.ppermute(array, axis, pairs)


def front_kernel(qkv_ref, tails_ref, w_ref, pole_ref, gain_ref, qc_ref, pin_ref, end_ref):
    tok, channels = qc_ref.shape
    modes = pole_ref.shape[0]
    for c0 in range(0, channels, LANES):
        cs = pl.ds(c0, LANES)
        row = lax.broadcasted_iota(jnp.int32, (tok, LANES), 0)
        feats = []
        for member in range(3):
            x = qkv_ref[member, :, cs].astype(jnp.float32)
            tl = tails_ref[member, :, cs].astype(jnp.float32)
            x1 = pltpu.roll(x, 1, 0)
            x1 = jnp.where(row == 0, tl[1:2, :], x1)
            x2 = pltpu.roll(x, 2, 0)
            x2 = jnp.where(row == 0, tl[0:1, :], jnp.where(row == 1, tl[1:2, :], x2))
            w = w_ref[member, :, cs]
            feats.append(w[0:1, :] * x + w[1:2, :] * x1 + w[2:3, :] * x2)
        qc_ref[:, cs] = feats[0]
        pin_ref[:, cs] = feats[1] * feats[2]

    for c0 in range(0, channels, WIDE):
        cs = pl.ds(c0, WIDE)
        pole = pole_ref[:, cs]

        def step(blk, acc):
            base = pl.multiple_of(blk * 8, 8)
            rows = pin_ref[pl.ds(base, 8), cs]
            for i in range(8):
                acc = pole * acc + jnp.broadcast_to(rows[i : i + 1, :], (modes, WIDE))
            return acc

        acc = lax.fori_loop(0, tok // 8, step, jnp.zeros((modes, WIDE), jnp.float32))
        end_ref[:, cs] = gain_ref[:, cs] * acc


def rows_summed(parts, sub):
    half = [
        jnp.where(sub < 4, parts[j] + pltpu.roll(parts[j], 4, 0), parts[j + 4] + pltpu.roll(parts[j + 4], 4, 0))
        for j in range(4)
    ]
    quarter = [
        jnp.where(sub % 4 < 2, half[j] + pltpu.roll(half[j], 6, 0), half[j + 2] + pltpu.roll(half[j + 2], 2, 0))
        for j in range(2)
    ]
    return jnp.where(
        sub % 2 == 0,
        quarter[0] + pltpu.roll(quarter[0], 7, 0),
        quarter[1] + pltpu.roll(quarter[1], 1, 0),
    )


def back_kernel(pin_ref, qc_ref, emb_ref, prefix_ref, near_ref, other_ref, before_ref, pole_ref, drive_ref, res_ref, out_ref):
    tok, channels = pin_ref.shape
    modes = pole_ref.shape[0]
    sub = lax.broadcasted_iota(jnp.int32, (modes, WIDE), 0)
    for c0 in range(0, channels, WIDE):
        cs = pl.ds(c0, WIDE)
        pole = pole_ref[:, cs]
        drive = drive_ref[:, cs]
        incoming = prefix_ref[:, cs] + near_ref[:, cs] * other_ref[:, cs] + before_ref[:, cs]
        start = res_ref[:, cs] * incoming

        def step(blk, state):
            base = pl.multiple_of(blk * 16, 16)
            rows = pin_ref[pl.ds(base, 16), cs]
            sums = []
            for half in range(2):
                parts = []
                for i in range(8):
                    r = half * 8 + i
                    state = pole * state + drive * jnp.broadcast_to(rows[r : r + 1, :], (modes, WIDE))
                    parts.append(state)
                sums.append(rows_summed(parts, sub))
            filtered = jnp.concatenate(sums, axis=0)
            total = emb_ref[pl.ds(base, 16), cs].astype(jnp.float32) + qc_ref[pl.ds(base, 16), cs] * filtered
            out_ref[pl.ds(base, 16), cs] = total.astype(out_ref.dtype)
            return state

        lax.fori_loop(0, tok // 16, step, start)


def vmem_specs(count):
    return [pl.BlockSpec(memory_space=pltpu.VMEM)] * count


def channel_spec(*lead):
    rank = len(lead) + 1
    return pl.BlockSpec(lead + (BLOCK,), lambda j: (0,) * (rank - 1) + (j,))


def front(qkv, tails, conv_weights, pole, gain):
    tok, channels = qkv.shape[1], qkv.shape[2]
    modes = pole.shape[0]
    taps = conv_weights.shape[1]
    return pl.pallas_call(
        front_kernel,
        out_shape=(
            jax.ShapeDtypeStruct((tok, channels), jnp.float32),
            jax.ShapeDtypeStruct((tok, channels), jnp.float32),
            jax.ShapeDtypeStruct((modes, channels), jnp.float32),
        ),
        grid=(channels // BLOCK,),
        in_specs=[
            channel_spec(3, tok),
            channel_spec(3, tails.shape[1]),
            channel_spec(3, taps),
            channel_spec(modes),
            channel_spec(modes),
        ],
        out_specs=(channel_spec(tok), channel_spec(tok), channel_spec(modes)),
        cost_estimate=pl.CostEstimate(
            flops=30 * tok * channels + 2 * tok * modes * channels,
            bytes_accessed=3 * tok * channels * 2 + 2 * tok * channels * 4,
            transcendentals=0,
        ),
    )(qkv, tails, conv_weights, pole, gain)


def back(pin, qc, embedded, prefix, near, other, before, pole, drive, residues):
    tok, channels = pin.shape
    modes = pole.shape[0]
    return pl.pallas_call(
        back_kernel,
        out_shape=jax.ShapeDtypeStruct((tok, channels), jnp.bfloat16),
        grid=(channels // BLOCK,),
        in_specs=[channel_spec(tok)] * 3 + [channel_spec(modes)] * 7,
        out_specs=channel_spec(tok),
        cost_estimate=pl.CostEstimate(
            flops=6 * tok * modes * channels,
            bytes_accessed=tok * channels * (4 + 4 + 2 + 2),
            transcendentals=0,
        ),
    )(pin, qc, embedded, prefix, near, other, before, pole, drive, residues)


def level_factors(decay_rates, me, block, radix, tok_local):
    digit = (me // block) % radix
    within = me % (block * radix)
    nears, takes = [], []
    for j in range(1, radix):
        theirs = digit ^ j
        lower = theirs < digit
        gap = jnp.where(lower, within - (theirs + 1) * block, 0).astype(jnp.float32) * tok_local
        nears.append(jnp.where(lower, jnp.exp(-decay_rates * gap), 0.0))
        takes.append(jnp.exp(-decay_rates * ((radix - 1 - theirs) * block * tok_local).astype(jnp.float32)))
    keep = jnp.exp(-decay_rates * ((radix - 1 - digit) * block * tok_local).astype(jnp.float32))
    return nears, keep, takes


def exchange_levels(count):
    levels = []
    while count > 4:
        levels.append(4)
        count //= 4
    return levels + [2] * (count.bit_length() - 1)


def butterfly(local_end, factors, decay_rates, tok_local, axis, levels, extra):
    count = lax.axis_size(axis)
    me = lax.axis_index(axis)
    total = local_end
    prefix = jnp.zeros_like(local_end)
    block = 1
    for level, radix in enumerate(levels):
        others = [
            lax.ppermute(total, axis, [(i, i ^ (j * block)) for i in range(count)]) for j in range(1, radix)
        ]
        nears, keep, takes = factors
        if level == len(levels) - 1:
            others, extra = lax.optimization_barrier((others, extra))
            return prefix, nears[0], others[0], total, keep, takes[0], extra
        nxt = level_factors(decay_rates, me, block * radix, levels[level + 1], tok_local)
        others, factors = lax.optimization_barrier((others, nxt))
        for near, other in zip(nears, others):
            prefix = prefix + near * other
        fresh = keep * total
        for take, other in zip(takes, others):
            fresh = fresh + take * other
        total = fresh
        block *= radix


def body(token_ids, embed_table, hyena_qkv, conv_weights, decay_rates, residues, prior_state):
    tok_local = hyena_qkv.shape[1]
    channels = hyena_qkv.shape[2]
    tap_count = conv_weights.shape[1]
    seq_count = lax.axis_size("seq")
    seq_index = lax.axis_index("seq")
    tails_local = hyena_qkv[:, tok_local - (tap_count - 1) :, :]
    ring = [(i, (i + 1) % seq_count) for i in range(seq_count)]
    tails_prev = lax.ppermute(tails_local, "seq", ring)
    tails_prev = jnp.where(seq_index == 0, jnp.zeros_like(tails_prev), tails_prev)
    levels = exchange_levels(seq_count)
    tails_prev, factors = lax.optimization_barrier(
        (tails_prev, level_factors(decay_rates, seq_index, 1, levels[0], tok_local))
    )
    pole = jnp.exp(-decay_rates)
    gain = jnp.sqrt(-jnp.expm1(-2.0 * decay_rates))
    qc, pin, local_end = front(hyena_qkv, tails_prev, conv_weights, pole, gain)
    share_cols = channels // seq_count
    mine = lambda a: lax.dynamic_slice_in_dim(a, seq_index * share_cols, share_cols, 1)
    after = jnp.exp(-mine(decay_rates) * float(seq_count * tok_local)) * mine(prior_state)
    before = jnp.exp(-decay_rates * (seq_index.astype(jnp.float32) * tok_local)) * prior_state
    prefix, near, other, total, keep, take, (after, before) = butterfly(
        local_end, factors, decay_rates, tok_local, "seq", levels, (after, before)
    )
    vocab_ids = jnp.arange(embed_table.shape[0], dtype=jnp.int32)
    one_hot = (token_ids[:, None] == vocab_ids[None, :]).astype(jnp.bfloat16)
    embedded = jnp.dot(one_hot, embed_table, preferred_element_type=jnp.float32).astype(jnp.bfloat16)
    hyena_out = back(pin, qc, embedded, prefix, near, other, before, pole, residues * gain, residues)
    end_state = mine(keep) * mine(total) + mine(take) * mine(other) + after
    return (hyena_out, end_state)


def solution(mesh):
    return jax.shard_map(
        body,
        mesh=mesh,
        in_specs=(
            P(("groups", "seq")),
            P(None, "tp"),
            P(None, ("groups", "seq"), "tp"),
            P(None, None, "tp"),
            P(None, "tp"),
            P(None, "tp"),
            P("groups", "tp"),
        ),
        out_specs=(P(("groups", "seq"), "tp"), P("groups", ("tp", "seq"))),
        check_vma=False,
    )
```

```python
import functools

import jax
import jax.numpy as jnp
from jax import lax
from jax.experimental import pallas as pl
from jax.experimental.pallas import tpu as pltpu
from jax.sharding import PartitionSpec as P

LANES = 128
WIDE = 1024
BLOCK = 1024


def shifted(array, axis, by):
    size = lax.axis_size(axis)
    pairs = [(i, i + by) for i in range(size) if 0 <= i + by < size]
    return lax.ppermute(array, axis, pairs)


def front_kernel(qkv_ref, tails_ref, w_ref, pole_ref, gain_ref, qc_ref, pin_ref, end_ref):
    tok, channels = qc_ref.shape
    modes = pole_ref.shape[0]
    for c0 in range(0, channels, LANES):
        cs = pl.ds(c0, LANES)
        row = lax.broadcasted_iota(jnp.int32, (tok, LANES), 0)
        feats = []
        for member in range(3):
            x = qkv_ref[member, :, cs].astype(jnp.float32)
            tl = tails_ref[member, :, cs].astype(jnp.float32)
            x1 = pltpu.roll(x, 1, 0)
            x1 = jnp.where(row == 0, tl[1:2, :], x1)
            x2 = pltpu.roll(x, 2, 0)
            x2 = jnp.where(row == 0, tl[0:1, :], jnp.where(row == 1, tl[1:2, :], x2))
            w = w_ref[member, :, cs]
            feats.append(w[0:1, :] * x + w[1:2, :] * x1 + w[2:3, :] * x2)
        qc_ref[:, cs] = feats[0]
        pin_ref[:, cs] = feats[1] * feats[2]

    for c0 in range(0, channels, WIDE):
        cs = pl.ds(c0, WIDE)
        pole = pole_ref[:, cs]

        def step(blk, acc):
            base = pl.multiple_of(blk * 8, 8)
            rows = pin_ref[pl.ds(base, 8), cs]
            for i in range(8):
                acc = pole * acc + jnp.broadcast_to(rows[i : i + 1, :], (modes, WIDE))
            return acc

        acc = lax.fori_loop(0, tok // 8, step, jnp.zeros((modes, WIDE), jnp.float32))
        end_ref[:, cs] = gain_ref[:, cs] * acc


def rows_summed(parts, sub):
    half = [
        jnp.where(sub < 4, parts[j] + pltpu.roll(parts[j], 4, 0), parts[j + 4] + pltpu.roll(parts[j + 4], 4, 0))
        for j in range(4)
    ]
    quarter = [
        jnp.where(sub % 4 < 2, half[j] + pltpu.roll(half[j], 6, 0), half[j + 2] + pltpu.roll(half[j + 2], 2, 0))
        for j in range(2)
    ]
    return jnp.where(
        sub % 2 == 0,
        quarter[0] + pltpu.roll(quarter[0], 7, 0),
        quarter[1] + pltpu.roll(quarter[1], 1, 0),
    )


def back_kernel(pin_ref, qc_ref, emb_ref, prefix_ref, near_ref, other_ref, before_ref, pole_ref, drive_ref, res_ref, out_ref):
    tok, channels = pin_ref.shape
    modes = pole_ref.shape[0]
    sub = lax.broadcasted_iota(jnp.int32, (modes, WIDE), 0)
    for c0 in range(0, channels, WIDE):
        cs = pl.ds(c0, WIDE)
        pole = pole_ref[:, cs]
        drive = drive_ref[:, cs]
        incoming = prefix_ref[:, cs] + near_ref[:, cs] * other_ref[:, cs] + before_ref[:, cs]
        start = res_ref[:, cs] * incoming

        def step(blk, state):
            base = pl.multiple_of(blk * 16, 16)
            rows = pin_ref[pl.ds(base, 16), cs]
            sums = []
            for half in range(2):
                parts = []
                for i in range(8):
                    r = half * 8 + i
                    state = pole * state + drive * jnp.broadcast_to(rows[r : r + 1, :], (modes, WIDE))
                    parts.append(state)
                sums.append(rows_summed(parts, sub))
            filtered = jnp.concatenate(sums, axis=0)
            total = emb_ref[pl.ds(base, 16), cs].astype(jnp.float32) + qc_ref[pl.ds(base, 16), cs] * filtered
            out_ref[pl.ds(base, 16), cs] = total.astype(out_ref.dtype)
            return state

        lax.fori_loop(0, tok // 16, step, start)


def vmem_specs(count):
    return [pl.BlockSpec(memory_space=pltpu.VMEM)] * count


def channel_spec(*lead):
    rank = len(lead) + 1
    return pl.BlockSpec(lead + (BLOCK,), lambda j: (0,) * (rank - 1) + (j,))


def front(qkv, tails, conv_weights, pole, gain):
    tok, channels = qkv.shape[1], qkv.shape[2]
    modes = pole.shape[0]
    taps = conv_weights.shape[1]
    return pl.pallas_call(
        front_kernel,
        out_shape=(
            jax.ShapeDtypeStruct((tok, channels), jnp.float32),
            jax.ShapeDtypeStruct((tok, channels), jnp.float32),
            jax.ShapeDtypeStruct((modes, channels), jnp.float32),
        ),
        grid=(channels // BLOCK,),
        in_specs=[
            channel_spec(3, tok),
            channel_spec(3, tails.shape[1]),
            channel_spec(3, taps),
            channel_spec(modes),
            channel_spec(modes),
        ],
        out_specs=(channel_spec(tok), channel_spec(tok), channel_spec(modes)),
        cost_estimate=pl.CostEstimate(
            flops=30 * tok * channels + 2 * tok * modes * channels,
            bytes_accessed=3 * tok * channels * 2 + 2 * tok * channels * 4,
            transcendentals=0,
        ),
    )(qkv, tails, conv_weights, pole, gain)


def back(pin, qc, embedded, prefix, near, other, before, pole, drive, residues):
    tok, channels = pin.shape
    modes = pole.shape[0]
    return pl.pallas_call(
        back_kernel,
        out_shape=jax.ShapeDtypeStruct((tok, channels), jnp.bfloat16),
        grid=(channels // BLOCK,),
        in_specs=[channel_spec(tok)] * 3 + [channel_spec(modes)] * 7,
        out_specs=channel_spec(tok),
        cost_estimate=pl.CostEstimate(
            flops=6 * tok * modes * channels,
            bytes_accessed=tok * channels * (4 + 4 + 2 + 2),
            transcendentals=0,
        ),
    )(pin, qc, embedded, prefix, near, other, before, pole, drive, residues)


def level_factors(decay_rates, me, block, radix, tok_local):
    digit = (me // block) % radix
    within = me % (block * radix)
    nears, takes = [], []
    for j in range(1, radix):
        theirs = digit ^ j
        lower = theirs < digit
        gap = jnp.where(lower, within - (theirs + 1) * block, 0).astype(jnp.float32) * tok_local
        nears.append(jnp.where(lower, jnp.exp(-decay_rates * gap), 0.0))
        takes.append(jnp.exp(-decay_rates * ((radix - 1 - theirs) * block * tok_local).astype(jnp.float32)))
    keep = jnp.exp(-decay_rates * ((radix - 1 - digit) * block * tok_local).astype(jnp.float32))
    return nears, keep, takes


def exchange_levels(count):
    levels = []
    while count > 4:
        levels.append(4)
        count //= 4
    return levels + [2] * (count.bit_length() - 1)


def butterfly(local_end, factors, decay_rates, tok_local, axis, levels, extra):
    count = lax.axis_size(axis)
    me = lax.axis_index(axis)
    total = local_end
    prefix = jnp.zeros_like(local_end)
    block = 1
    for level, radix in enumerate(levels):
        others = [
            lax.ppermute(total, axis, [(i, i ^ (j * block)) for i in range(count)]) for j in range(1, radix)
        ]
        nears, keep, takes = factors
        if level == len(levels) - 1:
            others, extra = lax.optimization_barrier((others, extra))
            return prefix, nears[0], others[0], total, keep, takes[0], extra
        nxt = level_factors(decay_rates, me, block * radix, levels[level + 1], tok_local)
        others, factors = lax.optimization_barrier((others, nxt))
        for near, other in zip(nears, others):
            prefix = prefix + near * other
        fresh = keep * total
        for take, other in zip(takes, others):
            fresh = fresh + take * other
        total = fresh
        block *= radix


def body(token_ids, embed_table, hyena_qkv, conv_weights, decay_rates, residues, prior_state):
    tok_local = hyena_qkv.shape[1]
    channels = hyena_qkv.shape[2]
    tap_count = conv_weights.shape[1]
    seq_count = lax.axis_size("seq")
    seq_index = lax.axis_index("seq")
    tails_local = hyena_qkv[:, tok_local - (tap_count - 1) :, :]
    ring = [(i, (i + 1) % seq_count) for i in range(seq_count)]
    tails_prev = lax.ppermute(tails_local, "seq", ring)
    tails_prev = jnp.where(seq_index == 0, jnp.zeros_like(tails_prev), tails_prev)
    levels = exchange_levels(seq_count)
    tails_prev, factors = lax.optimization_barrier(
        (tails_prev, level_factors(decay_rates, seq_index, 1, levels[0], tok_local))
    )
    pole = jnp.exp(-decay_rates)
    gain = jnp.sqrt(-jnp.expm1(-2.0 * decay_rates))
    qc, pin, local_end = front(hyena_qkv, tails_prev, conv_weights, pole, gain)
    share_cols = channels // seq_count
    mine = lambda a: lax.dynamic_slice_in_dim(a, seq_index * share_cols, share_cols, 1)
    after = jnp.exp(-mine(decay_rates) * float(seq_count * tok_local)) * mine(prior_state)
    before = jnp.exp(-decay_rates * (seq_index.astype(jnp.float32) * tok_local)) * prior_state
    prefix, near, other, total, keep, take, (after, before) = butterfly(
        local_end, factors, decay_rates, tok_local, "seq", levels, (after, before)
    )
    vocab_ids = jnp.arange(embed_table.shape[0], dtype=jnp.int32)
    one_hot = (token_ids[:, None] == vocab_ids[None, :]).astype(jnp.bfloat16)
    embedded = jnp.dot(one_hot, embed_table, preferred_element_type=jnp.float32).astype(jnp.bfloat16)
    hyena_out = back(pin, qc, embedded, prefix, near, other, before, pole, residues * gain, residues)
    end_state = mine(keep) * mine(total) + mine(take) * mine(other) + after
    return (hyena_out, end_state)


def solution(mesh):
    return jax.shard_map(
        body,
        mesh=mesh,
        in_specs=(
            P(("groups", "seq")),
            P(None, "tp"),
            P(None, ("groups", "seq"), "tp"),
            P(None, None, "tp"),
            P(None, "tp"),
            P(None, "tp"),
            P("groups", "tp"),
        ),
        out_specs=(P(("groups", "seq"), "tp"), P("groups", ("tp", "seq"))),
        check_vma=False,
    )
```

```python
import functools

import jax
import jax.numpy as jnp
from jax import lax
from jax.experimental import pallas as pl
from jax.experimental.pallas import tpu as pltpu
from jax.sharding import PartitionSpec as P

LANES = 256
WIDE = 1024
BLOCK = 1024


def shifted(array, axis, by):
    size = lax.axis_size(axis)
    pairs = [(i, i + by) for i in range(size) if 0 <= i + by < size]
    return lax.ppermute(array, axis, pairs)


def front_kernel(qkv_ref, tails_ref, w_ref, pole_ref, gain_ref, qc_ref, pin_ref, end_ref):
    tok, channels = qc_ref.shape
    modes = pole_ref.shape[0]
    for c0 in range(0, channels, LANES):
        cs = pl.ds(c0, LANES)
        row = lax.broadcasted_iota(jnp.int32, (tok, LANES), 0)
        feats = []
        for member in range(3):
            x = qkv_ref[member, :, cs].astype(jnp.float32)
            tl = tails_ref[member, :, cs].astype(jnp.float32)
            x1 = pltpu.roll(x, 1, 0)
            x1 = jnp.where(row == 0, tl[1:2, :], x1)
            x2 = pltpu.roll(x, 2, 0)
            x2 = jnp.where(row == 0, tl[0:1, :], jnp.where(row == 1, tl[1:2, :], x2))
            w = w_ref[member, :, cs]
            feats.append(w[0:1, :] * x + w[1:2, :] * x1 + w[2:3, :] * x2)
        qc_ref[:, cs] = feats[0]
        pin_ref[:, cs] = feats[1] * feats[2]

    for c0 in range(0, channels, WIDE):
        cs = pl.ds(c0, WIDE)
        pole = pole_ref[:, cs]

        def step(blk, acc):
            base = pl.multiple_of(blk * 8, 8)
            rows = pin_ref[pl.ds(base, 8), cs]
            for i in range(8):
                acc = pole * acc + jnp.broadcast_to(rows[i : i + 1, :], (modes, WIDE))
            return acc

        acc = lax.fori_loop(0, tok // 8, step, jnp.zeros((modes, WIDE), jnp.float32))
        end_ref[:, cs] = gain_ref[:, cs] * acc


def rows_summed(parts, sub):
    half = [
        jnp.where(sub < 4, parts[j] + pltpu.roll(parts[j], 4, 0), parts[j + 4] + pltpu.roll(parts[j + 4], 4, 0))
        for j in range(4)
    ]
    quarter = [
        jnp.where(sub % 4 < 2, half[j] + pltpu.roll(half[j], 6, 0), half[j + 2] + pltpu.roll(half[j + 2], 2, 0))
        for j in range(2)
    ]
    return jnp.where(
        sub % 2 == 0,
        quarter[0] + pltpu.roll(quarter[0], 7, 0),
        quarter[1] + pltpu.roll(quarter[1], 1, 0),
    )


def back_kernel(pin_ref, qc_ref, emb_ref, prefix_ref, near_ref, other_ref, before_ref, pole_ref, drive_ref, res_ref, out_ref):
    tok, channels = pin_ref.shape
    modes = pole_ref.shape[0]
    sub = lax.broadcasted_iota(jnp.int32, (modes, WIDE), 0)
    for c0 in range(0, channels, WIDE):
        cs = pl.ds(c0, WIDE)
        pole = pole_ref[:, cs]
        drive = drive_ref[:, cs]
        incoming = prefix_ref[:, cs] + near_ref[:, cs] * other_ref[:, cs] + before_ref[:, cs]
        start = res_ref[:, cs] * incoming

        def step(blk, state):
            base = pl.multiple_of(blk * 16, 16)
            rows = pin_ref[pl.ds(base, 16), cs]
            sums = []
            for half in range(2):
                parts = []
                for i in range(8):
                    r = half * 8 + i
                    state = pole * state + drive * jnp.broadcast_to(rows[r : r + 1, :], (modes, WIDE))
                    parts.append(state)
                sums.append(rows_summed(parts, sub))
            filtered = jnp.concatenate(sums, axis=0)
            total = emb_ref[pl.ds(base, 16), cs].astype(jnp.float32) + qc_ref[pl.ds(base, 16), cs] * filtered
            out_ref[pl.ds(base, 16), cs] = total.astype(out_ref.dtype)
            return state

        lax.fori_loop(0, tok // 16, step, start, unroll=2)


def vmem_specs(count):
    return [pl.BlockSpec(memory_space=pltpu.VMEM)] * count


def channel_spec(*lead):
    rank = len(lead) + 1
    return pl.BlockSpec(lead + (BLOCK,), lambda j: (0,) * (rank - 1) + (j,))


def front(qkv, tails, conv_weights, pole, gain):
    tok, channels = qkv.shape[1], qkv.shape[2]
    modes = pole.shape[0]
    taps = conv_weights.shape[1]
    return pl.pallas_call(
        front_kernel,
        out_shape=(
            jax.ShapeDtypeStruct((tok, channels), jnp.float32),
            jax.ShapeDtypeStruct((tok, channels), jnp.float32),
            jax.ShapeDtypeStruct((modes, channels), jnp.float32),
        ),
        grid=(channels // BLOCK,),
        in_specs=[
            channel_spec(3, tok),
            channel_spec(3, tails.shape[1]),
            channel_spec(3, taps),
            channel_spec(modes),
            channel_spec(modes),
        ],
        out_specs=(channel_spec(tok), channel_spec(tok), channel_spec(modes)),
        cost_estimate=pl.CostEstimate(
            flops=30 * tok * channels + 2 * tok * modes * channels,
            bytes_accessed=3 * tok * channels * 2 + 2 * tok * channels * 4,
            transcendentals=0,
        ),
    )(qkv, tails, conv_weights, pole, gain)


def back(pin, qc, embedded, prefix, near, other, before, pole, drive, residues):
    tok, channels = pin.shape
    modes = pole.shape[0]
    return pl.pallas_call(
        back_kernel,
        out_shape=jax.ShapeDtypeStruct((tok, channels), jnp.bfloat16),
        grid=(channels // BLOCK,),
        in_specs=[channel_spec(tok)] * 3 + [channel_spec(modes)] * 7,
        out_specs=channel_spec(tok),
        cost_estimate=pl.CostEstimate(
            flops=6 * tok * modes * channels,
            bytes_accessed=tok * channels * (4 + 4 + 2 + 2),
            transcendentals=0,
        ),
    )(pin, qc, embedded, prefix, near, other, before, pole, drive, residues)


def level_factors(decay_rates, me, block, radix, tok_local):
    digit = (me // block) % radix
    within = me % (block * radix)
    nears, takes = [], []
    for j in range(1, radix):
        theirs = digit ^ j
        lower = theirs < digit
        gap = jnp.where(lower, within - (theirs + 1) * block, 0).astype(jnp.float32) * tok_local
        nears.append(jnp.where(lower, jnp.exp(-decay_rates * gap), 0.0))
        takes.append(jnp.exp(-decay_rates * ((radix - 1 - theirs) * block * tok_local).astype(jnp.float32)))
    keep = jnp.exp(-decay_rates * ((radix - 1 - digit) * block * tok_local).astype(jnp.float32))
    return nears, keep, takes


def exchange_levels(count):
    levels = []
    while count > 4:
        levels.append(4)
        count //= 4
    return levels + [2] * (count.bit_length() - 1)


def butterfly(local_end, factors, decay_rates, tok_local, axis, levels, extra):
    count = lax.axis_size(axis)
    me = lax.axis_index(axis)
    total = local_end
    prefix = jnp.zeros_like(local_end)
    block = 1
    for level, radix in enumerate(levels):
        others = [
            lax.ppermute(total, axis, [(i, i ^ (j * block)) for i in range(count)]) for j in range(1, radix)
        ]
        nears, keep, takes = factors
        if level == len(levels) - 1:
            others, extra = lax.optimization_barrier((others, extra))
            return prefix, nears[0], others[0], total, keep, takes[0], extra
        nxt = level_factors(decay_rates, me, block * radix, levels[level + 1], tok_local)
        others, factors = lax.optimization_barrier((others, nxt))
        for near, other in zip(nears, others):
            prefix = prefix + near * other
        fresh = keep * total
        for take, other in zip(takes, others):
            fresh = fresh + take * other
        total = fresh
        block *= radix


def body(token_ids, embed_table, hyena_qkv, conv_weights, decay_rates, residues, prior_state):
    tok_local = hyena_qkv.shape[1]
    channels = hyena_qkv.shape[2]
    tap_count = conv_weights.shape[1]
    seq_count = lax.axis_size("seq")
    seq_index = lax.axis_index("seq")
    tails_local = hyena_qkv[:, tok_local - (tap_count - 1) :, :]
    ring = [(i, (i + 1) % seq_count) for i in range(seq_count)]
    tails_prev = lax.ppermute(tails_local, "seq", ring)
    tails_prev = jnp.where(seq_index == 0, jnp.zeros_like(tails_prev), tails_prev)
    levels = exchange_levels(seq_count)
    tails_prev, factors = lax.optimization_barrier(
        (tails_prev, level_factors(decay_rates, seq_index, 1, levels[0], tok_local))
    )
    pole = jnp.exp(-decay_rates)
    gain = jnp.sqrt(-jnp.expm1(-2.0 * decay_rates))
    qc, pin, local_end = front(hyena_qkv, tails_prev, conv_weights, pole, gain)
    share_cols = channels // seq_count
    mine = lambda a: lax.dynamic_slice_in_dim(a, seq_index * share_cols, share_cols, 1)
    after = jnp.exp(-mine(decay_rates) * float(seq_count * tok_local)) * mine(prior_state)
    before = jnp.exp(-decay_rates * (seq_index.astype(jnp.float32) * tok_local)) * prior_state
    prefix, near, other, total, keep, take, (after, before) = butterfly(
        local_end, factors, decay_rates, tok_local, "seq", levels, (after, before)
    )
    vocab_ids = jnp.arange(embed_table.shape[0], dtype=jnp.int32)
    one_hot = (token_ids[:, None] == vocab_ids[None, :]).astype(jnp.bfloat16)
    embedded = jnp.dot(one_hot, embed_table, preferred_element_type=jnp.float32).astype(jnp.bfloat16)
    hyena_out = back(pin, qc, embedded, prefix, near, other, before, pole, residues * gain, residues)
    end_state = mine(keep) * mine(total) + mine(take) * mine(other) + after
    return (hyena_out, end_state)


def solution(mesh):
    return jax.shard_map(
        body,
        mesh=mesh,
        in_specs=(
            P(("groups", "seq")),
            P(None, "tp"),
            P(None, ("groups", "seq"), "tp"),
            P(None, None, "tp"),
            P(None, "tp"),
            P(None, "tp"),
            P("groups", "tp"),
        ),
        out_specs=(P(("groups", "seq"), "tp"), P("groups", ("tp", "seq"))),
        check_vma=False,
    )
```

```python
import functools

import jax
import jax.numpy as jnp
from jax import lax
from jax.experimental import pallas as pl
from jax.experimental.pallas import tpu as pltpu
from jax.sharding import PartitionSpec as P

LANES = 256
WIDE = 1024
BLOCK = 1024


def shifted(array, axis, by):
    size = lax.axis_size(axis)
    pairs = [(i, i + by) for i in range(size) if 0 <= i + by < size]
    return lax.ppermute(array, axis, pairs)


def front_kernel(qkv_ref, tails_ref, w_ref, pole_ref, gain_ref, qc_ref, pin_ref, end_ref):
    tok, channels = qc_ref.shape
    modes = pole_ref.shape[0]
    for c0 in range(0, channels, LANES):
        cs = pl.ds(c0, LANES)
        row = lax.broadcasted_iota(jnp.int32, (tok, LANES), 0)
        feats = []
        for member in range(3):
            x = qkv_ref[member, :, cs].astype(jnp.float32)
            tl = tails_ref[member, :, cs].astype(jnp.float32)
            x1 = pltpu.roll(x, 1, 0)
            x1 = jnp.where(row == 0, tl[1:2, :], x1)
            x2 = pltpu.roll(x, 2, 0)
            x2 = jnp.where(row == 0, tl[0:1, :], jnp.where(row == 1, tl[1:2, :], x2))
            w = w_ref[member, :, cs]
            feats.append(w[0:1, :] * x + w[1:2, :] * x1 + w[2:3, :] * x2)
        qc_ref[:, cs] = feats[0]
        pin_ref[:, cs] = feats[1] * feats[2]

    for c0 in range(0, channels, WIDE):
        cs = pl.ds(c0, WIDE)
        pole = pole_ref[:, cs]

        def step(blk, acc):
            base = pl.multiple_of(blk * 8, 8)
            rows = pin_ref[pl.ds(base, 8), cs]
            for i in range(8):
                acc = pole * acc + jnp.broadcast_to(rows[i : i + 1, :], (modes, WIDE))
            return acc

        acc = lax.fori_loop(0, tok // 8, step, jnp.zeros((modes, WIDE), jnp.float32), unroll=2)
        end_ref[:, cs] = gain_ref[:, cs] * acc


def rows_summed(parts, sub):
    half = [
        jnp.where(sub < 4, parts[j] + pltpu.roll(parts[j], 4, 0), parts[j + 4] + pltpu.roll(parts[j + 4], 4, 0))
        for j in range(4)
    ]
    quarter = [
        jnp.where(sub % 4 < 2, half[j] + pltpu.roll(half[j], 6, 0), half[j + 2] + pltpu.roll(half[j + 2], 2, 0))
        for j in range(2)
    ]
    return jnp.where(
        sub % 2 == 0,
        quarter[0] + pltpu.roll(quarter[0], 7, 0),
        quarter[1] + pltpu.roll(quarter[1], 1, 0),
    )


def back_kernel(pin_ref, qc_ref, emb_ref, prefix_ref, near_ref, other_ref, before_ref, pole_ref, drive_ref, res_ref, out_ref):
    tok, channels = pin_ref.shape
    modes = pole_ref.shape[0]
    sub = lax.broadcasted_iota(jnp.int32, (modes, WIDE), 0)
    for c0 in range(0, channels, WIDE):
        cs = pl.ds(c0, WIDE)
        pole = pole_ref[:, cs]
        drive = drive_ref[:, cs]
        incoming = prefix_ref[:, cs] + near_ref[:, cs] * other_ref[:, cs] + before_ref[:, cs]
        start = res_ref[:, cs] * incoming

        def step(blk, state):
            base = pl.multiple_of(blk * 16, 16)
            rows = pin_ref[pl.ds(base, 16), cs]
            sums = []
            for half in range(2):
                parts = []
                for i in range(8):
                    r = half * 8 + i
                    state = pole * state + drive * jnp.broadcast_to(rows[r : r + 1, :], (modes, WIDE))
                    parts.append(state)
                sums.append(rows_summed(parts, sub))
            filtered = jnp.concatenate(sums, axis=0)
            total = emb_ref[pl.ds(base, 16), cs].astype(jnp.float32) + qc_ref[pl.ds(base, 16), cs] * filtered
            out_ref[pl.ds(base, 16), cs] = total.astype(out_ref.dtype)
            return state

        lax.fori_loop(0, tok // 16, step, start)


def vmem_specs(count):
    return [pl.BlockSpec(memory_space=pltpu.VMEM)] * count


def channel_spec(*lead):
    rank = len(lead) + 1
    return pl.BlockSpec(lead + (BLOCK,), lambda j: (0,) * (rank - 1) + (j,))


def front(qkv, tails, conv_weights, pole, gain):
    tok, channels = qkv.shape[1], qkv.shape[2]
    modes = pole.shape[0]
    taps = conv_weights.shape[1]
    return pl.pallas_call(
        front_kernel,
        out_shape=(
            jax.ShapeDtypeStruct((tok, channels), jnp.float32),
            jax.ShapeDtypeStruct((tok, channels), jnp.float32),
            jax.ShapeDtypeStruct((modes, channels), jnp.float32),
        ),
        grid=(channels // BLOCK,),
        in_specs=[
            channel_spec(3, tok),
            channel_spec(3, tails.shape[1]),
            channel_spec(3, taps),
            channel_spec(modes),
            channel_spec(modes),
        ],
        out_specs=(channel_spec(tok), channel_spec(tok), channel_spec(modes)),
        cost_estimate=pl.CostEstimate(
            flops=30 * tok * channels + 2 * tok * modes * channels,
            bytes_accessed=3 * tok * channels * 2 + 2 * tok * channels * 4,
            transcendentals=0,
        ),
    )(qkv, tails, conv_weights, pole, gain)


def back(pin, qc, embedded, prefix, near, other, before, pole, drive, residues):
    tok, channels = pin.shape
    modes = pole.shape[0]
    return pl.pallas_call(
        back_kernel,
        out_shape=jax.ShapeDtypeStruct((tok, channels), jnp.bfloat16),
        grid=(channels // BLOCK,),
        in_specs=[channel_spec(tok)] * 3 + [channel_spec(modes)] * 7,
        out_specs=channel_spec(tok),
        cost_estimate=pl.CostEstimate(
            flops=6 * tok * modes * channels,
            bytes_accessed=tok * channels * (4 + 4 + 2 + 2),
            transcendentals=0,
        ),
    )(pin, qc, embedded, prefix, near, other, before, pole, drive, residues)


def level_factors(decay_rates, me, block, radix, tok_local):
    digit = (me // block) % radix
    within = me % (block * radix)
    nears, takes = [], []
    for j in range(1, radix):
        theirs = digit ^ j
        lower = theirs < digit
        gap = jnp.where(lower, within - (theirs + 1) * block, 0).astype(jnp.float32) * tok_local
        nears.append(jnp.where(lower, jnp.exp(-decay_rates * gap), 0.0))
        takes.append(jnp.exp(-decay_rates * ((radix - 1 - theirs) * block * tok_local).astype(jnp.float32)))
    keep = jnp.exp(-decay_rates * ((radix - 1 - digit) * block * tok_local).astype(jnp.float32))
    return nears, keep, takes


def exchange_levels(count):
    levels = []
    while count > 4:
        levels.append(4)
        count //= 4
    return levels + [2] * (count.bit_length() - 1)


def butterfly(local_end, factors, decay_rates, tok_local, axis, levels, extra):
    count = lax.axis_size(axis)
    me = lax.axis_index(axis)
    total = local_end
    prefix = jnp.zeros_like(local_end)
    block = 1
    for level, radix in enumerate(levels):
        others = [
            lax.ppermute(total, axis, [(i, i ^ (j * block)) for i in range(count)]) for j in range(1, radix)
        ]
        nears, keep, takes = factors
        if level == len(levels) - 1:
            others, extra = lax.optimization_barrier((others, extra))
            return prefix, nears[0], others[0], total, keep, takes[0], extra
        nxt = level_factors(decay_rates, me, block * radix, levels[level + 1], tok_local)
        others, factors = lax.optimization_barrier((others, nxt))
        for near, other in zip(nears, others):
            prefix = prefix + near * other
        fresh = keep * total
        for take, other in zip(takes, others):
            fresh = fresh + take * other
        total = fresh
        block *= radix


def body(token_ids, embed_table, hyena_qkv, conv_weights, decay_rates, residues, prior_state):
    tok_local = hyena_qkv.shape[1]
    channels = hyena_qkv.shape[2]
    tap_count = conv_weights.shape[1]
    seq_count = lax.axis_size("seq")
    seq_index = lax.axis_index("seq")
    tails_local = hyena_qkv[:, tok_local - (tap_count - 1) :, :]
    ring = [(i, (i + 1) % seq_count) for i in range(seq_count)]
    tails_prev = lax.ppermute(tails_local, "seq", ring)
    tails_prev = jnp.where(seq_index == 0, jnp.zeros_like(tails_prev), tails_prev)
    levels = exchange_levels(seq_count)
    tails_prev, factors = lax.optimization_barrier(
        (tails_prev, level_factors(decay_rates, seq_index, 1, levels[0], tok_local))
    )
    pole = jnp.exp(-decay_rates)
    gain = jnp.sqrt(-jnp.expm1(-2.0 * decay_rates))
    qc, pin, local_end = front(hyena_qkv, tails_prev, conv_weights, pole, gain)
    share_cols = channels // seq_count
    mine = lambda a: lax.dynamic_slice_in_dim(a, seq_index * share_cols, share_cols, 1)
    after = jnp.exp(-mine(decay_rates) * float(seq_count * tok_local)) * mine(prior_state)
    before = jnp.exp(-decay_rates * (seq_index.astype(jnp.float32) * tok_local)) * prior_state
    prefix, near, other, total, keep, take, (after, before) = butterfly(
        local_end, factors, decay_rates, tok_local, "seq", levels, (after, before)
    )
    vocab_ids = jnp.arange(embed_table.shape[0], dtype=jnp.int32)
    one_hot = (token_ids[:, None] == vocab_ids[None, :]).astype(jnp.bfloat16)
    embedded = jnp.dot(one_hot, embed_table, preferred_element_type=jnp.float32).astype(jnp.bfloat16)
    hyena_out = back(pin, qc, embedded, prefix, near, other, before, pole, residues * gain, residues)
    end_state = mine(keep) * mine(total) + mine(take) * mine(other) + after
    return (hyena_out, end_state)


def solution(mesh):
    return jax.shard_map(
        body,
        mesh=mesh,
        in_specs=(
            P(("groups", "seq")),
            P(None, "tp"),
            P(None, ("groups", "seq"), "tp"),
            P(None, None, "tp"),
            P(None, "tp"),
            P(None, "tp"),
            P("groups", "tp"),
        ),
        out_specs=(P(("groups", "seq"), "tp"), P("groups", ("tp", "seq"))),
        check_vma=False,
    )
```
